32 devices in a mesh: patch: 8 (over z, y), band: 4 (over x, core).
Axes of the slice: x: 2, y: 2, z: 4, core: 2. Of those that a mesh axis runs over, the one named last changes fastest.
Arguments:
- exposures: float32 [64, 256, 128], P(('band', 'patch')), parts along dimension 0, may hold values from -6 to 6
- variance: float32 [64, 256, 128], P(('band', 'patch')), parts along dimension 0, may hold values from 0.01 to 60, as said below
- mask_bits: int32 [64, 256, 128], P(('band', 'patch')), parts along dimension 0, may hold values from 0 to 4095
- kernel_coeffs: float32 [64, 27, 6], P(('band', 'patch')), parts along dimension 0, may hold values from -3 to 3
- ccd_visit: int32 [64, 1], P(('band', 'patch')), parts along dimension 0, may hold values from 0 to 7
- strip_patch: int32 [2048, 1], P(('band', 'patch')), parts along dimension 0, may hold values from 0 to 7, as said below
- strip_row: int32 [2048], P(('band', 'patch')), parts along dimension 0, may hold values from 0 to 120
- strip_col: int32 [2048], P(('band', 'patch')), parts along dimension 0, may hold values from 0 to 384
Outputs:
- coadd_image: float32 [32, 128, 512], P(('band', 'patch')), parts along dimension 0
- weight_map: float32 [32, 128, 512], P(('band', 'patch')), parts along dimension 0
The draws below stay inside these ranges and needn't reach their ends.
There are 4 independent parts, one for each index of `band`. The reference program is written for one: setup_inputs(seed, part) draws one part's arguments, and reference() takes and returns one part's arrays. A program takes and returns all parts, laid end to end along the dimension named above; each array names one. Nothing has to cross between parts.
Inputs may be any that keep to these rules, and one draw needn't show every extreme that they name: `variance`: Positive. `ccd_visit`: every visit has at least one CCD. `strip_patch`: among the strips of one device (aligned blocks of 64 rows) no patch is named more than 16 times; one patch is named exactly 16 times in every block.
All inputs are finite; a program needn't handle non-finite values.
Results may differ from the reference program's by a relative error of at most 0.00011.
Values sent between devices are 32-bit elements; how exact they have to be, the bound alone decides.
No kernel may reach another device: no remote copies, remote signals or barrier semaphores. Data moves between devices by JAX's collectives and lax.ppermute only.
A program may use at most 64 MiB of HBM per device.

```python
import jax
import jax.numpy as jnp
from jax import lax

CH = 256
CW = 128
SR = 8
PH = 128
PW = 512
KS = 21
NB = 27
NSP = 6
VISITS = 8
CCDS = 16
STRIPS_DEV = 64
STRIPS = 512
PATCHES = 8
CAP = 16


def draw_variance(key, part):
    row_key, column_key, pixel_key = jax.random.split(jax.random.fold_in(key, 7), 3)
    ten_log = jnp.log(10.0)
    row_scale = jnp.exp(jax.random.uniform(row_key, (CCDS, CH, 1), jnp.float32) * ten_log)
    column_scale = jnp.exp(jax.random.uniform(column_key, (CCDS, 1, CW), jnp.float32) * ten_log)
    position = jnp.arange(CCDS).astype(jnp.float32) / max(CCDS - 1, 1)
    increasing_order = 1.0 + 2.0 * position
    pixel_scale = jnp.exp(jax.random.uniform(pixel_key, (CCDS, CH, CW), jnp.float32, -0.7, 0.7))
    return 0.03 * increasing_order[:, None, None] * row_scale * column_scale * pixel_scale


def draw_strip_patch(key, part):
    hot_key, bias_key, block_key = jax.random.split(jax.random.fold_in(key, 13), 3)
    hot_patch = jax.random.randint(hot_key, (), 0, PATCHES)
    patch_bias = jax.random.randint(bias_key, (PATCHES,), 0, 4) * 1024
    copies = jnp.repeat(jnp.arange(PATCHES, dtype=jnp.int32), CAP)
    tie_break = jnp.arange(PATCHES * CAP, dtype=jnp.int32)

    def one_block(sub_key):
        noise_key, shuffle_key = jax.random.split(sub_key)
        noise = jax.random.randint(noise_key, (PATCHES * CAP,), 0, 4096)
        score = noise + patch_bias[copies] + (copies == hot_patch).astype(jnp.int32) * 65536
        score = score * (PATCHES * CAP) + tie_break
        chosen = copies[lax.top_k(score, STRIPS_DEV)[1]]
        return chosen[jax.random.permutation(shuffle_key, STRIPS_DEV)]
    blocks = jax.vmap(one_block)(jax.random.split(block_key, PATCHES))
    return blocks.reshape(STRIPS, 1).astype(jnp.int32)


def touch_ends(values, stream_key, smallest, high):
    dims = values.shape
    place = [jax.random.randint(jax.random.fold_in(stream_key, axis), (), 0, dims[axis]) for axis in range(len(dims))]
    values = values.at[tuple(place)].set(smallest)
    longest = dims.index(max(dims))
    place[longest] = (place[longest] + 1) % dims[longest]
    return values.at[tuple(place)].set(high)


def shard_levels(stream_key, shape, shards, smallest, top_value):
    def one(axis_at, parts):
        heights = jax.random.uniform(jax.random.fold_in(jax.random.fold_in(stream_key, 6), axis_at), (parts,), jnp.float32, smallest / len(shards), top_value / len(shards))
        return jnp.repeat(jnp.exp(heights), shape[axis_at] // parts).reshape((-1,) + (1,) * (len(shape) - axis_at - 1))

    level = one(*shards[0])
    for cut in shards[1:]:
        level = level * one(*cut)
    return level


def different_ones(stream_key, rows, amount, top, lift):
    sequence = jax.random.permutation(jax.random.fold_in(stream_key, 1), amount)
    favour = sequence
    for power in range(3):
        favour = favour * favour // amount
    favour = favour * lift // amount
    tickets = jax.random.randint(jax.random.fold_in(stream_key, 2), (rows, amount), 0, 4096) + favour
    fixed_rows = jax.random.permutation(jax.random.fold_in(stream_key, 3), rows)[jnp.arange(amount) % rows]
    tickets = jnp.where(jnp.arange(rows)[:, None] == fixed_rows[None, :], 1 << 14, tickets)
    score = tickets * amount + jnp.arange(amount)
    return lax.top_k(score.astype(jnp.int32), top)[1].astype(jnp.int32)


def scatter_about(rng, dims, width, most, cuts=(), held_as=jnp.bfloat16):
    values = jax.random.normal(rng, dims, jnp.float32) * width
    if len(cuts) > 0:
        values = shard_levels(rng, dims, cuts, -0.22, 0.18) * values
    return jnp.clip(values, min=-most, max=most).astype(held_as)


def setup_inputs(seed: int = 0, part: int = 0) -> dict:
    key_list = jax.random.split(jax.random.key(seed), 9)
    part_splits = jax.random.split(jax.random.fold_in(key_list[8], part), 9)
    return {
        "exposures": scatter_about(part_splits[0], (CCDS, CH, CW), 1.0, 6.0, ((0, 8),), jnp.float32),
        "variance": draw_variance(jax.random.fold_in(jax.random.fold_in(key_list[8], part), 71), part),
        "mask_bits": touch_ends(jax.random.randint(part_splits[2], (CCDS, CH, CW), 0, 4096), jax.random.fold_in(part_splits[2], 1), 0, 4095).astype(jnp.int32),
        "kernel_coeffs": scatter_about(part_splits[3], (CCDS, NB, NSP), 0.4, 3.0, ((0, 8),), jnp.float32),
        "ccd_visit": different_ones(part_splits[4], CCDS, VISITS, 1, 0),
        "strip_patch": draw_strip_patch(jax.random.fold_in(jax.random.fold_in(key_list[8], part), 71), part),
        "strip_row": touch_ends(jax.random.randint(part_splits[6], (STRIPS,), 0, PH - SR + 1), jax.random.fold_in(part_splits[6], 1), 0, PH - SR).astype(jnp.int32),
        "strip_col": touch_ends(jax.random.randint(part_splits[7], (STRIPS,), 0, PW - CW + 1), jax.random.fold_in(part_splits[7], 1), 0, PW - CW).astype(jnp.int32),
    }


gauss_widths = (0.75, 1.5, 3.0)
largest_value = lax.Precision.HIGHEST


def tap_values(offsets, kernel_half_width):
    support = jnp.arange(-kernel_half_width, kernel_half_width + 1).astype(jnp.float32)
    inside = (jnp.abs(offsets) <= kernel_half_width).astype(jnp.float32)
    tables = []
    for spread in gauss_widths:
        gauss_total = jnp.sum(jnp.exp(-support * support / (2.0 * spread * spread)))
        profile = jnp.exp(-offsets * offsets / (2.0 * spread * spread)) / gauss_total * inside
        scaled = offsets / spread
        tables.append(jnp.stack([profile, profile * scaled, profile * scaled * scaled]))
    return jnp.stack(tables)


def row_filters(row_count, kernel_half_width):
    row_ids = jnp.arange(row_count)[:, None]
    window_ids = jnp.arange(row_count + 2 * kernel_half_width)[None, :]
    return tap_values((window_ids - row_ids - kernel_half_width).astype(jnp.float32), kernel_half_width)


def column_filters(column_count, kernel_half_width):
    source = jnp.arange(column_count)[:, None]
    target_patch = jnp.arange(column_count)[None, :]
    return tap_values((source - target_patch).astype(jnp.float32), kernel_half_width)


def convolve(windows, kernel_terms, row_starts, height):
    kernel_half_width = KS // 2
    batch_size = windows.shape[0]
    row_count = windows.shape[1] - 2 * kernel_half_width
    columns = windows.shape[2]
    smooth = jnp.einsum('gaij,njc->ngaic', row_filters(row_count, kernel_half_width), windows, precision=largest_value)
    column_ops = column_filters(columns, kernel_half_width)
    row_coords = row_starts[:, None] + jnp.arange(row_count).astype(jnp.float32)[None, :]
    y_plane = jnp.broadcast_to((2.0 * row_coords / (height - 1) - 1.0)[:, :, None], (batch_size, row_count, columns))
    x_line = 2.0 * jnp.arange(columns).astype(jnp.float32) / (columns - 1) - 1.0
    x_plane = jnp.broadcast_to(x_line[None, None, :], (batch_size, row_count, columns))
    ones_plane = jnp.ones((batch_size, row_count, columns), jnp.float32)
    poly_planes = jnp.stack([ones_plane, x_plane, y_plane, x_plane * x_plane, x_plane * y_plane, y_plane * y_plane], axis=1)
    kernel_split = kernel_terms.reshape(batch_size, 3, 9, kernel_terms.shape[2])
    result = jnp.zeros((batch_size, row_count, columns), jnp.float32)
    for gauss_index in range(3):
        basis_images = jnp.einsum('naic,bcd->nabid', smooth[:, gauss_index], column_ops[gauss_index], precision=largest_value)
        fields = jnp.einsum('nkp,npid->nkid', kernel_split[:, gauss_index], poly_planes, precision=largest_value)
        fields = fields.reshape(batch_size, 3, 3, row_count, columns)
        result = result + jnp.sum(basis_images * fields, axis=(1, 2))
    return result


def reference(exposures, variance, mask_bits, kernel_coeffs, ccd_visit, strip_patch, strip_row, strip_col):
    kernel_half_width = KS // 2
    usable = (jnp.bitwise_and(mask_bits, 3) != 3).astype(jnp.float32)
    visit_hot = (ccd_visit == jnp.arange(VISITS).astype(jnp.int32)[None, :]).astype(jnp.float32)
    visit_count = jnp.sum(jnp.sum(usable, axis=(1, 2))[:, None] * visit_hot, axis=0)
    visit_load = jnp.sum(jnp.sum(usable * variance, axis=(1, 2))[:, None] * visit_hot, axis=0)
    visit_weight = (visit_count + 1.0) / (visit_load + 1.0)
    detector_weight = jnp.sum(visit_hot * visit_weight[None, :], axis=1)
    padded = jnp.pad(exposures, ((0, 0), (kernel_half_width, kernel_half_width), (0, 0)))

    def match_one(ccd_pair):
        return convolve(ccd_pair[0][None], ccd_pair[1][None], jnp.zeros((1,), jnp.float32), CH)[0]

    convolved = lax.map(match_one, (padded, kernel_coeffs))
    plane_weight = detector_weight[:, None, None] * usable
    flux_strips = (plane_weight * convolved).reshape(STRIPS, SR, CW)
    weight_strips = plane_weight.reshape(STRIPS, SR, CW)
    target_patch = jnp.broadcast_to(strip_patch[:, 0][:, None, None], (STRIPS, SR, CW))
    row_index = jnp.broadcast_to(strip_row[:, None, None] + jnp.arange(SR).astype(jnp.int32)[None, :, None], (STRIPS, SR, CW))
    col_index = jnp.broadcast_to(strip_col[:, None, None] + jnp.arange(CW).astype(jnp.int32)[None, None, :], (STRIPS, SR, CW))
    numerator = jnp.zeros((PATCHES, PH, PW), jnp.float32).at[target_patch, row_index, col_index].add(flux_strips)
    weight_map = jnp.zeros((PATCHES, PH, PW), jnp.float32).at[target_patch, row_index, col_index].add(weight_strips)
    coadd_image = numerator / jnp.maximum(weight_map, 1.0)
    return (coadd_image, weight_map)
```

```python
import math

import jax
import jax.numpy as jnp
from jax import lax
from jax.sharding import PartitionSpec as P

PH = 128
PW = 512
KS = 21
VISITS = 8


gauss_widths = (0.75, 1.5, 3.0)
largest_value = lax.Precision.HIGHEST
mxu_value = lax.Precision.HIGH


def tap_values(offsets, kernel_half_width):
    support = jnp.arange(-kernel_half_width, kernel_half_width + 1).astype(jnp.float32)
    inside = (jnp.abs(offsets) <= kernel_half_width).astype(jnp.float32)
    tables = []
    for spread in gauss_widths:
        gauss_total = jnp.sum(jnp.exp(-support * support / (2.0 * spread * spread)))
        profile = jnp.exp(-offsets * offsets / (2.0 * spread * spread)) / gauss_total * inside
        scaled = offsets / spread
        tables.append(jnp.stack([profile, profile * scaled, profile * scaled * scaled]))
    return jnp.stack(tables)


def row_filters(row_count, kernel_half_width):
    row_ids = jnp.arange(row_count)[:, None]
    window_ids = jnp.arange(row_count + 2 * kernel_half_width)[None, :]
    return tap_values(
        (window_ids - row_ids - kernel_half_width).astype(jnp.float32), kernel_half_width
    )


def column_filters(column_count, kernel_half_width):
    source = jnp.arange(column_count)[:, None]
    target_patch = jnp.arange(column_count)[None, :]
    return tap_values((source - target_patch).astype(jnp.float32), kernel_half_width)


def convolve_all(padded, kernel_coeffs, height):
    kernel_half_width = KS // 2
    n, _, columns = padded.shape
    rows = row_filters(height, kernel_half_width).reshape(9, height, height + 2 * kernel_half_width)
    smooth = jnp.einsum("krj,njx->nkrx", rows, padded, precision=mxu_value)
    col_ops = column_filters(columns, kernel_half_width)
    x_line = 2.0 * jnp.arange(columns).astype(jnp.float32) / (columns - 1) - 1.0
    coef = kernel_coeffs.reshape(n, 3, 3, 3, 6)
    c = [coef[..., p, None] for p in range(6)]
    fx = jnp.stack(
        [
            c[0] + c[1] * x_line + c[3] * (x_line * x_line),
            c[2] + c[4] * x_line,
            jnp.broadcast_to(c[5], c[0].shape[:-1] + (columns,)),
        ],
        axis=4,
    )
    mixed = jnp.sum(
        col_ops[None, :, None, :, :, None, :] * fx[:, :, :, :, None, :, :], axis=3
    )
    mixed = mixed.reshape(n, 9, columns, 3 * columns)
    fields = jnp.einsum("nkry,nkyz->nrz", smooth, mixed, precision=mxu_value)
    y_line = (2.0 * jnp.arange(height).astype(jnp.float32) / (height - 1) - 1.0)[None, :, None]
    return (
        fields[:, :, :columns]
        + y_line * fields[:, :, columns : 2 * columns]
        + (y_line * y_line) * fields[:, :, 2 * columns :]
    )


def place_slots(flux_flat, weight_flat, offsets, patch_rows, patch_cols):
    slot_total, strip_rows, columns = flux_flat.shape
    group = math.gcd(slot_total, 16)
    pairs = jnp.stack([flux_flat, weight_flat], axis=1).reshape(
        slot_total // group, group, 2, strip_rows, columns
    )
    grouped_offsets = offsets.reshape(slot_total // group, group, offsets.shape[1])
    target_cols = jnp.arange(patch_cols)
    source_cols = jnp.arange(columns)
    target_rows = jnp.arange(patch_rows)
    source_rows = jnp.arange(strip_rows)

    def place_group(total, item):
        pixel_block_tile, block_offsets = item
        column_selection = (
            target_cols[None, None, :]
            == block_offsets[:, 1][:, None, None] + source_cols[None, :, None]
        ).astype(jnp.float32)
        row_select = (
            target_rows[None, :, None]
            == block_offsets[:, 0][:, None, None] + source_rows[None, None, :]
        ).astype(jnp.float32)
        broadened_width = jnp.einsum(
            "vmwn,vny->vmwy", pixel_block_tile, column_selection, precision=largest_value
        )
        return (
            total
            + jnp.einsum("gri,gkip->krp", row_select, broadened_width, precision=largest_value),
            None,
        )

    start = jnp.zeros((2, patch_rows, patch_cols), jnp.float32)
    placed, _ = lax.scan(place_group, start, (pairs, grouped_offsets))
    return (placed[0], placed[1])


def shards(
    exposures, variance, mask_bits, kernel_coeffs, ccd_visit, strip_patch, strip_row, strip_col
):
    ccd_count, height, columns = exposures.shape
    strip_total = strip_patch.shape[0]
    per_ccd = strip_total // ccd_count
    strip_rows = height // per_ccd
    devices = lax.axis_size("patch")
    capacity = 2 * strip_total // devices
    kernel_half_width = KS // 2
    usable = (jnp.bitwise_and(mask_bits, 3) != 3).astype(jnp.float32)
    visit_hot = (ccd_visit == jnp.arange(VISITS)[None, :]).astype(jnp.float32)
    local_count = jnp.sum(jnp.sum(usable, axis=(1, 2))[:, None] * visit_hot, axis=0)
    local_load = jnp.sum(jnp.sum(usable * variance, axis=(1, 2))[:, None] * visit_hot, axis=0)

    destination = strip_patch[:, 0]
    strip_ids = jnp.arange(strip_total)
    earlier = strip_ids[None, :] < strip_ids[:, None]
    same_target = destination[None, :] == destination[:, None]
    slot_rank = jnp.sum(jnp.logical_and(earlier, same_target).astype(jnp.int32), axis=1)
    slot_index = destination * capacity + slot_rank
    slot_total = devices * capacity
    chooser = (slot_index[None, :] == jnp.arange(slot_total)[:, None]).astype(jnp.float32)

    padded = jnp.pad(exposures, ((0, 0), (kernel_half_width, kernel_half_width), (0, 0)))
    convolved = convolve_all(padded, kernel_coeffs, height)
    tiles = jnp.concatenate(
        [
            (usable * convolved).reshape(strip_total, strip_rows, columns),
            usable.reshape(strip_total, strip_rows, columns),
        ],
        axis=1,
    ).reshape(strip_total, 2 * strip_rows * columns)
    packed = jnp.dot(chooser, tiles, precision=largest_value).reshape(
        devices, capacity * 2 * strip_rows, columns
    )
    strip_visit = jnp.repeat(ccd_visit[:, 0], per_ccd)
    placement = jnp.stack([strip_row, strip_col, strip_visit], axis=1).astype(jnp.float32)
    slot_meta = jnp.dot(chooser, placement, precision=largest_value).reshape(devices, capacity, 3)
    meta = jnp.zeros((devices, 8, columns), jnp.float32)
    meta = meta.at[:, 0:3, :capacity].set(jnp.swapaxes(slot_meta, 1, 2))
    meta = meta.at[:, 3, :VISITS].set(jnp.broadcast_to(local_count, (devices, VISITS)))
    meta = meta.at[:, 4, :VISITS].set(jnp.broadcast_to(local_load, (devices, VISITS)))
    payload = jnp.concatenate([packed, meta], axis=1)
    got = lax.all_to_all(payload, "patch", split_axis=0, concat_axis=0, tiled=True)
    body_rows = capacity * 2 * strip_rows
    got_meta = got[:, body_rows:, :]
    visit_count = jnp.sum(got_meta[:, 3, :VISITS], axis=0)
    visit_load = jnp.sum(got_meta[:, 4, :VISITS], axis=0)
    visit_weight = (visit_count + 1.0) / (visit_load + 1.0)
    slot_rows = got_meta[:, 0, :capacity].reshape(slot_total).astype(jnp.int32)
    slot_cols = got_meta[:, 1, :capacity].reshape(slot_total).astype(jnp.int32)
    slot_visit = got_meta[:, 2, :capacity].reshape(slot_total).astype(jnp.int32)
    slot_hot = (slot_visit[:, None] == jnp.arange(VISITS)[None, :]).astype(jnp.float32)
    slot_weight = jnp.sum(slot_hot * visit_weight[None, :], axis=1)
    body = got[:, :body_rows, :].reshape(slot_total, 2, strip_rows, columns)
    body = body * slot_weight[:, None, None, None]
    offsets = jnp.stack([slot_rows, slot_cols], axis=1)
    numerator, weight_map = place_slots(body[:, 0], body[:, 1], offsets, PH, PW)
    coadd_image = numerator / jnp.maximum(weight_map, 1.0)
    return (coadd_image[None], weight_map[None])


def solution(mesh):
    return jax.shard_map(
        shards,
        mesh=mesh,
        in_specs=(
            P(("band", "patch"), None, None),
            P(("band", "patch"), None, None),
            P(("band", "patch"), None, None),
            P(("band", "patch"), None, None),
            P(("band", "patch"), None),
            P(("band", "patch"), None),
            P(("band", "patch")),
            P(("band", "patch")),
        ),
        out_specs=(P(("band", "patch"), None, None), P(("band", "patch"), None, None)),
        check_vma=False,
    )
```

```python
import math

import jax
import numpy as np
import jax.numpy as jnp
from jax import lax
from jax.sharding import PartitionSpec as P

PH = 128
PW = 512
KS = 21
VISITS = 8


gauss_widths = (0.75, 1.5, 3.0)
largest_value = lax.Precision.HIGHEST
mxu_value = lax.Precision.HIGH


def tap_table(kernel_half_width):
    support = np.arange(-kernel_half_width, kernel_half_width + 1).astype(np.float64)
    tables = []
    for spread in gauss_widths:
        s32 = float(np.float32(spread))
        gauss_total = np.sum(np.exp(-support * support / (2.0 * s32 * s32)))
        profile = np.exp(-support * support / (2.0 * s32 * s32)) / gauss_total
        scaled = support / s32
        tables.append(np.stack([profile, profile * scaled, profile * scaled * scaled]))
    return np.stack(tables)


def row_blocks(block_rows, window_rows, kernel_half_width):
    taps = tap_table(kernel_half_width).reshape(9, 2 * kernel_half_width + 1)
    out = np.zeros((9, block_rows, window_rows), np.float64)
    for i in range(block_rows):
        out[:, i, i : i + 2 * kernel_half_width + 1] = taps
    return out.astype(np.float32)


def column_ops(column_count, kernel_half_width):
    taps = tap_table(kernel_half_width)
    out = np.zeros((3, 3, column_count, column_count), np.float64)
    for y in range(column_count):
        lo = max(0, y - kernel_half_width)
        hi = min(column_count, y + kernel_half_width + 1)
        for x in range(lo, hi):
            out[:, :, y, x] = taps[:, :, y - x + kernel_half_width]
    return out.astype(np.float32)


def convolve_all(exposures, kernel_coeffs):
    kernel_half_width = KS // 2
    n, height, columns = exposures.shape
    block = 8
    blocks = height // block
    span = 2 * kernel_half_width + block
    reach = -(-span // block)
    total_rows = (blocks + reach - 1) * block
    padded = jnp.pad(
        exposures, ((0, 0), (kernel_half_width, total_rows - height - kernel_half_width), (0, 0))
    ).reshape(n, blocks + reach - 1, block, columns)
    windows = jnp.concatenate([padded[:, j : j + blocks] for j in range(reach)], axis=2)
    rows = jnp.asarray(row_blocks(block, reach * block, kernel_half_width))
    smooth = jnp.einsum("kit,nqtx->nqkix", rows, windows, precision=mxu_value)
    col_ops = jnp.asarray(column_ops(columns, kernel_half_width))
    x_line = 2.0 * jnp.arange(columns).astype(jnp.float32) / (columns - 1) - 1.0
    coef = kernel_coeffs.reshape(n, 3, 3, 3, 6)
    c = [coef[..., p, None] for p in range(6)]
    fx = jnp.stack(
        [
            c[0] + c[1] * x_line + c[3] * (x_line * x_line),
            c[2] + c[4] * x_line,
            jnp.broadcast_to(c[5], c[0].shape[:-1] + (columns,)),
        ],
        axis=4,
    )
    mixed = jnp.sum(
        col_ops[None, :, None, :, :, None, :] * fx[:, :, :, :, None, :, :], axis=3
    )
    mixed = mixed.reshape(n, 9, columns, 3 * columns)
    fields = jnp.einsum("nqkiy,nkyz->nqiz", smooth, mixed, precision=mxu_value)
    fields = fields.reshape(n, height, 3 * columns)
    y_line = (2.0 * jnp.arange(height).astype(jnp.float32) / (height - 1) - 1.0)[None, :, None]
    return (
        fields[:, :, :columns]
        + y_line * fields[:, :, columns : 2 * columns]
        + (y_line * y_line) * fields[:, :, 2 * columns :]
    )


def place_slots(flux_flat, weight_flat, offsets, patch_rows, patch_cols):
    slot_total, strip_rows, columns = flux_flat.shape
    group = math.gcd(slot_total, 16)
    pairs = jnp.stack([flux_flat, weight_flat], axis=1).reshape(
        slot_total // group, group, 2, strip_rows, columns
    )
    grouped_offsets = offsets.reshape(slot_total // group, group, offsets.shape[1])
    target_cols = jnp.arange(patch_cols)
    source_cols = jnp.arange(columns)
    target_rows = jnp.arange(patch_rows)
    source_rows = jnp.arange(strip_rows)

    def place_group(total, item):
        pixel_block_tile, block_offsets = item
        column_selection = (
            target_cols[None, None, :]
            == block_offsets[:, 1][:, None, None] + source_cols[None, :, None]
        ).astype(jnp.float32)
        row_select = (
            target_rows[None, :, None]
            == block_offsets[:, 0][:, None, None] + source_rows[None, None, :]
        ).astype(jnp.float32)
        broadened_width = jnp.einsum(
            "vmwn,vny->vmwy", pixel_block_tile, column_selection, precision=largest_value
        )
        return (
            total
            + jnp.einsum("gri,gkip->krp", row_select, broadened_width, precision=largest_value),
            None,
        )

    start = jnp.zeros((2, patch_rows, patch_cols), jnp.float32)
    placed, _ = lax.scan(place_group, start, (pairs, grouped_offsets))
    return (placed[0], placed[1])


def shards(
    exposures, variance, mask_bits, kernel_coeffs, ccd_visit, strip_patch, strip_row, strip_col
):
    ccd_count, height, columns = exposures.shape
    strip_total = strip_patch.shape[0]
    per_ccd = strip_total // ccd_count
    strip_rows = height // per_ccd
    devices = lax.axis_size("patch")
    capacity = 2 * strip_total // devices
    usable = (jnp.bitwise_and(mask_bits, 3) != 3).astype(jnp.float32)
    visit_hot = (ccd_visit == jnp.arange(VISITS)[None, :]).astype(jnp.float32)
    local_count = jnp.sum(jnp.sum(usable, axis=(1, 2))[:, None] * visit_hot, axis=0)
    local_load = jnp.sum(jnp.sum(usable * variance, axis=(1, 2))[:, None] * visit_hot, axis=0)

    destination = strip_patch[:, 0]
    strip_ids = jnp.arange(strip_total)
    earlier = strip_ids[None, :] < strip_ids[:, None]
    same_target = destination[None, :] == destination[:, None]
    slot_rank = jnp.sum(jnp.logical_and(earlier, same_target).astype(jnp.int32), axis=1)
    slot_index = destination * capacity + slot_rank
    slot_total = devices * capacity
    chooser = (slot_index[None, :] == jnp.arange(slot_total)[:, None]).astype(jnp.float32)

    strip_visit = jnp.repeat(ccd_visit[:, 0], per_ccd)
    placement = jnp.stack([strip_row, strip_col, strip_visit], axis=1).astype(jnp.float32)
    slot_meta = jnp.dot(chooser, placement, precision=largest_value).reshape(devices, capacity, 3)
    meta = jnp.zeros((devices, 8, columns), jnp.float32)
    meta = meta.at[:, 0:3, :capacity].set(jnp.swapaxes(slot_meta, 1, 2))
    meta = meta.at[:, 3, :VISITS].set(jnp.broadcast_to(local_count, (devices, VISITS)))
    meta = meta.at[:, 4, :VISITS].set(jnp.broadcast_to(local_load, (devices, VISITS)))
    body_rows = capacity * strip_rows
    weight_tiles = usable.reshape(strip_total, strip_rows * columns)
    weight_packed = jnp.dot(chooser, weight_tiles, precision=largest_value).reshape(
        devices, body_rows, columns
    )
    first = jnp.concatenate([weight_packed, meta], axis=1)
    got_first = lax.all_to_all(first, "patch", split_axis=0, concat_axis=0, tiled=True)

    convolved = convolve_all(exposures, kernel_coeffs)
    flux_tiles = (usable * convolved).reshape(strip_total, strip_rows * columns)
    flux_packed = jnp.dot(chooser, flux_tiles, precision=largest_value).reshape(
        devices, body_rows, columns
    )
    got_flux = lax.all_to_all(flux_packed, "patch", split_axis=0, concat_axis=0, tiled=True)

    got_meta = got_first[:, body_rows:, :]
    visit_count = jnp.sum(got_meta[:, 3, :VISITS], axis=0)
    visit_load = jnp.sum(got_meta[:, 4, :VISITS], axis=0)
    visit_weight = (visit_count + 1.0) / (visit_load + 1.0)
    slot_rows = got_meta[:, 0, :capacity].reshape(slot_total).astype(jnp.int32)
    slot_cols = got_meta[:, 1, :capacity].reshape(slot_total).astype(jnp.int32)
    slot_visit = got_meta[:, 2, :capacity].reshape(slot_total).astype(jnp.int32)
    slot_hot = (slot_visit[:, None] == jnp.arange(VISITS)[None, :]).astype(jnp.float32)
    slot_weight = jnp.sum(slot_hot * visit_weight[None, :], axis=1)
    weight_body = got_first[:, :body_rows, :].reshape(slot_total, strip_rows, columns)
    flux_body = got_flux.reshape(slot_total, strip_rows, columns)
    weight_body = weight_body * slot_weight[:, None, None]
    flux_body = flux_body * slot_weight[:, None, None]
    offsets = jnp.stack([slot_rows, slot_cols], axis=1)
    numerator, weight_map = place_slots(flux_body, weight_body, offsets, PH, PW)
    coadd_image = numerator / jnp.maximum(weight_map, 1.0)
    return (coadd_image[None], weight_map[None])


def solution(mesh):
    return jax.shard_map(
        shards,
        mesh=mesh,
        in_specs=(
            P(("band", "patch"), None, None),
            P(("band", "patch"), None, None),
            P(("band", "patch"), None, None),
            P(("band", "patch"), None, None),
            P(("band", "patch"), None),
            P(("band", "patch"), None),
            P(("band", "patch")),
            P(("band", "patch")),
        ),
        out_specs=(P(("band", "patch"), None, None), P(("band", "patch"), None, None)),
        check_vma=False,
    )
```

```python
import jax
import numpy as np
import jax.numpy as jnp
from jax import lax
from jax.experimental import pallas as pl
from jax.experimental.pallas import tpu as pltpu
from jax.sharding import PartitionSpec as P

PH = 128
PW = 512
KS = 21
VISITS = 8


gauss_widths = (0.75, 1.5, 3.0)
largest_value = lax.Precision.HIGHEST
mxu_value = lax.Precision.HIGH


def tap_table(kernel_half_width):
    support = np.arange(-kernel_half_width, kernel_half_width + 1).astype(np.float64)
    tables = []
    for spread in gauss_widths:
        s32 = float(np.float32(spread))
        gauss_total = np.sum(np.exp(-support * support / (2.0 * s32 * s32)))
        profile = np.exp(-support * support / (2.0 * s32 * s32)) / gauss_total
        scaled = support / s32
        tables.append(np.stack([profile, profile * scaled, profile * scaled * scaled]))
    return np.stack(tables)


def row_blocks(block_rows, window_rows, kernel_half_width):
    taps = tap_table(kernel_half_width).reshape(9, 2 * kernel_half_width + 1)
    out = np.zeros((9, block_rows, window_rows), np.float64)
    for i in range(block_rows):
        out[:, i, i : i + 2 * kernel_half_width + 1] = taps
    return out.astype(np.float32)


def column_ops(column_count, kernel_half_width):
    taps = tap_table(kernel_half_width)
    out = np.zeros((3, 3, column_count, column_count), np.float64)
    for y in range(column_count):
        lo = max(0, y - kernel_half_width)
        hi = min(column_count, y + kernel_half_width + 1)
        for x in range(lo, hi):
            out[:, :, y, x] = taps[:, :, y - x + kernel_half_width]
    return out.astype(np.float32)


def convolve_all(exposures, kernel_coeffs):
    kernel_half_width = KS // 2
    n, height, columns = exposures.shape
    block = 8
    blocks = height // block
    span = 2 * kernel_half_width + block
    reach = -(-span // block)
    total_rows = (blocks + reach - 1) * block
    padded = jnp.pad(
        exposures, ((0, 0), (kernel_half_width, total_rows - height - kernel_half_width), (0, 0))
    ).reshape(n, blocks + reach - 1, block, columns)
    windows = jnp.concatenate([padded[:, j : j + blocks] for j in range(reach)], axis=2)
    rows = jnp.asarray(row_blocks(block, reach * block, kernel_half_width))
    smooth = jnp.einsum("kit,nqtx->nqkix", rows, windows, precision=mxu_value)
    col_ops = jnp.asarray(column_ops(columns, kernel_half_width))
    x_line = 2.0 * jnp.arange(columns).astype(jnp.float32) / (columns - 1) - 1.0
    coef = kernel_coeffs.reshape(n, 3, 3, 3, 6)
    c = [coef[..., p, None] for p in range(6)]
    fx = jnp.stack(
        [
            c[0] + c[1] * x_line + c[3] * (x_line * x_line),
            c[2] + c[4] * x_line,
            jnp.broadcast_to(c[5], c[0].shape[:-1] + (columns,)),
        ],
        axis=4,
    )
    mixed = jnp.sum(
        col_ops[None, :, None, :, :, None, :] * fx[:, :, :, :, None, :, :], axis=3
    )
    mixed = mixed.reshape(n, 9, columns, 3 * columns)
    fields = jnp.einsum("nqkiy,nkyz->nqiz", smooth, mixed, precision=mxu_value)
    fields = fields.reshape(n, height, 3 * columns)
    y_line = (2.0 * jnp.arange(height).astype(jnp.float32) / (height - 1) - 1.0)[None, :, None]
    return (
        fields[:, :, :columns]
        + y_line * fields[:, :, columns : 2 * columns]
        + (y_line * y_line) * fields[:, :, 2 * columns :]
    )


def place_kernel(rows_ref, cols_ref, wts_ref, flux_ref, weight_ref, coadd_ref, wmap_ref, acc_n, acc_w):
    slots, strip_rows, lanes = flux_ref.shape
    lane_blocks = acc_n.shape[0] - 1
    out_rows = coadd_ref.shape[0]
    acc_n[...] = jnp.zeros(acc_n.shape, jnp.float32)
    acc_w[...] = jnp.zeros(acc_w.shape, jnp.float32)
    lane = lax.broadcasted_iota(jnp.int32, (strip_rows, lanes), 1)
    sub = lax.broadcasted_iota(jnp.int32, (strip_rows, lanes), 0)

    def body(s, carry):
        r = rows_ref[s]
        c = cols_ref[s]
        wt = wts_ref[s]
        q = c // lanes
        rem = c - q * lanes
        rq = r // strip_rows
        rr = r - rq * strip_rows
        lane_lo = lane >= rem
        sub_lo = sub >= rr
        top = pl.multiple_of(rq * strip_rows, strip_rows)
        nxt = pl.multiple_of(top + strip_rows, strip_rows)
        for src, acc in ((flux_ref, acc_n), (weight_ref, acc_w)):
            v = src[s] * wt
            v = pltpu.roll(v, rem, 1)
            v = pltpu.roll(v, rr, 0)
            zero = jnp.zeros_like(v)
            a = jnp.where(sub_lo, v, zero)
            b = v - a
            acc[q, pl.ds(top, strip_rows), :] += jnp.where(lane_lo, a, zero)
            acc[q + 1, pl.ds(top, strip_rows), :] += jnp.where(lane_lo, zero, a)
            acc[q, pl.ds(nxt, strip_rows), :] += jnp.where(lane_lo, b, zero)
            acc[q + 1, pl.ds(nxt, strip_rows), :] += jnp.where(lane_lo, zero, b)
        return carry

    lax.fori_loop(0, slots, body, 0)
    for j in range(lane_blocks):
        n = acc_n[j, pl.ds(0, out_rows), :]
        w = acc_w[j, pl.ds(0, out_rows), :]
        wmap_ref[:, pl.ds(j * lanes, lanes)] = w
        coadd_ref[:, pl.ds(j * lanes, lanes)] = n / jnp.maximum(w, 1.0)


def place(flux, weight, rows, cols, wts, patch_rows, patch_cols):
    slots, strip_rows, lanes = flux.shape
    lane_blocks = patch_cols // lanes
    smem = pltpu.SMEM
    return pl.pallas_call(
        place_kernel,
        out_shape=(
            jax.ShapeDtypeStruct((patch_rows, patch_cols), jnp.float32),
            jax.ShapeDtypeStruct((patch_rows, patch_cols), jnp.float32),
        ),
        in_specs=[
            pl.BlockSpec(memory_space=smem),
            pl.BlockSpec(memory_space=smem),
            pl.BlockSpec(memory_space=smem),
            pl.BlockSpec(memory_space=pltpu.VMEM),
            pl.BlockSpec(memory_space=pltpu.VMEM),
        ],
        out_specs=(pl.BlockSpec(memory_space=pltpu.VMEM), pl.BlockSpec(memory_space=pltpu.VMEM)),
        scratch_shapes=[
            pltpu.VMEM((lane_blocks + 1, patch_rows + strip_rows, lanes), jnp.float32),
            pltpu.VMEM((lane_blocks + 1, patch_rows + strip_rows, lanes), jnp.float32),
        ],
    )(rows, cols, wts, flux, weight)


def shards(
    exposures, variance, mask_bits, kernel_coeffs, ccd_visit, strip_patch, strip_row, strip_col
):
    ccd_count, height, columns = exposures.shape
    strip_total = strip_patch.shape[0]
    per_ccd = strip_total // ccd_count
    strip_rows = height // per_ccd
    devices = lax.axis_size("patch")
    capacity = 2 * strip_total // devices
    usable = (jnp.bitwise_and(mask_bits, 3) != 3).astype(jnp.float32)
    visit_hot = (ccd_visit == jnp.arange(VISITS)[None, :]).astype(jnp.float32)
    local_count = jnp.sum(jnp.sum(usable, axis=(1, 2))[:, None] * visit_hot, axis=0)
    local_load = jnp.sum(jnp.sum(usable * variance, axis=(1, 2))[:, None] * visit_hot, axis=0)

    destination = strip_patch[:, 0]
    strip_ids = jnp.arange(strip_total)
    earlier = strip_ids[None, :] < strip_ids[:, None]
    same_target = destination[None, :] == destination[:, None]
    slot_rank = jnp.sum(jnp.logical_and(earlier, same_target).astype(jnp.int32), axis=1)
    slot_index = destination * capacity + slot_rank
    slot_total = devices * capacity
    chooser = (slot_index[None, :] == jnp.arange(slot_total)[:, None]).astype(jnp.float32)

    strip_visit = jnp.repeat(ccd_visit[:, 0], per_ccd)
    placement = jnp.stack([strip_row, strip_col, strip_visit], axis=1).astype(jnp.float32)
    slot_meta = jnp.dot(chooser, placement, precision=largest_value).reshape(devices, capacity, 3)
    meta = jnp.zeros((devices, 8, columns), jnp.float32)
    meta = meta.at[:, 0:3, :capacity].set(jnp.swapaxes(slot_meta, 1, 2))
    meta = meta.at[:, 3, :VISITS].set(jnp.broadcast_to(local_count, (devices, VISITS)))
    meta = meta.at[:, 4, :VISITS].set(jnp.broadcast_to(local_load, (devices, VISITS)))
    body_rows = capacity * strip_rows
    weight_tiles = usable.reshape(strip_total, strip_rows * columns)
    weight_packed = jnp.dot(chooser, weight_tiles, precision=largest_value).reshape(
        devices, body_rows, columns
    )
    first = jnp.concatenate([weight_packed, meta], axis=1)
    got_first = lax.all_to_all(first, "patch", split_axis=0, concat_axis=0, tiled=True)

    convolved = convolve_all(exposures, kernel_coeffs)
    flux_tiles = (usable * convolved).reshape(strip_total, strip_rows * columns)
    flux_packed = jnp.dot(chooser, flux_tiles, precision=largest_value).reshape(
        devices, body_rows, columns
    )
    got_flux = lax.all_to_all(flux_packed, "patch", split_axis=0, concat_axis=0, tiled=True)

    got_meta = got_first[:, body_rows:, :]
    visit_count = jnp.sum(got_meta[:, 3, :VISITS], axis=0)
    visit_load = jnp.sum(got_meta[:, 4, :VISITS], axis=0)
    visit_weight = (visit_count + 1.0) / (visit_load + 1.0)
    slot_rows = got_meta[:, 0, :capacity].reshape(slot_total).astype(jnp.int32)
    slot_cols = got_meta[:, 1, :capacity].reshape(slot_total).astype(jnp.int32)
    slot_visit = got_meta[:, 2, :capacity].reshape(slot_total).astype(jnp.int32)
    slot_hot = (slot_visit[:, None] == jnp.arange(VISITS)[None, :]).astype(jnp.float32)
    slot_weight = jnp.sum(slot_hot * visit_weight[None, :], axis=1)
    weight_body = got_first[:, :body_rows, :].reshape(slot_total, strip_rows, columns)
    flux_body = got_flux.reshape(slot_total, strip_rows, columns)
    coadd_image, weight_map = place(
        flux_body, weight_body, slot_rows, slot_cols, slot_weight, PH, PW
    )
    return (coadd_image[None], weight_map[None])


def solution(mesh):
    return jax.shard_map(
        shards,
        mesh=mesh,
        in_specs=(
            P(("band", "patch"), None, None),
            P(("band", "patch"), None, None),
            P(("band", "patch"), None, None),
            P(("band", "patch"), None, None),
            P(("band", "patch"), None),
            P(("band", "patch"), None),
            P(("band", "patch")),
            P(("band", "patch")),
        ),
        out_specs=(P(("band", "patch"), None, None), P(("band", "patch"), None, None)),
        check_vma=False,
    )
```

```python
import jax
import numpy as np
import jax.numpy as jnp
from jax import lax
from jax.experimental import pallas as pl
from jax.experimental.pallas import tpu as pltpu
from jax.sharding import PartitionSpec as P

PH = 128
PW = 512
KS = 21
VISITS = 8


gauss_widths = (0.75, 1.5, 3.0)
largest_value = lax.Precision.HIGHEST
mxu_value = lax.Precision.HIGH


def tap_table(kernel_half_width):
    support = np.arange(-kernel_half_width, kernel_half_width + 1).astype(np.float64)
    tables = []
    for spread in gauss_widths:
        s32 = float(np.float32(spread))
        gauss_total = np.sum(np.exp(-support * support / (2.0 * s32 * s32)))
        profile = np.exp(-support * support / (2.0 * s32 * s32)) / gauss_total
        scaled = support / s32
        tables.append(np.stack([profile, profile * scaled, profile * scaled * scaled]))
    return np.stack(tables)


def row_blocks(block_rows, window_rows, kernel_half_width):
    taps = tap_table(kernel_half_width).reshape(9, 2 * kernel_half_width + 1)
    out = np.zeros((9, block_rows, window_rows), np.float64)
    for i in range(block_rows):
        out[:, i, i : i + 2 * kernel_half_width + 1] = taps
    return out.astype(np.float32)


def column_ops(column_count, kernel_half_width):
    taps = tap_table(kernel_half_width)
    out = np.zeros((3, 3, column_count, column_count), np.float64)
    for y in range(column_count):
        lo = max(0, y - kernel_half_width)
        hi = min(column_count, y + kernel_half_width + 1)
        for x in range(lo, hi):
            out[:, :, y, x] = taps[:, :, y - x + kernel_half_width]
    return out.astype(np.float32)


def convolve_all(exposures, kernel_coeffs):
    kernel_half_width = KS // 2
    n, height, columns = exposures.shape
    block = 8
    blocks = height // block
    span = 2 * kernel_half_width + block
    reach = -(-span // block)
    total_rows = (blocks + reach - 1) * block
    padded = jnp.pad(
        exposures, ((0, 0), (kernel_half_width, total_rows - height - kernel_half_width), (0, 0))
    ).reshape(n, blocks + reach - 1, block, columns)
    windows = jnp.concatenate([padded[:, j : j + blocks] for j in range(reach)], axis=2)
    rows = jnp.asarray(row_blocks(block, reach * block, kernel_half_width))
    smooth = jnp.einsum("kit,nqtx->nqkix", rows, windows, precision=mxu_value)
    col_ops = jnp.asarray(column_ops(columns, kernel_half_width))
    x_line = 2.0 * jnp.arange(columns).astype(jnp.float32) / (columns - 1) - 1.0
    coef = kernel_coeffs.reshape(n, 3, 3, 3, 6)
    c = [coef[..., p, None] for p in range(6)]
    fx = jnp.stack(
        [
            c[0] + c[1] * x_line + c[3] * (x_line * x_line),
            c[2] + c[4] * x_line,
            jnp.broadcast_to(c[5], c[0].shape[:-1] + (columns,)),
        ],
        axis=4,
    )
    mixed = jnp.sum(
        col_ops[None, :, None, :, :, None, :] * fx[:, :, :, :, None, :, :], axis=3
    )
    mixed = mixed.reshape(n, 9, columns, 3 * columns)
    fields = jnp.einsum("nqkiy,nkyz->nqiz", smooth, mixed, precision=mxu_value)
    fields = fields.reshape(n, height, 3 * columns)
    y_line = (2.0 * jnp.arange(height).astype(jnp.float32) / (height - 1) - 1.0)[None, :, None]
    return (
        fields[:, :, :columns]
        + y_line * fields[:, :, columns : 2 * columns]
        + (y_line * y_line) * fields[:, :, 2 * columns :]
    )


def place_kernel(rows_ref, cols_ref, wts_ref, tiles_ref, coadd_ref, wmap_ref, acc_n, acc_w):
    slots, tile_rows, lanes = tiles_ref.shape
    strip_rows = tile_rows // 2
    lane_blocks = acc_n.shape[0] - 1
    out_rows = coadd_ref.shape[0]
    acc_n[...] = jnp.zeros(acc_n.shape, jnp.float32)
    acc_w[...] = jnp.zeros(acc_w.shape, jnp.float32)
    lane = lax.broadcasted_iota(jnp.int32, (strip_rows, lanes), 1)
    sub = lax.broadcasted_iota(jnp.int32, (strip_rows, lanes), 0)

    def body(s, carry):
        r = rows_ref[s]
        c = cols_ref[s]
        wt = wts_ref[s]
        q = c // lanes
        rem = c - q * lanes
        rq = r // strip_rows
        rr = r - rq * strip_rows
        lane_lo = lane >= rem
        sub_lo = sub >= rr
        top = pl.multiple_of(rq * strip_rows, strip_rows)
        nxt = pl.multiple_of(top + strip_rows, strip_rows)
        for part, acc in ((1, acc_n), (0, acc_w)):
            v = tiles_ref[s, pl.ds(part * strip_rows, strip_rows), :] * wt
            v = pltpu.roll(v, rem, 1)
            v = pltpu.roll(v, rr, 0)
            zero = jnp.zeros_like(v)
            a = jnp.where(sub_lo, v, zero)
            b = v - a
            acc[q, pl.ds(top, strip_rows), :] += jnp.where(lane_lo, a, zero)
            acc[q + 1, pl.ds(top, strip_rows), :] += jnp.where(lane_lo, zero, a)
            acc[q, pl.ds(nxt, strip_rows), :] += jnp.where(lane_lo, b, zero)
            acc[q + 1, pl.ds(nxt, strip_rows), :] += jnp.where(lane_lo, zero, b)
        return carry

    lax.fori_loop(0, slots, body, 0, unroll=4)
    for j in range(lane_blocks):
        n = acc_n[j, pl.ds(0, out_rows), :]
        w = acc_w[j, pl.ds(0, out_rows), :]
        wmap_ref[:, pl.ds(j * lanes, lanes)] = w
        coadd_ref[:, pl.ds(j * lanes, lanes)] = n / jnp.maximum(w, 1.0)


def place(tiles, rows, cols, wts, patch_rows, patch_cols):
    slots, tile_rows, lanes = tiles.shape
    strip_rows = tile_rows // 2
    lane_blocks = patch_cols // lanes
    smem = pltpu.SMEM
    return pl.pallas_call(
        place_kernel,
        out_shape=(
            jax.ShapeDtypeStruct((patch_rows, patch_cols), jnp.float32),
            jax.ShapeDtypeStruct((patch_rows, patch_cols), jnp.float32),
        ),
        in_specs=[
            pl.BlockSpec(memory_space=smem),
            pl.BlockSpec(memory_space=smem),
            pl.BlockSpec(memory_space=smem),
            pl.BlockSpec(memory_space=pltpu.VMEM),
        ],
        out_specs=(pl.BlockSpec(memory_space=pltpu.VMEM), pl.BlockSpec(memory_space=pltpu.VMEM)),
        scratch_shapes=[
            pltpu.VMEM((lane_blocks + 1, patch_rows + strip_rows, lanes), jnp.float32),
            pltpu.VMEM((lane_blocks + 1, patch_rows + strip_rows, lanes), jnp.float32),
        ],
    )(rows, cols, wts, tiles)


def shards(
    exposures, variance, mask_bits, kernel_coeffs, ccd_visit, strip_patch, strip_row, strip_col
):
    ccd_count, height, columns = exposures.shape
    strip_total = strip_patch.shape[0]
    per_ccd = strip_total // ccd_count
    strip_rows = height // per_ccd
    devices = lax.axis_size("patch")
    capacity = 2 * strip_total // devices
    usable = (jnp.bitwise_and(mask_bits, 3) != 3).astype(jnp.float32)
    visit_hot = (ccd_visit == jnp.arange(VISITS)[None, :]).astype(jnp.float32)
    local_count = jnp.sum(jnp.sum(usable, axis=(1, 2))[:, None] * visit_hot, axis=0)
    local_load = jnp.sum(jnp.sum(usable * variance, axis=(1, 2))[:, None] * visit_hot, axis=0)

    destination = strip_patch[:, 0]
    strip_ids = jnp.arange(strip_total)
    earlier = strip_ids[None, :] < strip_ids[:, None]
    same_target = destination[None, :] == destination[:, None]
    slot_rank = jnp.sum(jnp.logical_and(earlier, same_target).astype(jnp.int32), axis=1)
    slot_index = destination * capacity + slot_rank
    slot_total = devices * capacity
    chooser = (slot_index[None, :] == jnp.arange(slot_total)[:, None]).astype(jnp.float32)

    strip_visit = jnp.repeat(ccd_visit[:, 0], per_ccd)
    placement = jnp.stack([strip_row, strip_col, strip_visit], axis=1).astype(jnp.float32)
    slot_meta = jnp.dot(chooser, placement, precision=largest_value).reshape(devices, capacity, 3)
    meta = jnp.zeros((devices, 8, columns), jnp.float32)
    meta = meta.at[:, 0:3, :capacity].set(jnp.swapaxes(slot_meta, 1, 2))
    meta = meta.at[:, 3, :VISITS].set(jnp.broadcast_to(local_count, (devices, VISITS)))
    meta = meta.at[:, 4, :VISITS].set(jnp.broadcast_to(local_load, (devices, VISITS)))
    body_rows = capacity * strip_rows
    convolved = convolve_all(exposures, kernel_coeffs)
    tiles = jnp.concatenate(
        [
            usable.reshape(strip_total, strip_rows * columns),
            (usable * convolved).reshape(strip_total, strip_rows * columns),
        ],
        axis=1,
    )
    packed = jnp.dot(chooser, tiles, precision=largest_value).reshape(
        devices, 2 * body_rows, columns
    )
    payload = jnp.concatenate([packed, meta], axis=1)
    got = lax.all_to_all(payload, "patch", split_axis=0, concat_axis=0, tiled=True)
    got_meta = got[:, 2 * body_rows :, :]
    visit_count = jnp.sum(got_meta[:, 3, :VISITS], axis=0)
    visit_load = jnp.sum(got_meta[:, 4, :VISITS], axis=0)
    visit_weight = (visit_count + 1.0) / (visit_load + 1.0)
    slot_rows = got_meta[:, 0, :capacity].reshape(slot_total).astype(jnp.int32)
    slot_cols = got_meta[:, 1, :capacity].reshape(slot_total).astype(jnp.int32)
    slot_visit = got_meta[:, 2, :capacity].reshape(slot_total).astype(jnp.int32)
    slot_hot = (slot_visit[:, None] == jnp.arange(VISITS)[None, :]).astype(jnp.float32)
    slot_weight = jnp.sum(slot_hot * visit_weight[None, :], axis=1)
    body = got[:, : 2 * body_rows].reshape(slot_total, 2 * strip_rows, columns)
    coadd_image, weight_map = place(body, slot_rows, slot_cols, slot_weight, PH, PW)
    return (coadd_image[None], weight_map[None])


def solution(mesh):
    return jax.shard_map(
        shards,
        mesh=mesh,
        in_specs=(
            P(("band", "patch"), None, None),
            P(("band", "patch"), None, None),
            P(("band", "patch"), None, None),
            P(("band", "patch"), None, None),
            P(("band", "patch"), None),
            P(("band", "patch"), None),
            P(("band", "patch")),
            P(("band", "patch")),
        ),
        out_specs=(P(("band", "patch"), None, None), P(("band", "patch"), None, None)),
        check_vma=False,
    )
```

```python
import jax
import numpy as np
import jax.numpy as jnp
from jax import lax
from jax.experimental import pallas as pl
from jax.experimental.pallas import tpu as pltpu
from jax.sharding import PartitionSpec as P


PH = 128
PW = 512
KS = 21
VISITS = 8


gauss_widths = (0.75, 1.5, 3.0)
largest_value = lax.Precision.HIGHEST
mxu_value = lax.Precision.HIGH


def tap_table(kernel_half_width):
    support = np.arange(-kernel_half_width, kernel_half_width + 1).astype(np.float64)
    tables = []
    for spread in gauss_widths:
        s32 = float(np.float32(spread))
        gauss_total = np.sum(np.exp(-support * support / (2.0 * s32 * s32)))
        profile = np.exp(-support * support / (2.0 * s32 * s32)) / gauss_total
        scaled = support / s32
        tables.append(np.stack([profile, profile * scaled, profile * scaled * scaled]))
    return np.stack(tables)


def row_blocks(block_rows, window_rows, kernel_half_width):
    taps = tap_table(kernel_half_width).reshape(9, 2 * kernel_half_width + 1)
    out = np.zeros((9, block_rows, window_rows), np.float64)
    for i in range(block_rows):
        out[:, i, i : i + 2 * kernel_half_width + 1] = taps
    return out.astype(np.float32)


def column_ops(column_count, kernel_half_width):
    taps = tap_table(kernel_half_width)
    out = np.zeros((3, 3, column_count, column_count), np.float64)
    for y in range(column_count):
        lo = max(0, y - kernel_half_width)
        hi = min(column_count, y + kernel_half_width + 1)
        for x in range(lo, hi):
            out[:, :, y, x] = taps[:, :, y - x + kernel_half_width]
    return out.astype(np.float32)


def convolve_all(exposures, kernel_coeffs):
    kernel_half_width = KS // 2
    n, height, columns = exposures.shape
    block = 8
    blocks = height // block
    span = 2 * kernel_half_width + block
    reach = -(-span // block)
    total_rows = (blocks + reach - 1) * block
    padded = jnp.pad(
        exposures, ((0, 0), (kernel_half_width, total_rows - height - kernel_half_width), (0, 0))
    ).reshape(n, blocks + reach - 1, block, columns)
    windows = jnp.concatenate([padded[:, j : j + blocks] for j in range(reach)], axis=2)
    rows = jnp.asarray(row_blocks(block, reach * block, kernel_half_width))
    smooth = jnp.einsum("kit,nqtx->nqkix", rows, windows, precision=mxu_value)
    col_ops = jnp.asarray(column_ops(columns, kernel_half_width))
    x_line = 2.0 * jnp.arange(columns).astype(jnp.float32) / (columns - 1) - 1.0
    coef = kernel_coeffs.reshape(n, 3, 3, 3, 6)
    c = [coef[..., p, None] for p in range(6)]
    fx = jnp.stack(
        [
            c[0] + c[1] * x_line + c[3] * (x_line * x_line),
            c[2] + c[4] * x_line,
            jnp.broadcast_to(c[5], c[0].shape[:-1] + (columns,)),
        ],
        axis=4,
    )
    mixed = jnp.sum(
        col_ops[None, :, None, :, :, None, :] * fx[:, :, :, :, None, :, :], axis=3
    )
    mixed = mixed.reshape(n, 9, columns, 3 * columns)
    fields = jnp.einsum("nqkiy,nkyz->nqiz", smooth, mixed, precision=mxu_value)
    fields = fields.reshape(n, height, 3 * columns)
    y_line = (2.0 * jnp.arange(height).astype(jnp.float32) / (height - 1) - 1.0)[None, :, None]
    return (
        fields[:, :, :columns]
        + y_line * fields[:, :, columns : 2 * columns]
        + (y_line * y_line) * fields[:, :, 2 * columns :]
    )


def place_kernel(rows_ref, cols_ref, wts_ref, tiles_ref, coadd_ref, wmap_ref, acc_n, acc_w):
    slots, tile_rows, lanes = tiles_ref.shape
    strip_rows = tile_rows // 2
    lane_blocks = acc_n.shape[0] - 1
    out_rows = coadd_ref.shape[0]
    acc_n[...] = jnp.zeros(acc_n.shape, jnp.float32)
    acc_w[...] = jnp.zeros(acc_w.shape, jnp.float32)
    lane = lax.broadcasted_iota(jnp.int32, (strip_rows, lanes), 1)
    sub = lax.broadcasted_iota(jnp.int32, (strip_rows, lanes), 0)

    def body(s, carry):
        r = rows_ref[s]
        c = cols_ref[s]
        wt = wts_ref[s]
        q = c // lanes
        rem = c - q * lanes
        rq = r // strip_rows
        rr = r - rq * strip_rows
        lane_lo = lane >= rem
        sub_lo = sub >= rr
        top = pl.multiple_of(rq * strip_rows, strip_rows)
        nxt = pl.multiple_of(top + strip_rows, strip_rows)
        for part, acc in ((1, acc_n), (0, acc_w)):
            v = tiles_ref[s, pl.ds(part * strip_rows, strip_rows), :] * wt
            v = pltpu.roll(v, rem, 1)
            v = pltpu.roll(v, rr, 0)
            zero = jnp.zeros_like(v)
            a = jnp.where(sub_lo, v, zero)
            b = v - a
            acc[q, pl.ds(top, strip_rows), :] += jnp.where(lane_lo, a, zero)
            acc[q + 1, pl.ds(top, strip_rows), :] += jnp.where(lane_lo, zero, a)
            acc[q, pl.ds(nxt, strip_rows), :] += jnp.where(lane_lo, b, zero)
            acc[q + 1, pl.ds(nxt, strip_rows), :] += jnp.where(lane_lo, zero, b)
        return carry

    lax.fori_loop(0, slots, body, 0, unroll=4)
    for j in range(lane_blocks):
        n = acc_n[j, pl.ds(0, out_rows), :]
        w = acc_w[j, pl.ds(0, out_rows), :]
        wmap_ref[:, pl.ds(j * lanes, lanes)] = w
        coadd_ref[:, pl.ds(j * lanes, lanes)] = n / jnp.maximum(w, 1.0)


def place(tiles, rows, cols, wts, patch_rows, patch_cols):
    slots, tile_rows, lanes = tiles.shape
    strip_rows = tile_rows // 2
    lane_blocks = patch_cols // lanes
    smem = pltpu.SMEM
    return pl.pallas_call(
        place_kernel,
        out_shape=(
            jax.ShapeDtypeStruct((patch_rows, patch_cols), jnp.float32),
            jax.ShapeDtypeStruct((patch_rows, patch_cols), jnp.float32),
        ),
        in_specs=[
            pl.BlockSpec(memory_space=smem),
            pl.BlockSpec(memory_space=smem),
            pl.BlockSpec(memory_space=smem),
            pl.BlockSpec(memory_space=pltpu.VMEM),
        ],
        out_specs=(pl.BlockSpec(memory_space=pltpu.VMEM), pl.BlockSpec(memory_space=pltpu.VMEM)),
        scratch_shapes=[
            pltpu.VMEM((lane_blocks + 1, patch_rows + strip_rows, lanes), jnp.float32),
            pltpu.VMEM((lane_blocks + 1, patch_rows + strip_rows, lanes), jnp.float32),
        ],
    )(rows, cols, wts, tiles)


def shards(
    exposures, variance, mask_bits, kernel_coeffs, ccd_visit, strip_patch, strip_row, strip_col
):
    ccd_count, height, columns = exposures.shape
    strip_total = strip_patch.shape[0]
    per_ccd = strip_total // ccd_count
    strip_rows = height // per_ccd
    devices = lax.axis_size("patch")
    capacity = 2 * strip_total // devices
    usable = (jnp.bitwise_and(mask_bits, 3) != 3).astype(jnp.float32)
    visit_hot = (ccd_visit == jnp.arange(VISITS)[None, :]).astype(jnp.float32)
    local_count = jnp.sum(jnp.sum(usable, axis=(1, 2))[:, None] * visit_hot, axis=0)
    local_load = jnp.sum(jnp.sum(usable * variance, axis=(1, 2))[:, None] * visit_hot, axis=0)

    destination = strip_patch[:, 0]
    strip_ids = jnp.arange(strip_total)
    earlier = strip_ids[None, :] < strip_ids[:, None]
    same_target = destination[None, :] == destination[:, None]
    slot_rank = jnp.sum(jnp.logical_and(earlier, same_target).astype(jnp.int32), axis=1)
    slot_index = destination * capacity + slot_rank
    slot_total = devices * capacity
    chooser = (slot_index[None, :] == jnp.arange(slot_total)[:, None]).astype(jnp.float32)

    strip_visit = jnp.repeat(ccd_visit[:, 0], per_ccd)
    placement = jnp.stack([strip_row, strip_col, strip_visit], axis=1).astype(jnp.float32)
    slot_meta = jnp.dot(chooser, placement, precision=largest_value).reshape(devices, capacity, 3)
    meta = jnp.zeros((devices, 8, columns), jnp.float32)
    meta = meta.at[:, 0:3, :capacity].set(jnp.swapaxes(slot_meta, 1, 2))
    meta = meta.at[:, 3, :VISITS].set(jnp.broadcast_to(local_count, (devices, VISITS)))
    meta = meta.at[:, 4, :VISITS].set(jnp.broadcast_to(local_load, (devices, VISITS)))
    body_rows = capacity * strip_rows
    convolved = convolve_all(exposures, kernel_coeffs)
    tiles = jnp.concatenate(
        [
            usable.reshape(strip_total, strip_rows * columns),
            (usable * convolved).reshape(strip_total, strip_rows * columns),
        ],
        axis=1,
    )
    packed = jnp.dot(chooser, tiles, precision=largest_value).reshape(
        devices, 2 * body_rows, columns
    )
    payload = jnp.concatenate([packed, meta], axis=1)
    me = lax.axis_index("patch")
    received = [lax.dynamic_index_in_dim(payload, me, 0, keepdims=False)]
    for shift in range(1, devices):
        chunk = lax.dynamic_index_in_dim(payload, (me + shift) % devices, 0, keepdims=False)
        pairs = [(i, (i + shift) % devices) for i in range(devices)]
        received.append(lax.ppermute(chunk, "patch", pairs))
    got = jnp.stack(received, axis=0)
    got_meta = got[:, 2 * body_rows :, :]
    visit_count = jnp.sum(got_meta[:, 3, :VISITS], axis=0)
    visit_load = jnp.sum(got_meta[:, 4, :VISITS], axis=0)
    visit_weight = (visit_count + 1.0) / (visit_load + 1.0)
    slot_rows = got_meta[:, 0, :capacity].reshape(slot_total).astype(jnp.int32)
    slot_cols = got_meta[:, 1, :capacity].reshape(slot_total).astype(jnp.int32)
    slot_visit = got_meta[:, 2, :capacity].reshape(slot_total).astype(jnp.int32)
    slot_hot = (slot_visit[:, None] == jnp.arange(VISITS)[None, :]).astype(jnp.float32)
    slot_weight = jnp.sum(slot_hot * visit_weight[None, :], axis=1)
    body = got[:, : 2 * body_rows].reshape(slot_total, 2 * strip_rows, columns)
    coadd_image, weight_map = place(body, slot_rows, slot_cols, slot_weight, PH, PW)
    return (coadd_image[None], weight_map[None])


def solution(mesh):
    return jax.shard_map(
        shards,
        mesh=mesh,
        in_specs=(
            P(("band", "patch"), None, None),
            P(("band", "patch"), None, None),
            P(("band", "patch"), None, None),
            P(("band", "patch"), None, None),
            P(("band", "patch"), None),
            P(("band", "patch"), None),
            P(("band", "patch")),
            P(("band", "patch")),
        ),
        out_specs=(P(("band", "patch"), None, None), P(("band", "patch"), None, None)),
        check_vma=False,
    )
```

```python
import jax
import numpy as np
import jax.numpy as jnp
from jax import lax
from jax.experimental import pallas as pl
from jax.experimental.pallas import tpu as pltpu
from jax.sharding import PartitionSpec as P


PH = 128
PW = 512
KS = 21
VISITS = 8


gauss_widths = (0.75, 1.5, 3.0)
largest_value = lax.Precision.HIGHEST
mxu_value = lax.Precision.HIGH


def tap_table(kernel_half_width):
    support = np.arange(-kernel_half_width, kernel_half_width + 1).astype(np.float64)
    tables = []
    for spread in gauss_widths:
        s32 = float(np.float32(spread))
        gauss_total = np.sum(np.exp(-support * support / (2.0 * s32 * s32)))
        profile = np.exp(-support * support / (2.0 * s32 * s32)) / gauss_total
        scaled = support / s32
        tables.append(np.stack([profile, profile * scaled, profile * scaled * scaled]))
    return np.stack(tables)


def row_blocks(block_rows, window_rows, kernel_half_width):
    taps = tap_table(kernel_half_width).reshape(9, 2 * kernel_half_width + 1)
    out = np.zeros((9, block_rows, window_rows), np.float64)
    for i in range(block_rows):
        out[:, i, i : i + 2 * kernel_half_width + 1] = taps
    return out.astype(np.float32)


def column_ops(column_count, kernel_half_width):
    taps = tap_table(kernel_half_width)
    out = np.zeros((3, 3, column_count, column_count), np.float64)
    for y in range(column_count):
        lo = max(0, y - kernel_half_width)
        hi = min(column_count, y + kernel_half_width + 1)
        for x in range(lo, hi):
            out[:, :, y, x] = taps[:, :, y - x + kernel_half_width]
    return out.astype(np.float32)


def convolve_all(exposures, kernel_coeffs):
    kernel_half_width = KS // 2
    n, height, columns = exposures.shape
    block = 8
    blocks = height // block
    span = 2 * kernel_half_width + block
    reach = -(-span // block)
    total_rows = (blocks + reach - 1) * block
    padded = jnp.pad(
        exposures, ((0, 0), (kernel_half_width, total_rows - height - kernel_half_width), (0, 0))
    ).reshape(n, blocks + reach - 1, block, columns)
    windows = jnp.concatenate([padded[:, j : j + blocks] for j in range(reach)], axis=2)
    rows = jnp.asarray(row_blocks(block, reach * block, kernel_half_width))
    smooth = jnp.einsum("kit,nqtx->nqkix", rows, windows, precision=mxu_value)
    col_ops = jnp.asarray(column_ops(columns, kernel_half_width))
    x_line = 2.0 * jnp.arange(columns).astype(jnp.float32) / (columns - 1) - 1.0
    coef = kernel_coeffs.reshape(n, 3, 3, 3, 6)
    c = [coef[..., p, None] for p in range(6)]
    fx = jnp.stack(
        [
            c[0] + c[1] * x_line + c[3] * (x_line * x_line),
            c[2] + c[4] * x_line,
            jnp.broadcast_to(c[5], c[0].shape[:-1] + (columns,)),
        ],
        axis=4,
    )
    mixed = jnp.sum(
        col_ops[None, :, None, :, :, None, :] * fx[:, :, :, :, None, :, :], axis=3
    )
    mixed = mixed.reshape(n, 9, columns, 3 * columns)
    fields = jnp.einsum("nqkiy,nkyz->nqiz", smooth, mixed, precision=mxu_value)
    fields = fields.reshape(n, height, 3 * columns)
    y_line = (2.0 * jnp.arange(height).astype(jnp.float32) / (height - 1) - 1.0)[None, :, None]
    return (
        fields[:, :, :columns]
        + y_line * fields[:, :, columns : 2 * columns]
        + (y_line * y_line) * fields[:, :, 2 * columns :]
    )


def place_kernel(rows_ref, cols_ref, wts_ref, *refs):
    chunks = refs[:-4]
    coadd_ref, wmap_ref, acc_n, acc_w = refs[-4:]
    senders = len(chunks)
    capacity = rows_ref.shape[0] // senders
    strip_rows = 8
    lanes = chunks[0].shape[1]
    lane_blocks = acc_n.shape[0] - 1
    out_rows = coadd_ref.shape[0]
    acc_n[...] = jnp.zeros(acc_n.shape, jnp.float32)
    acc_w[...] = jnp.zeros(acc_w.shape, jnp.float32)
    lane = lax.broadcasted_iota(jnp.int32, (strip_rows, lanes), 1)
    sub = lax.broadcasted_iota(jnp.int32, (strip_rows, lanes), 0)

    for d, chunk in enumerate(chunks):

        def body(j, carry, chunk=chunk, d=d):
            s = d * capacity + j
            r = rows_ref[s]
            c = cols_ref[s]
            wt = wts_ref[s]
            q = c // lanes
            rem = c - q * lanes
            rq = r // strip_rows
            rr = r - rq * strip_rows
            lane_lo = lane >= rem
            sub_lo = sub >= rr
            top = pl.multiple_of(rq * strip_rows, strip_rows)
            nxt = pl.multiple_of(top + strip_rows, strip_rows)
            for part, acc in ((1, acc_n), (0, acc_w)):
                at = pl.multiple_of(j * (2 * strip_rows) + part * strip_rows, strip_rows)
                v = chunk[pl.ds(at, strip_rows), :] * wt
                v = pltpu.roll(v, rem, 1)
                v = pltpu.roll(v, rr, 0)
                zero = jnp.zeros_like(v)
                a = jnp.where(sub_lo, v, zero)
                b = v - a
                acc[q, pl.ds(top, strip_rows), :] += jnp.where(lane_lo, a, zero)
                acc[q + 1, pl.ds(top, strip_rows), :] += jnp.where(lane_lo, zero, a)
                acc[q, pl.ds(nxt, strip_rows), :] += jnp.where(lane_lo, b, zero)
                acc[q + 1, pl.ds(nxt, strip_rows), :] += jnp.where(lane_lo, zero, b)
            return carry

        lax.fori_loop(0, capacity, body, 0, unroll=min(4, capacity))
    for j in range(lane_blocks):
        n = acc_n[j, pl.ds(0, out_rows), :]
        w = acc_w[j, pl.ds(0, out_rows), :]
        wmap_ref[:, pl.ds(j * lanes, lanes)] = w
        coadd_ref[:, pl.ds(j * lanes, lanes)] = n / jnp.maximum(w, 1.0)


def place(chunks, rows, cols, wts, patch_rows, patch_cols):
    lanes = chunks[0].shape[1]
    strip_rows = 8
    lane_blocks = patch_cols // lanes
    smem = pltpu.SMEM
    return pl.pallas_call(
        place_kernel,
        out_shape=(
            jax.ShapeDtypeStruct((patch_rows, patch_cols), jnp.float32),
            jax.ShapeDtypeStruct((patch_rows, patch_cols), jnp.float32),
        ),
        in_specs=[pl.BlockSpec(memory_space=smem)] * 3
        + [pl.BlockSpec(memory_space=pltpu.VMEM)] * len(chunks),
        out_specs=(pl.BlockSpec(memory_space=pltpu.VMEM), pl.BlockSpec(memory_space=pltpu.VMEM)),
        scratch_shapes=[
            pltpu.VMEM((lane_blocks + 1, patch_rows + strip_rows, lanes), jnp.float32),
            pltpu.VMEM((lane_blocks + 1, patch_rows + strip_rows, lanes), jnp.float32),
        ],
    )(rows, cols, wts, *chunks)


def shards(
    exposures, variance, mask_bits, kernel_coeffs, ccd_visit, strip_patch, strip_row, strip_col
):
    ccd_count, height, columns = exposures.shape
    strip_total = strip_patch.shape[0]
    per_ccd = strip_total // ccd_count
    strip_rows = height // per_ccd
    devices = lax.axis_size("patch")
    capacity = 2 * strip_total // devices
    usable = (jnp.bitwise_and(mask_bits, 3) != 3).astype(jnp.float32)
    visit_hot = (ccd_visit == jnp.arange(VISITS)[None, :]).astype(jnp.float32)
    local_count = jnp.sum(jnp.sum(usable, axis=(1, 2))[:, None] * visit_hot, axis=0)
    local_load = jnp.sum(jnp.sum(usable * variance, axis=(1, 2))[:, None] * visit_hot, axis=0)

    destination = strip_patch[:, 0]
    strip_ids = jnp.arange(strip_total)
    earlier = strip_ids[None, :] < strip_ids[:, None]
    same_target = destination[None, :] == destination[:, None]
    slot_rank = jnp.sum(jnp.logical_and(earlier, same_target).astype(jnp.int32), axis=1)
    slot_index = destination * capacity + slot_rank
    slot_total = devices * capacity
    chooser = (slot_index[None, :] == jnp.arange(slot_total)[:, None]).astype(jnp.float32)

    strip_visit = jnp.repeat(ccd_visit[:, 0], per_ccd)
    placement = jnp.stack([strip_row, strip_col, strip_visit], axis=1).astype(jnp.float32)
    slot_meta = jnp.dot(chooser, placement, precision=largest_value).reshape(devices, capacity, 3)
    meta = jnp.zeros((devices, 8, columns), jnp.float32)
    meta = meta.at[:, 0:3, :capacity].set(jnp.swapaxes(slot_meta, 1, 2))
    meta = meta.at[:, 3, :VISITS].set(jnp.broadcast_to(local_count, (devices, VISITS)))
    meta = meta.at[:, 4, :VISITS].set(jnp.broadcast_to(local_load, (devices, VISITS)))
    body_rows = capacity * strip_rows
    convolved = convolve_all(exposures, kernel_coeffs)
    tiles = jnp.concatenate(
        [
            usable.reshape(strip_total, strip_rows * columns),
            (usable * convolved).reshape(strip_total, strip_rows * columns),
        ],
        axis=1,
    )
    packed = jnp.dot(chooser, tiles, precision=largest_value).reshape(
        devices, 2 * body_rows, columns
    )
    payload = jnp.concatenate([packed, meta], axis=1)
    me = lax.axis_index("patch")
    received = [lax.dynamic_index_in_dim(payload, me, 0, keepdims=False)]
    for shift in range(1, devices):
        chunk = lax.dynamic_index_in_dim(payload, (me + shift) % devices, 0, keepdims=False)
        pairs = [(i, (i + shift) % devices) for i in range(devices)]
        received.append(lax.ppermute(chunk, "patch", pairs))
    got_meta = jnp.stack([chunk[2 * body_rows :, :] for chunk in received], axis=0)
    visit_count = jnp.sum(got_meta[:, 3, :VISITS], axis=0)
    visit_load = jnp.sum(got_meta[:, 4, :VISITS], axis=0)
    visit_weight = (visit_count + 1.0) / (visit_load + 1.0)
    slot_rows = got_meta[:, 0, :capacity].reshape(slot_total).astype(jnp.int32)
    slot_cols = got_meta[:, 1, :capacity].reshape(slot_total).astype(jnp.int32)
    slot_visit = got_meta[:, 2, :capacity].reshape(slot_total).astype(jnp.int32)
    slot_hot = (slot_visit[:, None] == jnp.arange(VISITS)[None, :]).astype(jnp.float32)
    slot_weight = jnp.sum(slot_hot * visit_weight[None, :], axis=1)
    coadd_image, weight_map = place(received, slot_rows, slot_cols, slot_weight, PH, PW)
    return (coadd_image[None], weight_map[None])


def solution(mesh):
    return jax.shard_map(
        shards,
        mesh=mesh,
        in_specs=(
            P(("band", "patch"), None, None),
            P(("band", "patch"), None, None),
            P(("band", "patch"), None, None),
            P(("band", "patch"), None, None),
            P(("band", "patch"), None),
            P(("band", "patch"), None),
            P(("band", "patch")),
            P(("band", "patch")),
        ),
        out_specs=(P(("band", "patch"), None, None), P(("band", "patch"), None, None)),
        check_vma=False,
    )
```

```python
import jax
import numpy as np
import jax.numpy as jnp
from jax import lax
from jax.experimental import pallas as pl
from jax.experimental.pallas import tpu as pltpu
from jax.sharding import PartitionSpec as P


PH = 128
PW = 512
KS = 21
VISITS = 8


gauss_widths = (0.75, 1.5, 3.0)
largest_value = lax.Precision.HIGHEST
mxu_value = lax.Precision.HIGH


def tap_table(kernel_half_width):
    support = np.arange(-kernel_half_width, kernel_half_width + 1).astype(np.float64)
    tables = []
    for spread in gauss_widths:
        s32 = float(np.float32(spread))
        gauss_total = np.sum(np.exp(-support * support / (2.0 * s32 * s32)))
        profile = np.exp(-support * support / (2.0 * s32 * s32)) / gauss_total
        scaled = support / s32
        tables.append(np.stack([profile, profile * scaled, profile * scaled * scaled]))
    return np.stack(tables)


def row_blocks(block_rows, window_rows, kernel_half_width):
    taps = tap_table(kernel_half_width).reshape(9, 2 * kernel_half_width + 1)
    out = np.zeros((9, block_rows, window_rows), np.float64)
    for i in range(block_rows):
        out[:, i, i : i + 2 * kernel_half_width + 1] = taps
    return out.astype(np.float32)


def column_ops(column_count, kernel_half_width):
    taps = tap_table(kernel_half_width)
    out = np.zeros((3, 3, column_count, column_count), np.float64)
    for y in range(column_count):
        lo = max(0, y - kernel_half_width)
        hi = min(column_count, y + kernel_half_width + 1)
        for x in range(lo, hi):
            out[:, :, y, x] = taps[:, :, y - x + kernel_half_width]
    return out.astype(np.float32)


def convolve_all(exposures, kernel_coeffs):
    kernel_half_width = KS // 2
    n, height, columns = exposures.shape
    block = 8
    blocks = height // block
    span = 2 * kernel_half_width + block
    reach = -(-span // block)
    total_rows = (blocks + reach - 1) * block
    padded = jnp.pad(
        exposures, ((0, 0), (kernel_half_width, total_rows - height - kernel_half_width), (0, 0))
    ).reshape(n, blocks + reach - 1, block, columns)
    windows = jnp.concatenate([padded[:, j : j + blocks] for j in range(reach)], axis=2)
    rows = jnp.asarray(row_blocks(block, reach * block, kernel_half_width))
    smooth = jnp.einsum("kit,nqtx->nqkix", rows, windows, precision=mxu_value)
    x_line = 2.0 * jnp.arange(columns).astype(jnp.float32) / (columns - 1) - 1.0
    coef = kernel_coeffs.reshape(n, 3, 3, 3, 6)
    c = [coef[..., p, None] for p in range(6)]
    fx = jnp.stack(
        [
            c[0] + c[1] * x_line + c[3] * (x_line * x_line),
            c[2] + c[4] * x_line,
            jnp.broadcast_to(c[5], c[0].shape[:-1] + (columns,)),
        ],
        axis=4,
    )
    col_t = jnp.asarray(np.swapaxes(column_ops(columns, kernel_half_width), 2, 3))
    mixed = jnp.sum(
        col_t[None, :, None, :, None, :, :] * fx[:, :, :, :, :, :, None], axis=3
    )
    mixed = mixed.reshape(n, 9, 3 * columns, columns)
    fields = jnp.einsum("nqkiy,nkzy->nqiz", smooth, mixed, precision=mxu_value)
    fields = fields.reshape(n, height, 3 * columns)
    y_line = (2.0 * jnp.arange(height).astype(jnp.float32) / (height - 1) - 1.0)[None, :, None]
    return (
        fields[:, :, :columns]
        + y_line * fields[:, :, columns : 2 * columns]
        + (y_line * y_line) * fields[:, :, 2 * columns :]
    )


def place_kernel(rows_ref, cols_ref, wts_ref, *refs):
    chunks = refs[:-4]
    coadd_ref, wmap_ref, acc_n, acc_w = refs[-4:]
    senders = len(chunks)
    capacity = rows_ref.shape[0] // senders
    strip_rows = 8
    lanes = chunks[0].shape[1]
    lane_blocks = acc_n.shape[0] - 1
    out_rows = coadd_ref.shape[0]
    acc_n[...] = jnp.zeros(acc_n.shape, jnp.float32)
    acc_w[...] = jnp.zeros(acc_w.shape, jnp.float32)
    lane = lax.broadcasted_iota(jnp.int32, (strip_rows, lanes), 1)
    sub = lax.broadcasted_iota(jnp.int32, (strip_rows, lanes), 0)

    for d, chunk in enumerate(chunks):

        def body(j, carry, chunk=chunk, d=d):
            s = d * capacity + j
            r = rows_ref[s]
            c = cols_ref[s]
            wt = wts_ref[s]
            q = c // lanes
            rem = c - q * lanes
            rq = r // strip_rows
            rr = r - rq * strip_rows
            lane_lo = lane >= rem
            sub_lo = sub >= rr
            top = pl.multiple_of(rq * strip_rows, strip_rows)
            nxt = pl.multiple_of(top + strip_rows, strip_rows)
            for part, acc in ((1, acc_n), (0, acc_w)):
                at = pl.multiple_of(j * (2 * strip_rows) + part * strip_rows, strip_rows)
                v = chunk[pl.ds(at, strip_rows), :] * wt
                v = pltpu.roll(v, rem, 1)
                v = pltpu.roll(v, rr, 0)
                zero = jnp.zeros_like(v)
                a = jnp.where(sub_lo, v, zero)
                b = v - a
                acc[q, pl.ds(top, strip_rows), :] += jnp.where(lane_lo, a, zero)
                acc[q + 1, pl.ds(top, strip_rows), :] += jnp.where(lane_lo, zero, a)
                acc[q, pl.ds(nxt, strip_rows), :] += jnp.where(lane_lo, b, zero)
                acc[q + 1, pl.ds(nxt, strip_rows), :] += jnp.where(lane_lo, zero, b)
            return carry

        lax.fori_loop(0, capacity, body, 0, unroll=min(4, capacity))
    for j in range(lane_blocks):
        n = acc_n[j, pl.ds(0, out_rows), :]
        w = acc_w[j, pl.ds(0, out_rows), :]
        wmap_ref[:, pl.ds(j * lanes, lanes)] = w
        coadd_ref[:, pl.ds(j * lanes, lanes)] = n / jnp.maximum(w, 1.0)


def place(chunks, rows, cols, wts, patch_rows, patch_cols):
    lanes = chunks[0].shape[1]
    strip_rows = 8
    lane_blocks = patch_cols // lanes
    smem = pltpu.SMEM
    return pl.pallas_call(
        place_kernel,
        out_shape=(
            jax.ShapeDtypeStruct((patch_rows, patch_cols), jnp.float32),
            jax.ShapeDtypeStruct((patch_rows, patch_cols), jnp.float32),
        ),
        in_specs=[pl.BlockSpec(memory_space=smem)] * 3
        + [pl.BlockSpec(memory_space=pltpu.VMEM)] * len(chunks),
        out_specs=(pl.BlockSpec(memory_space=pltpu.VMEM), pl.BlockSpec(memory_space=pltpu.VMEM)),
        scratch_shapes=[
            pltpu.VMEM((lane_blocks + 1, patch_rows + strip_rows, lanes), jnp.float32),
            pltpu.VMEM((lane_blocks + 1, patch_rows + strip_rows, lanes), jnp.float32),
        ],
    )(rows, cols, wts, *chunks)


def shards(
    exposures, variance, mask_bits, kernel_coeffs, ccd_visit, strip_patch, strip_row, strip_col
):
    ccd_count, height, columns = exposures.shape
    strip_total = strip_patch.shape[0]
    per_ccd = strip_total // ccd_count
    strip_rows = height // per_ccd
    devices = lax.axis_size("patch")
    capacity = 2 * strip_total // devices
    usable = (jnp.bitwise_and(mask_bits, 3) != 3).astype(jnp.float32)
    visit_hot = (ccd_visit == jnp.arange(VISITS)[None, :]).astype(jnp.float32)
    local_count = jnp.sum(jnp.sum(usable, axis=(1, 2))[:, None] * visit_hot, axis=0)
    local_load = jnp.sum(jnp.sum(usable * variance, axis=(1, 2))[:, None] * visit_hot, axis=0)

    destination = strip_patch[:, 0]
    strip_ids = jnp.arange(strip_total)
    earlier = strip_ids[None, :] < strip_ids[:, None]
    same_target = destination[None, :] == destination[:, None]
    slot_rank = jnp.sum(jnp.logical_and(earlier, same_target).astype(jnp.int32), axis=1)
    slot_index = destination * capacity + slot_rank
    slot_total = devices * capacity
    chooser = (slot_index[None, :] == jnp.arange(slot_total)[:, None]).astype(jnp.float32)

    strip_visit = jnp.repeat(ccd_visit[:, 0], per_ccd)
    placement = jnp.stack([strip_row, strip_col, strip_visit], axis=1).astype(jnp.float32)
    slot_meta = jnp.dot(chooser, placement, precision=largest_value).reshape(devices, capacity, 3)
    meta = jnp.zeros((devices, 8, columns), jnp.float32)
    meta = meta.at[:, 0:3, :capacity].set(jnp.swapaxes(slot_meta, 1, 2))
    meta = meta.at[:, 3, :VISITS].set(jnp.broadcast_to(local_count, (devices, VISITS)))
    meta = meta.at[:, 4, :VISITS].set(jnp.broadcast_to(local_load, (devices, VISITS)))
    body_rows = capacity * strip_rows
    convolved = convolve_all(exposures, kernel_coeffs)
    tiles = jnp.concatenate(
        [
            usable.reshape(strip_total, strip_rows * columns),
            (usable * convolved).reshape(strip_total, strip_rows * columns),
        ],
        axis=1,
    )
    packed = jnp.dot(chooser, tiles, precision=largest_value).reshape(
        devices, 2 * body_rows, columns
    )
    payload = jnp.concatenate([packed, meta], axis=1)
    me = lax.axis_index("patch")
    received = [lax.dynamic_index_in_dim(payload, me, 0, keepdims=False)]
    for shift in range(1, devices):
        chunk = lax.dynamic_index_in_dim(payload, (me + shift) % devices, 0, keepdims=False)
        pairs = [(i, (i + shift) % devices) for i in range(devices)]
        received.append(lax.ppermute(chunk, "patch", pairs))
    got_meta = jnp.stack([chunk[2 * body_rows :, :] for chunk in received], axis=0)
    visit_count = jnp.sum(got_meta[:, 3, :VISITS], axis=0)
    visit_load = jnp.sum(got_meta[:, 4, :VISITS], axis=0)
    visit_weight = (visit_count + 1.0) / (visit_load + 1.0)
    slot_rows = got_meta[:, 0, :capacity].reshape(slot_total).astype(jnp.int32)
    slot_cols = got_meta[:, 1, :capacity].reshape(slot_total).astype(jnp.int32)
    slot_visit = got_meta[:, 2, :capacity].reshape(slot_total).astype(jnp.int32)
    slot_hot = (slot_visit[:, None] == jnp.arange(VISITS)[None, :]).astype(jnp.float32)
    slot_weight = jnp.sum(slot_hot * visit_weight[None, :], axis=1)
    coadd_image, weight_map = place(received, slot_rows, slot_cols, slot_weight, PH, PW)
    return (coadd_image[None], weight_map[None])


def solution(mesh):
    return jax.shard_map(
        shards,
        mesh=mesh,
        in_specs=(
            P(("band", "patch"), None, None),
            P(("band", "patch"), None, None),
            P(("band", "patch"), None, None),
            P(("band", "patch"), None, None),
            P(("band", "patch"), None),
            P(("band", "patch"), None),
            P(("band", "patch")),
            P(("band", "patch")),
        ),
        out_specs=(P(("band", "patch"), None, None), P(("band", "patch"), None, None)),
        check_vma=False,
    )
```

```python
import jax
import numpy as np
import jax.numpy as jnp
from jax import lax
from jax.experimental import pallas as pl
from jax.experimental.pallas import tpu as pltpu
from jax.sharding import PartitionSpec as P


PH = 128
PW = 512
KS = 21
VISITS = 8


gauss_widths = (0.75, 1.5, 3.0)
largest_value = lax.Precision.HIGHEST
mxu_value = lax.Precision.HIGH


def tap_table(kernel_half_width):
    support = np.arange(-kernel_half_width, kernel_half_width + 1).astype(np.float64)
    tables = []
    for spread in gauss_widths:
        s32 = float(np.float32(spread))
        gauss_total = np.sum(np.exp(-support * support / (2.0 * s32 * s32)))
        profile = np.exp(-support * support / (2.0 * s32 * s32)) / gauss_total
        scaled = support / s32
        tables.append(np.stack([profile, profile * scaled, profile * scaled * scaled]))
    return np.stack(tables)


def row_blocks(block_rows, window_rows, kernel_half_width):
    taps = tap_table(kernel_half_width).reshape(9, 2 * kernel_half_width + 1)
    out = np.zeros((9, block_rows, window_rows), np.float64)
    for i in range(block_rows):
        out[:, i, i : i + 2 * kernel_half_width + 1] = taps
    return out.astype(np.float32)


def column_ops(column_count, kernel_half_width):
    taps = tap_table(kernel_half_width)
    out = np.zeros((3, 3, column_count, column_count), np.float64)
    for y in range(column_count):
        lo = max(0, y - kernel_half_width)
        hi = min(column_count, y + kernel_half_width + 1)
        for x in range(lo, hi):
            out[:, :, y, x] = taps[:, :, y - x + kernel_half_width]
    return out.astype(np.float32)


def convolve_all(exposures, kernel_coeffs):
    kernel_half_width = KS // 2
    n, height, columns = exposures.shape
    block = 8
    blocks = height // block
    span = 2 * kernel_half_width + block
    reach = -(-span // block)
    total_rows = (blocks + reach - 1) * block
    padded = jnp.pad(
        exposures, ((0, 0), (kernel_half_width, total_rows - height - kernel_half_width), (0, 0))
    ).reshape(n, blocks + reach - 1, block, columns)
    windows = jnp.concatenate([padded[:, j : j + blocks] for j in range(reach)], axis=2)
    rows = jnp.asarray(row_blocks(block, reach * block, kernel_half_width))
    smooth = jnp.einsum("kit,nqtx->nqkix", rows, windows, precision=mxu_value)
    x_np = 2.0 * np.arange(columns, dtype=np.float32) / np.float32(columns - 1) - 1.0
    basis = np.zeros((6, 3, columns), np.float32)
    basis[0, 0] = 1.0
    basis[1, 0] = x_np
    basis[3, 0] = x_np * x_np
    basis[2, 1] = 1.0
    basis[4, 1] = x_np
    basis[5, 2] = 1.0
    fx = jnp.dot(
        kernel_coeffs.reshape(n * 27, 6), jnp.asarray(basis.reshape(6, 3 * columns)),
        precision=largest_value,
    ).reshape(n, 3, 3, 3, 3, columns)
    col_t = jnp.asarray(np.swapaxes(column_ops(columns, kernel_half_width), 2, 3))
    mixed = jnp.sum(
        col_t[None, :, None, :, None, :, :] * fx[:, :, :, :, :, :, None], axis=3
    )
    mixed = mixed.reshape(n, 9, 3 * columns, columns)
    fields = jnp.einsum("nqkiy,nkzy->nqiz", smooth, mixed, precision=mxu_value)
    fields = fields.reshape(n, height, 3 * columns)
    y_line = (2.0 * jnp.arange(height).astype(jnp.float32) / (height - 1) - 1.0)[None, :, None]
    return (
        fields[:, :, :columns]
        + y_line * fields[:, :, columns : 2 * columns]
        + (y_line * y_line) * fields[:, :, 2 * columns :]
    )


def place_kernel(meta_ref, visit_weight_ref, *refs):
    chunks = refs[:-4]
    coadd_ref, wmap_ref, acc_n, acc_w = refs[-4:]
    senders = len(chunks)
    slots = meta_ref.shape[0] // 3
    capacity = slots // senders
    strip_rows = 8
    lanes = chunks[0].shape[1]
    lane_blocks = acc_n.shape[0] - 1
    out_rows = coadd_ref.shape[0]
    acc_n[...] = jnp.zeros(acc_n.shape, jnp.float32)
    acc_w[...] = jnp.zeros(acc_w.shape, jnp.float32)
    lane = lax.broadcasted_iota(jnp.int32, (strip_rows, lanes), 1)
    sub = lax.broadcasted_iota(jnp.int32, (strip_rows, lanes), 0)

    for d, chunk in enumerate(chunks):

        def body(j, carry, chunk=chunk, d=d):
            s = d * capacity + j
            r = meta_ref[s].astype(jnp.int32)
            c = meta_ref[slots + s].astype(jnp.int32)
            wt = visit_weight_ref[meta_ref[2 * slots + s].astype(jnp.int32)]
            q = c // lanes
            rem = c - q * lanes
            rq = r // strip_rows
            rr = r - rq * strip_rows
            lane_lo = lane >= rem
            sub_lo = sub >= rr
            top = pl.multiple_of(rq * strip_rows, strip_rows)
            nxt = pl.multiple_of(top + strip_rows, strip_rows)
            for part, acc in ((1, acc_n), (0, acc_w)):
                at = pl.multiple_of(j * (2 * strip_rows) + part * strip_rows, strip_rows)
                v = chunk[pl.ds(at, strip_rows), :] * wt
                v = pltpu.roll(v, rem, 1)
                v = pltpu.roll(v, rr, 0)
                zero = jnp.zeros_like(v)
                a = jnp.where(sub_lo, v, zero)
                b = v - a
                acc[q, pl.ds(top, strip_rows), :] += jnp.where(lane_lo, a, zero)
                acc[q + 1, pl.ds(top, strip_rows), :] += jnp.where(lane_lo, zero, a)
                acc[q, pl.ds(nxt, strip_rows), :] += jnp.where(lane_lo, b, zero)
                acc[q + 1, pl.ds(nxt, strip_rows), :] += jnp.where(lane_lo, zero, b)
            return carry

        lax.fori_loop(0, capacity, body, 0, unroll=min(4, capacity))
    for j in range(lane_blocks):
        n = acc_n[j, pl.ds(0, out_rows), :]
        w = acc_w[j, pl.ds(0, out_rows), :]
        wmap_ref[:, pl.ds(j * lanes, lanes)] = w
        coadd_ref[:, pl.ds(j * lanes, lanes)] = n / jnp.maximum(w, 1.0)


def place(chunks, meta, visit_weight, patch_rows, patch_cols):
    lanes = chunks[0].shape[1]
    strip_rows = 8
    lane_blocks = patch_cols // lanes
    smem = pltpu.SMEM
    return pl.pallas_call(
        place_kernel,
        out_shape=(
            jax.ShapeDtypeStruct((patch_rows, patch_cols), jnp.float32),
            jax.ShapeDtypeStruct((patch_rows, patch_cols), jnp.float32),
        ),
        in_specs=[pl.BlockSpec(memory_space=smem)] * 2
        + [pl.BlockSpec(memory_space=pltpu.VMEM)] * len(chunks),
        out_specs=(pl.BlockSpec(memory_space=pltpu.VMEM), pl.BlockSpec(memory_space=pltpu.VMEM)),
        scratch_shapes=[
            pltpu.VMEM((lane_blocks + 1, patch_rows + strip_rows, lanes), jnp.float32),
            pltpu.VMEM((lane_blocks + 1, patch_rows + strip_rows, lanes), jnp.float32),
        ],
    )(meta, visit_weight, *chunks)


def shards(
    exposures, variance, mask_bits, kernel_coeffs, ccd_visit, strip_patch, strip_row, strip_col
):
    ccd_count, height, columns = exposures.shape
    strip_total = strip_patch.shape[0]
    per_ccd = strip_total // ccd_count
    strip_rows = height // per_ccd
    devices = lax.axis_size("patch")
    capacity = 2 * strip_total // devices
    usable = (jnp.bitwise_and(mask_bits, 3) != 3).astype(jnp.float32)
    visit_hot = (ccd_visit == jnp.arange(VISITS)[None, :]).astype(jnp.float32)
    local_count = jnp.sum(jnp.sum(usable, axis=(1, 2))[:, None] * visit_hot, axis=0)
    local_load = jnp.sum(jnp.sum(usable * variance, axis=(1, 2))[:, None] * visit_hot, axis=0)

    destination = strip_patch[:, 0]
    strip_ids = jnp.arange(strip_total)
    earlier = strip_ids[None, :] < strip_ids[:, None]
    same_target = destination[None, :] == destination[:, None]
    slot_rank = jnp.sum(jnp.logical_and(earlier, same_target).astype(jnp.int32), axis=1)
    slot_index = destination * capacity + slot_rank
    slot_total = devices * capacity
    chooser = (slot_index[None, :] == jnp.arange(slot_total)[:, None]).astype(jnp.float32)

    strip_visit = jnp.repeat(ccd_visit[:, 0], per_ccd)
    placement = jnp.stack([strip_row, strip_col, strip_visit], axis=1).astype(jnp.float32)
    slot_meta = jnp.dot(chooser, placement, precision=largest_value).reshape(devices, capacity, 3)
    meta = jnp.concatenate(
        [
            jnp.pad(jnp.swapaxes(slot_meta, 1, 2), ((0, 0), (0, 0), (0, columns - capacity))),
            jnp.broadcast_to(
                jnp.pad(
                    jnp.stack([local_count, local_load])[None],
                    ((0, 0), (0, 3), (0, columns - VISITS)),
                ),
                (devices, 5, columns),
            ),
        ],
        axis=1,
    )
    body_rows = capacity * strip_rows
    convolved = convolve_all(exposures, kernel_coeffs)
    tiles = jnp.concatenate(
        [
            usable.reshape(strip_total, strip_rows * columns),
            (usable * convolved).reshape(strip_total, strip_rows * columns),
        ],
        axis=1,
    )
    packed = jnp.dot(chooser, tiles, precision=largest_value).reshape(
        devices, 2 * body_rows, columns
    )
    payload = jnp.concatenate([packed, meta], axis=1)
    me = lax.axis_index("patch")
    received = [lax.dynamic_index_in_dim(payload, me, 0, keepdims=False)]
    for shift in range(1, devices):
        chunk = lax.dynamic_index_in_dim(payload, (me + shift) % devices, 0, keepdims=False)
        pairs = [(i, (i + shift) % devices) for i in range(devices)]
        received.append(lax.ppermute(chunk, "patch", pairs))
    got_meta = jnp.stack([chunk[2 * body_rows :, :] for chunk in received], axis=0)
    visit_count = jnp.sum(got_meta[:, 3, :VISITS], axis=0)
    visit_load = jnp.sum(got_meta[:, 4, :VISITS], axis=0)
    visit_weight = (visit_count + 1.0) / (visit_load + 1.0)
    slot_meta_all = jnp.swapaxes(got_meta[:, 0:3, :capacity], 0, 1).reshape(3 * slot_total)
    coadd_image, weight_map = place(received, slot_meta_all, visit_weight, PH, PW)
    return (coadd_image[None], weight_map[None])


def solution(mesh):
    return jax.shard_map(
        shards,
        mesh=mesh,
        in_specs=(
            P(("band", "patch"), None, None),
            P(("band", "patch"), None, None),
            P(("band", "patch"), None, None),
            P(("band", "patch"), None, None),
            P(("band", "patch"), None),
            P(("band", "patch"), None),
            P(("band", "patch")),
            P(("band", "patch")),
        ),
        out_specs=(P(("band", "patch"), None, None), P(("band", "patch"), None, None)),
        check_vma=False,
    )
```

```python
import jax
import numpy as np
import jax.numpy as jnp
from jax import lax
from jax.experimental import pallas as pl
from jax.experimental.pallas import tpu as pltpu
from jax.sharding import PartitionSpec as P


PH = 128
PW = 512
KS = 21
VISITS = 8


gauss_widths = (0.75, 1.5, 3.0)
largest_value = lax.Precision.HIGHEST
mxu_value = lax.Precision.HIGH


def tap_table(kernel_half_width):
    support = np.arange(-kernel_half_width, kernel_half_width + 1).astype(np.float64)
    tables = []
    for spread in gauss_widths:
        s32 = float(np.float32(spread))
        gauss_total = np.sum(np.exp(-support * support / (2.0 * s32 * s32)))
        profile = np.exp(-support * support / (2.0 * s32 * s32)) / gauss_total
        scaled = support / s32
        tables.append(np.stack([profile, profile * scaled, profile * scaled * scaled]))
    return np.stack(tables)


def row_blocks(block_rows, window_rows, kernel_half_width):
    taps = tap_table(kernel_half_width).reshape(9, 2 * kernel_half_width + 1)
    out = np.zeros((9, block_rows, window_rows), np.float64)
    for i in range(block_rows):
        out[:, i, i : i + 2 * kernel_half_width + 1] = taps
    return out.astype(np.float32)


def column_ops(column_count, kernel_half_width):
    taps = tap_table(kernel_half_width)
    out = np.zeros((3, 3, column_count, column_count), np.float64)
    for y in range(column_count):
        lo = max(0, y - kernel_half_width)
        hi = min(column_count, y + kernel_half_width + 1)
        for x in range(lo, hi):
            out[:, :, y, x] = taps[:, :, y - x + kernel_half_width]
    return out.astype(np.float32)


def convolve_all(exposures, kernel_coeffs):
    kernel_half_width = KS // 2
    n, height, columns = exposures.shape
    block = 8
    blocks = height // block
    span = 2 * kernel_half_width + block
    reach = -(-span // block)
    total_rows = (blocks + reach - 1) * block
    padded = jnp.pad(
        exposures, ((0, 0), (kernel_half_width, total_rows - height - kernel_half_width), (0, 0))
    ).reshape(n, blocks + reach - 1, block, columns)
    windows = jnp.concatenate([padded[:, j : j + blocks] for j in range(reach)], axis=2)
    rows = jnp.asarray(row_blocks(block, reach * block, kernel_half_width))
    smooth = jnp.einsum("kit,nqtx->nqkix", rows, windows, precision=mxu_value)
    x_np = 2.0 * np.arange(columns, dtype=np.float32) / np.float32(columns - 1) - 1.0
    basis = np.zeros((6, 3, columns), np.float32)
    basis[0, 0] = 1.0
    basis[1, 0] = x_np
    basis[3, 0] = x_np * x_np
    basis[2, 1] = 1.0
    basis[4, 1] = x_np
    basis[5, 2] = 1.0
    fx = jnp.dot(
        kernel_coeffs.reshape(n * 27, 6), jnp.asarray(basis.reshape(6, 3 * columns)),
        precision=largest_value,
    ).reshape(n, 3, 3, 3, 3, columns)
    col_t = jnp.asarray(np.swapaxes(column_ops(columns, kernel_half_width), 2, 3))
    mixed = (
        col_t[None, :, None, 0, None, :, :] * fx[:, :, :, 0, :, :, None]
        + col_t[None, :, None, 1, None, :, :] * fx[:, :, :, 1, :, :, None]
        + col_t[None, :, None, 2, None, :, :] * fx[:, :, :, 2, :, :, None]
    )
    mixed = mixed.reshape(n, 9, 3 * columns, columns)
    fields = jnp.einsum("nqkiy,nkzy->nqiz", smooth, mixed, precision=mxu_value)
    fields = fields.reshape(n, height, 3 * columns)
    y_line = (2.0 * jnp.arange(height).astype(jnp.float32) / (height - 1) - 1.0)[None, :, None]
    return (
        fields[:, :, :columns]
        + y_line * fields[:, :, columns : 2 * columns]
        + (y_line * y_line) * fields[:, :, 2 * columns :]
    )


def place_kernel(meta_ref, visit_weight_ref, *refs):
    chunks = refs[:-4]
    coadd_ref, wmap_ref, acc_n, acc_w = refs[-4:]
    senders = len(chunks)
    slots = meta_ref.shape[0] // 3
    capacity = slots // senders
    strip_rows = 8
    lanes = chunks[0].shape[1]
    lane_blocks = acc_n.shape[0] - 1
    out_rows = coadd_ref.shape[0]
    acc_n[...] = jnp.zeros(acc_n.shape, jnp.float32)
    acc_w[...] = jnp.zeros(acc_w.shape, jnp.float32)
    lane = lax.broadcasted_iota(jnp.int32, (strip_rows, lanes), 1)
    sub = lax.broadcasted_iota(jnp.int32, (strip_rows, lanes), 0)

    for d, chunk in enumerate(chunks):

        def body(j, carry, chunk=chunk, d=d):
            s = d * capacity + j
            r = meta_ref[s].astype(jnp.int32)
            c = meta_ref[slots + s].astype(jnp.int32)
            wt = visit_weight_ref[meta_ref[2 * slots + s].astype(jnp.int32)]
            q = c // lanes
            rem = c - q * lanes
            rq = r // strip_rows
            rr = r - rq * strip_rows
            lane_lo = lane >= rem
            sub_lo = sub >= rr
            top = pl.multiple_of(rq * strip_rows, strip_rows)
            nxt = pl.multiple_of(top + strip_rows, strip_rows)
            for part, acc in ((1, acc_n), (0, acc_w)):
                at = pl.multiple_of(j * (2 * strip_rows) + part * strip_rows, strip_rows)
                v = chunk[pl.ds(at, strip_rows), :] * wt
                v = pltpu.roll(v, rem, 1)
                v = pltpu.roll(v, rr, 0)
                zero = jnp.zeros_like(v)
                a = jnp.where(sub_lo, v, zero)
                b = v - a
                acc[q, pl.ds(top, strip_rows), :] += jnp.where(lane_lo, a, zero)
                acc[q + 1, pl.ds(top, strip_rows), :] += jnp.where(lane_lo, zero, a)
                acc[q, pl.ds(nxt, strip_rows), :] += jnp.where(lane_lo, b, zero)
                acc[q + 1, pl.ds(nxt, strip_rows), :] += jnp.where(lane_lo, zero, b)
            return carry

        lax.fori_loop(0, capacity, body, 0, unroll=min(8, capacity))
    for j in range(lane_blocks):
        n = acc_n[j, pl.ds(0, out_rows), :]
        w = acc_w[j, pl.ds(0, out_rows), :]
        wmap_ref[:, pl.ds(j * lanes, lanes)] = w
        coadd_ref[:, pl.ds(j * lanes, lanes)] = n / jnp.maximum(w, 1.0)


def place(chunks, meta, visit_weight, patch_rows, patch_cols):
    lanes = chunks[0].shape[1]
    strip_rows = 8
    lane_blocks = patch_cols // lanes
    smem = pltpu.SMEM
    return pl.pallas_call(
        place_kernel,
        out_shape=(
            jax.ShapeDtypeStruct((patch_rows, patch_cols), jnp.float32),
            jax.ShapeDtypeStruct((patch_rows, patch_cols), jnp.float32),
        ),
        in_specs=[pl.BlockSpec(memory_space=smem)] * 2
        + [pl.BlockSpec(memory_space=pltpu.VMEM)] * len(chunks),
        out_specs=(pl.BlockSpec(memory_space=pltpu.VMEM), pl.BlockSpec(memory_space=pltpu.VMEM)),
        scratch_shapes=[
            pltpu.VMEM((lane_blocks + 1, patch_rows + strip_rows, lanes), jnp.float32),
            pltpu.VMEM((lane_blocks + 1, patch_rows + strip_rows, lanes), jnp.float32),
        ],
    )(meta, visit_weight, *chunks)


def shards(
    exposures, variance, mask_bits, kernel_coeffs, ccd_visit, strip_patch, strip_row, strip_col
):
    ccd_count, height, columns = exposures.shape
    strip_total = strip_patch.shape[0]
    per_ccd = strip_total // ccd_count
    strip_rows = height // per_ccd
    devices = lax.axis_size("patch")
    capacity = 2 * strip_total // devices
    usable = (jnp.bitwise_and(mask_bits, 3) != 3).astype(jnp.float32)
    visit_hot = (ccd_visit == jnp.arange(VISITS)[None, :]).astype(jnp.float32)
    local_count = jnp.sum(jnp.sum(usable, axis=(1, 2))[:, None] * visit_hot, axis=0)
    local_load = jnp.sum(jnp.sum(usable * variance, axis=(1, 2))[:, None] * visit_hot, axis=0)

    destination = strip_patch[:, 0]
    strip_ids = jnp.arange(strip_total)
    earlier = strip_ids[None, :] < strip_ids[:, None]
    same_target = destination[None, :] == destination[:, None]
    slot_rank = jnp.sum(jnp.logical_and(earlier, same_target).astype(jnp.int32), axis=1)
    slot_index = destination * capacity + slot_rank
    slot_total = devices * capacity
    chooser = (slot_index[None, :] == jnp.arange(slot_total)[:, None]).astype(jnp.float32)

    strip_visit = jnp.repeat(ccd_visit[:, 0], per_ccd)
    placement = jnp.stack([strip_row, strip_col, strip_visit], axis=1).astype(jnp.float32)
    slot_meta = jnp.dot(chooser, placement, precision=largest_value).reshape(devices, capacity, 3)
    meta = jnp.concatenate(
        [
            jnp.pad(jnp.swapaxes(slot_meta, 1, 2), ((0, 0), (0, 0), (0, columns - capacity))),
            jnp.broadcast_to(
                jnp.pad(
                    jnp.stack([local_count, local_load])[None],
                    ((0, 0), (0, 3), (0, columns - VISITS)),
                ),
                (devices, 5, columns),
            ),
        ],
        axis=1,
    )
    body_rows = capacity * strip_rows
    convolved = convolve_all(exposures, kernel_coeffs)
    tiles = jnp.concatenate(
        [
            usable.reshape(strip_total, strip_rows * columns),
            (usable * convolved).reshape(strip_total, strip_rows * columns),
        ],
        axis=1,
    )
    packed = jnp.dot(chooser, tiles, precision=largest_value).reshape(
        devices, 2 * body_rows, columns
    )
    payload = jnp.concatenate([packed, meta], axis=1)
    me = lax.axis_index("patch")
    received = [lax.dynamic_index_in_dim(payload, me, 0, keepdims=False)]
    for shift in range(1, devices):
        chunk = lax.dynamic_index_in_dim(payload, (me + shift) % devices, 0, keepdims=False)
        pairs = [(i, (i + shift) % devices) for i in range(devices)]
        received.append(lax.ppermute(chunk, "patch", pairs))
    got_meta = jnp.stack([chunk[2 * body_rows :, :] for chunk in received], axis=0)
    visit_count = jnp.sum(got_meta[:, 3, :VISITS], axis=0)
    visit_load = jnp.sum(got_meta[:, 4, :VISITS], axis=0)
    visit_weight = (visit_count + 1.0) / (visit_load + 1.0)
    slot_meta_all = jnp.swapaxes(got_meta[:, 0:3, :capacity], 0, 1).reshape(3 * slot_total)
    coadd_image, weight_map = place(received, slot_meta_all, visit_weight, PH, PW)
    return (coadd_image[None], weight_map[None])


def solution(mesh):
    return jax.shard_map(
        shards,
        mesh=mesh,
        in_specs=(
            P(("band", "patch"), None, None),
            P(("band", "patch"), None, None),
            P(("band", "patch"), None, None),
            P(("band", "patch"), None, None),
            P(("band", "patch"), None),
            P(("band", "patch"), None),
            P(("band", "patch")),
            P(("band", "patch")),
        ),
        out_specs=(P(("band", "patch"), None, None), P(("band", "patch"), None, None)),
        check_vma=False,
    )
```

```python
import jax
import numpy as np
import jax.numpy as jnp
from jax import lax
from jax.experimental import pallas as pl
from jax.experimental.pallas import tpu as pltpu
from jax.sharding import PartitionSpec as P


PH = 128
PW = 512
KS = 21
VISITS = 8


gauss_widths = (0.75, 1.5, 3.0)
largest_value = lax.Precision.HIGHEST
mxu_value = lax.Precision.HIGH


def tap_table(kernel_half_width):
    support = np.arange(-kernel_half_width, kernel_half_width + 1).astype(np.float64)
    tables = []
    for spread in gauss_widths:
        s32 = float(np.float32(spread))
        gauss_total = np.sum(np.exp(-support * support / (2.0 * s32 * s32)))
        profile = np.exp(-support * support / (2.0 * s32 * s32)) / gauss_total
        scaled = support / s32
        tables.append(np.stack([profile, profile * scaled, profile * scaled * scaled]))
    return np.stack(tables)


def row_blocks(block_rows, window_rows, kernel_half_width, lead):
    taps = tap_table(kernel_half_width).reshape(9, 2 * kernel_half_width + 1)
    out = np.zeros((9, block_rows, window_rows), np.float64)
    for i in range(block_rows):
        start = lead + i - kernel_half_width
        out[:, i, start : start + 2 * kernel_half_width + 1] = taps
    return out.astype(np.float32)


def column_ops(column_count, kernel_half_width):
    taps = tap_table(kernel_half_width)
    out = np.zeros((3, 3, column_count, column_count), np.float64)
    for y in range(column_count):
        lo = max(0, y - kernel_half_width)
        hi = min(column_count, y + kernel_half_width + 1)
        for x in range(lo, hi):
            out[:, :, y, x] = taps[:, :, y - x + kernel_half_width]
    return out.astype(np.float32)


def convolve_all(exposures, kernel_coeffs):
    kernel_half_width = KS // 2
    n, height, columns = exposures.shape
    block = 8
    blocks = height // block
    lead = -(-kernel_half_width // block) * block
    reach = -(-(lead + kernel_half_width + block) // block)
    total_rows = (blocks + reach - 1) * block
    padded = jnp.pad(
        exposures, ((0, 0), (lead, total_rows - height - lead), (0, 0))
    ).reshape(n, blocks + reach - 1, block, columns)
    windows = jnp.concatenate([padded[:, j : j + blocks] for j in range(reach)], axis=2)
    rows = jnp.asarray(row_blocks(block, reach * block, kernel_half_width, lead))
    smooth = jnp.einsum("kit,nqtx->nqkix", rows, windows, precision=mxu_value)
    x_np = 2.0 * np.arange(columns, dtype=np.float32) / np.float32(columns - 1) - 1.0
    basis = np.zeros((6, 3, columns), np.float32)
    basis[0, 0] = 1.0
    basis[1, 0] = x_np
    basis[3, 0] = x_np * x_np
    basis[2, 1] = 1.0
    basis[4, 1] = x_np
    basis[5, 2] = 1.0
    fx = jnp.dot(
        kernel_coeffs.reshape(n * 27, 6), jnp.asarray(basis.reshape(6, 3 * columns)),
        precision=largest_value,
    ).reshape(n, 3, 3, 3, 3, columns)
    col_t = jnp.asarray(np.swapaxes(column_ops(columns, kernel_half_width), 2, 3))
    mixed = (
        col_t[None, :, None, 0, None, :, :] * fx[:, :, :, 0, :, :, None]
        + col_t[None, :, None, 1, None, :, :] * fx[:, :, :, 1, :, :, None]
        + col_t[None, :, None, 2, None, :, :] * fx[:, :, :, 2, :, :, None]
    )
    mixed = mixed.reshape(n, 9, 3 * columns, columns)
    fields = jnp.einsum("nqkiy,nkzy->nqiz", smooth, mixed, precision=mxu_value)
    fields = fields.reshape(n, height, 3 * columns)
    y_line = (2.0 * jnp.arange(height).astype(jnp.float32) / (height - 1) - 1.0)[None, :, None]
    return (
        fields[:, :, :columns]
        + y_line * fields[:, :, columns : 2 * columns]
        + (y_line * y_line) * fields[:, :, 2 * columns :]
    )


def place_kernel(meta_ref, visit_weight_ref, *refs):
    chunks = refs[:-4]
    coadd_ref, wmap_ref, acc_n, acc_w = refs[-4:]
    senders = len(chunks)
    slots = meta_ref.shape[0] // 3
    capacity = slots // senders
    strip_rows = 8
    lanes = chunks[0].shape[1]
    lane_blocks = acc_n.shape[0] - 1
    out_rows = coadd_ref.shape[0]
    acc_n[...] = jnp.zeros(acc_n.shape, jnp.float32)
    acc_w[...] = jnp.zeros(acc_w.shape, jnp.float32)
    lane = lax.broadcasted_iota(jnp.int32, (strip_rows, lanes), 1)
    sub = lax.broadcasted_iota(jnp.int32, (strip_rows, lanes), 0)

    for d, chunk in enumerate(chunks):

        def body(j, carry, chunk=chunk, d=d):
            s = d * capacity + j
            r = meta_ref[s].astype(jnp.int32)
            c = meta_ref[slots + s].astype(jnp.int32)
            wt = visit_weight_ref[meta_ref[2 * slots + s].astype(jnp.int32)]
            q = c // lanes
            rem = c - q * lanes
            rq = r // strip_rows
            rr = r - rq * strip_rows
            lane_lo = lane >= rem
            sub_lo = sub >= rr
            top = pl.multiple_of(rq * strip_rows, strip_rows)
            nxt = pl.multiple_of(top + strip_rows, strip_rows)
            for part, acc in ((1, acc_n), (0, acc_w)):
                at = pl.multiple_of(j * (2 * strip_rows) + part * strip_rows, strip_rows)
                v = chunk[pl.ds(at, strip_rows), :] * wt
                v = pltpu.roll(v, rem, 1)
                v = pltpu.roll(v, rr, 0)
                zero = jnp.zeros_like(v)
                a = jnp.where(sub_lo, v, zero)
                b = v - a
                acc[q, pl.ds(top, strip_rows), :] += jnp.where(lane_lo, a, zero)
                acc[q + 1, pl.ds(top, strip_rows), :] += jnp.where(lane_lo, zero, a)
                acc[q, pl.ds(nxt, strip_rows), :] += jnp.where(lane_lo, b, zero)
                acc[q + 1, pl.ds(nxt, strip_rows), :] += jnp.where(lane_lo, zero, b)
            return carry

        lax.fori_loop(0, capacity, body, 0, unroll=min(8, capacity))
    for j in range(lane_blocks):
        n = acc_n[j, pl.ds(0, out_rows), :]
        w = acc_w[j, pl.ds(0, out_rows), :]
        wmap_ref[:, pl.ds(j * lanes, lanes)] = w
        coadd_ref[:, pl.ds(j * lanes, lanes)] = n / jnp.maximum(w, 1.0)


def place(chunks, meta, visit_weight, patch_rows, patch_cols):
    lanes = chunks[0].shape[1]
    strip_rows = 8
    lane_blocks = patch_cols // lanes
    smem = pltpu.SMEM
    return pl.pallas_call(
        place_kernel,
        out_shape=(
            jax.ShapeDtypeStruct((patch_rows, patch_cols), jnp.float32),
            jax.ShapeDtypeStruct((patch_rows, patch_cols), jnp.float32),
        ),
        in_specs=[pl.BlockSpec(memory_space=smem)] * 2
        + [pl.BlockSpec(memory_space=pltpu.VMEM)] * len(chunks),
        out_specs=(pl.BlockSpec(memory_space=pltpu.VMEM), pl.BlockSpec(memory_space=pltpu.VMEM)),
        scratch_shapes=[
            pltpu.VMEM((lane_blocks + 1, patch_rows + strip_rows, lanes), jnp.float32),
            pltpu.VMEM((lane_blocks + 1, patch_rows + strip_rows, lanes), jnp.float32),
        ],
    )(meta, visit_weight, *chunks)


def shards(
    exposures, variance, mask_bits, kernel_coeffs, ccd_visit, strip_patch, strip_row, strip_col
):
    ccd_count, height, columns = exposures.shape
    strip_total = strip_patch.shape[0]
    per_ccd = strip_total // ccd_count
    strip_rows = height // per_ccd
    devices = lax.axis_size("patch")
    capacity = 2 * strip_total // devices
    usable = (jnp.bitwise_and(mask_bits, 3) != 3).astype(jnp.float32)
    visit_hot = (ccd_visit == jnp.arange(VISITS)[None, :]).astype(jnp.float32)
    local_count = jnp.sum(jnp.sum(usable, axis=(1, 2))[:, None] * visit_hot, axis=0)
    local_load = jnp.sum(jnp.sum(usable * variance, axis=(1, 2))[:, None] * visit_hot, axis=0)

    destination = strip_patch[:, 0]
    strip_ids = jnp.arange(strip_total)
    earlier = strip_ids[None, :] < strip_ids[:, None]
    same_target = destination[None, :] == destination[:, None]
    slot_rank = jnp.sum(jnp.logical_and(earlier, same_target).astype(jnp.int32), axis=1)
    me = lax.axis_index("patch")
    slot_index = ((destination - me) % devices) * capacity + slot_rank
    slot_total = devices * capacity
    chooser = (slot_index[None, :] == jnp.arange(slot_total)[:, None]).astype(jnp.float32)

    strip_visit = jnp.repeat(ccd_visit[:, 0], per_ccd)
    placement = jnp.stack([strip_row, strip_col, strip_visit], axis=1).astype(jnp.float32)
    slot_meta = jnp.dot(chooser, placement, precision=largest_value).reshape(devices, capacity, 3)
    meta = jnp.concatenate(
        [
            jnp.pad(jnp.swapaxes(slot_meta, 1, 2), ((0, 0), (0, 0), (0, columns - capacity))),
            jnp.broadcast_to(
                jnp.pad(
                    jnp.stack([local_count, local_load])[None],
                    ((0, 0), (0, 3), (0, columns - VISITS)),
                ),
                (devices, 5, columns),
            ),
        ],
        axis=1,
    )
    body_rows = capacity * strip_rows
    convolved = convolve_all(exposures, kernel_coeffs)
    tiles = jnp.concatenate(
        [
            usable.reshape(strip_total, strip_rows * columns),
            (usable * convolved).reshape(strip_total, strip_rows * columns),
        ],
        axis=1,
    )
    packed = jnp.dot(chooser, tiles, precision=largest_value).reshape(
        devices, 2 * body_rows, columns
    )
    payload = jnp.concatenate([packed, meta], axis=1)
    received = [payload[0]]
    for shift in range(1, devices):
        pairs = [(i, (i + shift) % devices) for i in range(devices)]
        received.append(lax.ppermute(payload[shift], "patch", pairs))
    got_meta = jnp.stack([chunk[2 * body_rows :, :] for chunk in received], axis=0)
    visit_count = jnp.sum(got_meta[:, 3, :VISITS], axis=0)
    visit_load = jnp.sum(got_meta[:, 4, :VISITS], axis=0)
    visit_weight = (visit_count + 1.0) / (visit_load + 1.0)
    slot_meta_all = jnp.swapaxes(got_meta[:, 0:3, :capacity], 0, 1).reshape(3 * slot_total)
    coadd_image, weight_map = place(received, slot_meta_all, visit_weight, PH, PW)
    return (coadd_image[None], weight_map[None])


def solution(mesh):
    return jax.shard_map(
        shards,
        mesh=mesh,
        in_specs=(
            P(("band", "patch"), None, None),
            P(("band", "patch"), None, None),
            P(("band", "patch"), None, None),
            P(("band", "patch"), None, None),
            P(("band", "patch"), None),
            P(("band", "patch"), None),
            P(("band", "patch")),
            P(("band", "patch")),
        ),
        out_specs=(P(("band", "patch"), None, None), P(("band", "patch"), None, None)),
        check_vma=False,
    )
```

```python
import jax
import numpy as np
import jax.numpy as jnp
from jax import lax
from jax.experimental import pallas as pl
from jax.experimental.pallas import tpu as pltpu
from jax.sharding import PartitionSpec as P


PH = 128
PW = 512
KS = 21
VISITS = 8


gauss_widths = (0.75, 1.5, 3.0)
largest_value = lax.Precision.HIGHEST
mxu_value = lax.Precision.HIGH


def tap_table(kernel_half_width):
    support = np.arange(-kernel_half_width, kernel_half_width + 1).astype(np.float64)
    tables = []
    for spread in gauss_widths:
        s32 = float(np.float32(spread))
        gauss_total = np.sum(np.exp(-support * support / (2.0 * s32 * s32)))
        profile = np.exp(-support * support / (2.0 * s32 * s32)) / gauss_total
        scaled = support / s32
        tables.append(np.stack([profile, profile * scaled, profile * scaled * scaled]))
    return np.stack(tables)


def row_blocks(block_rows, window_rows, kernel_half_width, lead):
    taps = tap_table(kernel_half_width).reshape(9, 2 * kernel_half_width + 1)
    out = np.zeros((9, block_rows, window_rows), np.float64)
    for i in range(block_rows):
        start = lead + i - kernel_half_width
        out[:, i, start : start + 2 * kernel_half_width + 1] = taps
    return out.astype(np.float32)


def column_ops(column_count, kernel_half_width):
    taps = tap_table(kernel_half_width)
    out = np.zeros((3, 3, column_count, column_count), np.float64)
    for y in range(column_count):
        lo = max(0, y - kernel_half_width)
        hi = min(column_count, y + kernel_half_width + 1)
        for x in range(lo, hi):
            out[:, :, y, x] = taps[:, :, y - x + kernel_half_width]
    return out.astype(np.float32)


def convolve_all(exposures, kernel_coeffs):
    kernel_half_width = KS // 2
    n, height, columns = exposures.shape
    block = 8
    blocks = height // block
    lead = -(-kernel_half_width // block) * block
    reach = -(-(lead + kernel_half_width + block) // block)
    total_rows = (blocks + reach - 1) * block
    padded = jnp.pad(
        exposures, ((0, 0), (lead, total_rows - height - lead), (0, 0))
    ).reshape(n, blocks + reach - 1, block, columns)
    windows = jnp.concatenate([padded[:, j : j + blocks] for j in range(reach)], axis=2)
    rows = jnp.asarray(row_blocks(block, reach * block, kernel_half_width, lead))
    smooth = jnp.einsum("kit,nqtx->nqkix", rows, windows, precision=mxu_value)
    x_np = 2.0 * np.arange(columns, dtype=np.float32) / np.float32(columns - 1) - 1.0
    basis = np.zeros((6, 3, columns), np.float32)
    basis[0, 0] = 1.0
    basis[1, 0] = x_np
    basis[3, 0] = x_np * x_np
    basis[2, 1] = 1.0
    basis[4, 1] = x_np
    basis[5, 2] = 1.0
    fx = jnp.dot(
        kernel_coeffs.reshape(n * 27, 6), jnp.asarray(basis.reshape(6, 3 * columns)),
        precision=largest_value,
    ).reshape(n, 3, 3, 3, 3, columns)
    col_t = jnp.asarray(np.swapaxes(column_ops(columns, kernel_half_width), 2, 3))
    mixed = (
        col_t[None, :, None, 0, None, :, :] * fx[:, :, :, 0, :, :, None]
        + col_t[None, :, None, 1, None, :, :] * fx[:, :, :, 1, :, :, None]
        + col_t[None, :, None, 2, None, :, :] * fx[:, :, :, 2, :, :, None]
    )
    mixed = mixed.reshape(n, 9, 3 * columns, columns)
    fields = jnp.einsum("nqkiy,nkzy->nqiz", smooth, mixed, precision=mxu_value)
    fields = fields.reshape(n, height, 3 * columns)
    y_line = (2.0 * jnp.arange(height).astype(jnp.float32) / (height - 1) - 1.0)[None, :, None]
    return (
        fields[:, :, :columns]
        + y_line * fields[:, :, columns : 2 * columns]
        + (y_line * y_line) * fields[:, :, 2 * columns :]
    )


def place_kernel(meta_ref, *refs):
    chunks = refs[:-4]
    coadd_ref, wmap_ref, acc_n, acc_w = refs[-4:]
    senders = len(chunks)
    slots = (meta_ref.shape[0] - VISITS) // 3
    capacity = slots // senders
    strip_rows = 8
    lanes = chunks[0].shape[-1]
    lane_blocks = acc_n.shape[0] - 1
    out_rows = coadd_ref.shape[0]
    acc_n[...] = jnp.zeros(acc_n.shape, jnp.float32)
    acc_w[...] = jnp.zeros(acc_w.shape, jnp.float32)
    lane = lax.broadcasted_iota(jnp.int32, (strip_rows, lanes), 1)
    sub = lax.broadcasted_iota(jnp.int32, (strip_rows, lanes), 0)

    for d, chunk in enumerate(chunks):

        def body(j, carry, chunk=chunk, d=d):
            s = d * capacity + j
            r = meta_ref[s].astype(jnp.int32)
            c = meta_ref[slots + s].astype(jnp.int32)
            wt = meta_ref[3 * slots + meta_ref[2 * slots + s].astype(jnp.int32)]
            q = c // lanes
            rem = c - q * lanes
            rq = r // strip_rows
            rr = r - rq * strip_rows
            lane_lo = lane >= rem
            sub_lo = sub >= rr
            top = pl.multiple_of(rq * strip_rows, strip_rows)
            nxt = pl.multiple_of(top + strip_rows, strip_rows)
            for part, acc in ((1, acc_n), (0, acc_w)):
                at = pl.multiple_of(j * (2 * strip_rows) + part * strip_rows, strip_rows)
                if len(chunk.shape) == 3:
                    v = chunk[0, pl.ds(at, strip_rows), :] * wt
                else:
                    v = chunk[pl.ds(at, strip_rows), :] * wt
                v = pltpu.roll(v, rem, 1)
                v = pltpu.roll(v, rr, 0)
                zero = jnp.zeros_like(v)
                a = jnp.where(sub_lo, v, zero)
                b = v - a
                acc[q, pl.ds(top, strip_rows), :] += jnp.where(lane_lo, a, zero)
                acc[q + 1, pl.ds(top, strip_rows), :] += jnp.where(lane_lo, zero, a)
                acc[q, pl.ds(nxt, strip_rows), :] += jnp.where(lane_lo, b, zero)
                acc[q + 1, pl.ds(nxt, strip_rows), :] += jnp.where(lane_lo, zero, b)
            return carry

        lax.fori_loop(0, capacity, body, 0, unroll=min(8, capacity))
    for j in range(lane_blocks):
        n = acc_n[j, pl.ds(0, out_rows), :]
        w = acc_w[j, pl.ds(0, out_rows), :]
        wmap_ref[:, pl.ds(j * lanes, lanes)] = w
        coadd_ref[:, pl.ds(j * lanes, lanes)] = n / jnp.maximum(w, 1.0)


def place(chunks, meta, patch_rows, patch_cols):
    lanes = chunks[0].shape[-1]
    strip_rows = 8
    lane_blocks = patch_cols // lanes
    smem = pltpu.SMEM
    return pl.pallas_call(
        place_kernel,
        out_shape=(
            jax.ShapeDtypeStruct((patch_rows, patch_cols), jnp.float32),
            jax.ShapeDtypeStruct((patch_rows, patch_cols), jnp.float32),
        ),
        in_specs=[pl.BlockSpec(memory_space=smem)]
        + [pl.BlockSpec(memory_space=pltpu.VMEM)] * len(chunks),
        out_specs=(pl.BlockSpec(memory_space=pltpu.VMEM), pl.BlockSpec(memory_space=pltpu.VMEM)),
        scratch_shapes=[
            pltpu.VMEM((lane_blocks + 1, patch_rows + strip_rows, lanes), jnp.float32),
            pltpu.VMEM((lane_blocks + 1, patch_rows + strip_rows, lanes), jnp.float32),
        ],
    )(meta, *chunks)


def shards(
    exposures, variance, mask_bits, kernel_coeffs, ccd_visit, strip_patch, strip_row, strip_col
):
    ccd_count, height, columns = exposures.shape
    strip_total = strip_patch.shape[0]
    per_ccd = strip_total // ccd_count
    strip_rows = height // per_ccd
    devices = lax.axis_size("patch")
    capacity = 2 * strip_total // devices
    usable = (jnp.bitwise_and(mask_bits, 3) != 3).astype(jnp.float32)
    visit_hot = (ccd_visit == jnp.arange(VISITS)[None, :]).astype(jnp.float32)
    local_count = jnp.sum(jnp.sum(usable, axis=(1, 2))[:, None] * visit_hot, axis=0)
    local_load = jnp.sum(jnp.sum(usable * variance, axis=(1, 2))[:, None] * visit_hot, axis=0)

    destination = strip_patch[:, 0]
    strip_ids = jnp.arange(strip_total)
    earlier = strip_ids[None, :] < strip_ids[:, None]
    same_target = destination[None, :] == destination[:, None]
    slot_rank = jnp.sum(jnp.logical_and(earlier, same_target).astype(jnp.int32), axis=1)
    me = lax.axis_index("patch")
    slot_index = ((destination - me) % devices) * capacity + slot_rank
    slot_total = devices * capacity
    chooser = (slot_index[None, :] == jnp.arange(slot_total)[:, None]).astype(jnp.float32)

    strip_visit = jnp.repeat(ccd_visit[:, 0], per_ccd)
    placement = jnp.stack([strip_row, strip_col, strip_visit], axis=1).astype(jnp.float32)
    slot_meta = jnp.dot(chooser, placement, precision=largest_value).reshape(devices, capacity, 3)
    meta = jnp.concatenate(
        [
            jnp.pad(jnp.swapaxes(slot_meta, 1, 2), ((0, 0), (0, 0), (0, columns - capacity))),
            jnp.broadcast_to(
                jnp.pad(
                    jnp.stack([local_count, local_load])[None],
                    ((0, 0), (0, 3), (0, columns - VISITS)),
                ),
                (devices, 5, columns),
            ),
        ],
        axis=1,
    )
    body_rows = capacity * strip_rows
    convolved = convolve_all(exposures, kernel_coeffs)
    tiles = jnp.concatenate(
        [
            usable.reshape(strip_total, strip_rows * columns),
            (usable * convolved).reshape(strip_total, strip_rows * columns),
        ],
        axis=1,
    )
    packed = jnp.dot(chooser, tiles, precision=largest_value).reshape(
        devices, 2 * body_rows, columns
    )
    payload = jnp.concatenate([packed, meta], axis=1)
    received = [payload[0]]
    for shift in range(1, devices):
        pairs = [(i, (i + shift) % devices) for i in range(devices)]
        received.append(lax.ppermute(payload[shift], "patch", pairs))
    got_meta = jnp.stack([chunk[2 * body_rows :, :] for chunk in received], axis=0)
    visit_count = jnp.sum(got_meta[:, 3, :VISITS], axis=0)
    visit_load = jnp.sum(got_meta[:, 4, :VISITS], axis=0)
    visit_weight = (visit_count + 1.0) / (visit_load + 1.0)
    slot_meta_all = jnp.swapaxes(got_meta[:, 0:3, :capacity], 0, 1).reshape(3 * slot_total)
    meta_all = jnp.concatenate([slot_meta_all, visit_weight])
    coadd_image, weight_map = place([payload] + received[1:], meta_all, PH, PW)
    return (coadd_image[None], weight_map[None])


def solution(mesh):
    return jax.shard_map(
        shards,
        mesh=mesh,
        in_specs=(
            P(("band", "patch"), None, None),
            P(("band", "patch"), None, None),
            P(("band", "patch"), None, None),
            P(("band", "patch"), None, None),
            P(("band", "patch"), None),
            P(("band", "patch"), None),
            P(("band", "patch")),
            P(("band", "patch")),
        ),
        out_specs=(P(("band", "patch"), None, None), P(("band", "patch"), None, None)),
        check_vma=False,
    )
```

```python
import jax
import numpy as np
import jax.numpy as jnp
from jax import lax
from jax.experimental import pallas as pl
from jax.experimental.pallas import tpu as pltpu
from jax.sharding import PartitionSpec as P


PH = 128
PW = 512
KS = 21
VISITS = 8
ACC_SETS = 4


gauss_widths = (0.75, 1.5, 3.0)
largest_value = lax.Precision.HIGHEST
mxu_value = lax.Precision.HIGH


def tap_table(kernel_half_width):
    support = np.arange(-kernel_half_width, kernel_half_width + 1).astype(np.float64)
    tables = []
    for spread in gauss_widths:
        s32 = float(np.float32(spread))
        gauss_total = np.sum(np.exp(-support * support / (2.0 * s32 * s32)))
        profile = np.exp(-support * support / (2.0 * s32 * s32)) / gauss_total
        scaled = support / s32
        tables.append(np.stack([profile, profile * scaled, profile * scaled * scaled]))
    return np.stack(tables)


def row_blocks(block_rows, window_rows, kernel_half_width, lead):
    taps = tap_table(kernel_half_width).reshape(9, 2 * kernel_half_width + 1)
    out = np.zeros((9, block_rows, window_rows), np.float64)
    for i in range(block_rows):
        start = lead + i - kernel_half_width
        out[:, i, start : start + 2 * kernel_half_width + 1] = taps
    return out.astype(np.float32)


def column_ops(column_count, kernel_half_width):
    taps = tap_table(kernel_half_width)
    out = np.zeros((3, 3, column_count, column_count), np.float64)
    for y in range(column_count):
        lo = max(0, y - kernel_half_width)
        hi = min(column_count, y + kernel_half_width + 1)
        for x in range(lo, hi):
            out[:, :, y, x] = taps[:, :, y - x + kernel_half_width]
    return out.astype(np.float32)


def convolve_all(exposures, kernel_coeffs):
    kernel_half_width = KS // 2
    n, height, columns = exposures.shape
    block = 8
    blocks = height // block
    lead = -(-kernel_half_width // block) * block
    reach = -(-(lead + kernel_half_width + block) // block)
    total_rows = (blocks + reach - 1) * block
    padded = jnp.pad(
        exposures, ((0, 0), (lead, total_rows - height - lead), (0, 0))
    ).reshape(n, blocks + reach - 1, block, columns)
    windows = jnp.concatenate([padded[:, j : j + blocks] for j in range(reach)], axis=2)
    rows = jnp.asarray(row_blocks(block, reach * block, kernel_half_width, lead))
    smooth = jnp.einsum("kit,nqtx->nqkix", rows, windows, precision=mxu_value)
    x_np = 2.0 * np.arange(columns, dtype=np.float32) / np.float32(columns - 1) - 1.0
    basis = np.zeros((6, 3, columns), np.float32)
    basis[0, 0] = 1.0
    basis[1, 0] = x_np
    basis[3, 0] = x_np * x_np
    basis[2, 1] = 1.0
    basis[4, 1] = x_np
    basis[5, 2] = 1.0
    fx = jnp.dot(
        kernel_coeffs.reshape(n * 27, 6), jnp.asarray(basis.reshape(6, 3 * columns)),
        precision=largest_value,
    ).reshape(n, 3, 3, 3, 3, columns)
    col_t = jnp.asarray(np.swapaxes(column_ops(columns, kernel_half_width), 2, 3))
    mixed = (
        col_t[None, :, None, 0, None, :, :] * fx[:, :, :, 0, :, :, None]
        + col_t[None, :, None, 1, None, :, :] * fx[:, :, :, 1, :, :, None]
        + col_t[None, :, None, 2, None, :, :] * fx[:, :, :, 2, :, :, None]
    )
    mixed = mixed.reshape(n, 9, 3 * columns, columns)
    fields = jnp.einsum("nqkiy,nkzy->nqiz", smooth, mixed, precision=mxu_value)
    fields = fields.reshape(n, height, 3 * columns)
    y_line = (2.0 * jnp.arange(height).astype(jnp.float32) / (height - 1) - 1.0)[None, :, None]
    return (
        fields[:, :, :columns]
        + y_line * fields[:, :, columns : 2 * columns]
        + (y_line * y_line) * fields[:, :, 2 * columns :]
    )


def place_kernel(meta_ref, *refs):
    coadd_ref, wmap_ref = refs[-2 - 2 * ACC_SETS : -2 * ACC_SETS]
    accs_n = refs[-2 * ACC_SETS : -ACC_SETS]
    accs_w = refs[-ACC_SETS:]
    chunks = refs[: -2 - 2 * ACC_SETS]
    senders = len(chunks)
    slots = (meta_ref.shape[0] - VISITS) // 3
    capacity = slots // senders
    ways = min(ACC_SETS, capacity)
    strip_rows = 8
    lanes = chunks[0].shape[-1]
    lane_blocks = accs_n[0].shape[0] - 1
    out_rows = coadd_ref.shape[0]
    for acc in accs_n + accs_w:
        acc[...] = jnp.zeros(acc.shape, jnp.float32)
    lane = lax.broadcasted_iota(jnp.int32, (strip_rows, lanes), 1)
    sub = lax.broadcasted_iota(jnp.int32, (strip_rows, lanes), 0)

    def one_slot(chunk, d, j, acc_n, acc_w):
        s = d * capacity + j
        r = meta_ref[s].astype(jnp.int32)
        c = meta_ref[slots + s].astype(jnp.int32)
        wt = meta_ref[3 * slots + meta_ref[2 * slots + s].astype(jnp.int32)]
        q = c // lanes
        rem = c - q * lanes
        rq = r // strip_rows
        rr = r - rq * strip_rows
        lane_lo = lane >= rem
        sub_lo = sub >= rr
        top = pl.multiple_of(rq * strip_rows, strip_rows)
        nxt = pl.multiple_of(top + strip_rows, strip_rows)
        for part, acc in ((1, acc_n), (0, acc_w)):
            at = pl.multiple_of(j * (2 * strip_rows) + part * strip_rows, strip_rows)
            if len(chunk.shape) == 3:
                v = chunk[0, pl.ds(at, strip_rows), :] * wt
            else:
                v = chunk[pl.ds(at, strip_rows), :] * wt
            v = pltpu.roll(v, rem, 1)
            v = pltpu.roll(v, rr, 0)
            zero = jnp.zeros_like(v)
            a = jnp.where(sub_lo, v, zero)
            b = v - a
            acc[q, pl.ds(top, strip_rows), :] += jnp.where(lane_lo, a, zero)
            acc[q + 1, pl.ds(top, strip_rows), :] += jnp.where(lane_lo, zero, a)
            acc[q, pl.ds(nxt, strip_rows), :] += jnp.where(lane_lo, b, zero)
            acc[q + 1, pl.ds(nxt, strip_rows), :] += jnp.where(lane_lo, zero, b)

    for d, chunk in enumerate(chunks):

        def body(jj, carry, chunk=chunk, d=d):
            for t in range(ways):
                one_slot(chunk, d, jj * ways + t, accs_n[t], accs_w[t])
            return carry

        rounds = capacity // ways
        lax.fori_loop(0, rounds, body, 0, unroll=max(1, min(2, rounds)))
    for j in range(lane_blocks):
        n = accs_n[0][j, pl.ds(0, out_rows), :]
        w = accs_w[0][j, pl.ds(0, out_rows), :]
        for t in range(1, ways):
            n = n + accs_n[t][j, pl.ds(0, out_rows), :]
            w = w + accs_w[t][j, pl.ds(0, out_rows), :]
        wmap_ref[:, pl.ds(j * lanes, lanes)] = w
        coadd_ref[:, pl.ds(j * lanes, lanes)] = n / jnp.maximum(w, 1.0)


def place(chunks, meta, patch_rows, patch_cols):
    lanes = chunks[0].shape[-1]
    strip_rows = 8
    lane_blocks = patch_cols // lanes
    smem = pltpu.SMEM
    acc_shape = (lane_blocks + 1, patch_rows + strip_rows, lanes)
    return pl.pallas_call(
        place_kernel,
        out_shape=(
            jax.ShapeDtypeStruct((patch_rows, patch_cols), jnp.float32),
            jax.ShapeDtypeStruct((patch_rows, patch_cols), jnp.float32),
        ),
        in_specs=[pl.BlockSpec(memory_space=smem)]
        + [pl.BlockSpec(memory_space=pltpu.VMEM)] * len(chunks),
        out_specs=(pl.BlockSpec(memory_space=pltpu.VMEM), pl.BlockSpec(memory_space=pltpu.VMEM)),
        scratch_shapes=[pltpu.VMEM(acc_shape, jnp.float32)] * (2 * ACC_SETS),
    )(meta, *chunks)


def shards(
    exposures, variance, mask_bits, kernel_coeffs, ccd_visit, strip_patch, strip_row, strip_col
):
    ccd_count, height, columns = exposures.shape
    strip_total = strip_patch.shape[0]
    per_ccd = strip_total // ccd_count
    strip_rows = height // per_ccd
    devices = lax.axis_size("patch")
    capacity = 2 * strip_total // devices
    usable = (jnp.bitwise_and(mask_bits, 3) != 3).astype(jnp.float32)
    visit_hot = (ccd_visit == jnp.arange(VISITS)[None, :]).astype(jnp.float32)
    local_count = jnp.sum(jnp.sum(usable, axis=(1, 2))[:, None] * visit_hot, axis=0)
    local_load = jnp.sum(jnp.sum(usable * variance, axis=(1, 2))[:, None] * visit_hot, axis=0)

    destination = strip_patch[:, 0]
    strip_ids = jnp.arange(strip_total)
    earlier = strip_ids[None, :] < strip_ids[:, None]
    same_target = destination[None, :] == destination[:, None]
    slot_rank = jnp.sum(jnp.logical_and(earlier, same_target).astype(jnp.int32), axis=1)
    me = lax.axis_index("patch")
    slot_index = ((destination - me) % devices) * capacity + slot_rank
    slot_total = devices * capacity
    chooser = (slot_index[None, :] == jnp.arange(slot_total)[:, None]).astype(jnp.float32)

    strip_visit = jnp.repeat(ccd_visit[:, 0], per_ccd)
    placement = jnp.stack([strip_row, strip_col, strip_visit], axis=1).astype(jnp.float32)
    slot_meta = jnp.dot(chooser, placement, precision=largest_value).reshape(devices, capacity, 3)
    meta = jnp.concatenate(
        [
            jnp.pad(jnp.swapaxes(slot_meta, 1, 2), ((0, 0), (0, 0), (0, columns - capacity))),
            jnp.broadcast_to(
                jnp.pad(
                    jnp.stack([local_count, local_load])[None],
                    ((0, 0), (0, 3), (0, columns - VISITS)),
                ),
                (devices, 5, columns),
            ),
        ],
        axis=1,
    )
    body_rows = capacity * strip_rows
    convolved = convolve_all(exposures, kernel_coeffs)
    tiles = jnp.concatenate(
        [
            usable.reshape(strip_total, strip_rows * columns),
            (usable * convolved).reshape(strip_total, strip_rows * columns),
        ],
        axis=1,
    )
    packed = jnp.dot(chooser, tiles, precision=largest_value).reshape(
        devices, 2 * body_rows, columns
    )
    payload = jnp.concatenate([packed, meta], axis=1)
    received = [payload[0]]
    for shift in range(1, devices):
        pairs = [(i, (i + shift) % devices) for i in range(devices)]
        received.append(lax.ppermute(payload[shift], "patch", pairs))
    got_meta = jnp.stack([chunk[2 * body_rows :, :] for chunk in received], axis=0)
    visit_count = jnp.sum(got_meta[:, 3, :VISITS], axis=0)
    visit_load = jnp.sum(got_meta[:, 4, :VISITS], axis=0)
    visit_weight = (visit_count + 1.0) / (visit_load + 1.0)
    slot_meta_all = jnp.swapaxes(got_meta[:, 0:3, :capacity], 0, 1).reshape(3 * slot_total)
    meta_all = jnp.concatenate([slot_meta_all, visit_weight])
    coadd_image, weight_map = place([payload] + received[1:], meta_all, PH, PW)
    return (coadd_image[None], weight_map[None])


def solution(mesh):
    return jax.shard_map(
        shards,
        mesh=mesh,
        in_specs=(
            P(("band", "patch"), None, None),
            P(("band", "patch"), None, None),
            P(("band", "patch"), None, None),
            P(("band", "patch"), None, None),
            P(("band", "patch"), None),
            P(("band", "patch"), None),
            P(("band", "patch")),
            P(("band", "patch")),
        ),
        out_specs=(P(("band", "patch"), None, None), P(("band", "patch"), None, None)),
        check_vma=False,
    )
```

```python
import jax
import numpy as np
import jax.numpy as jnp
from jax import lax
from jax.experimental import pallas as pl
from jax.experimental.pallas import tpu as pltpu
from jax.sharding import PartitionSpec as P


PH = 128
PW = 512
KS = 21
VISITS = 8


gauss_widths = (0.75, 1.5, 3.0)
largest_value = lax.Precision.HIGHEST
mxu_value = lax.Precision.HIGH


def tap_table(kernel_half_width):
    support = np.arange(-kernel_half_width, kernel_half_width + 1).astype(np.float64)
    tables = []
    for spread in gauss_widths:
        s32 = float(np.float32(spread))
        gauss_total = np.sum(np.exp(-support * support / (2.0 * s32 * s32)))
        profile = np.exp(-support * support / (2.0 * s32 * s32)) / gauss_total
        scaled = support / s32
        tables.append(np.stack([profile, profile * scaled, profile * scaled * scaled]))
    return np.stack(tables)


def row_blocks(block_rows, window_rows, kernel_half_width, lead):
    taps = tap_table(kernel_half_width).reshape(9, 2 * kernel_half_width + 1)
    out = np.zeros((9, block_rows, window_rows), np.float64)
    for i in range(block_rows):
        start = lead + i - kernel_half_width
        out[:, i, start : start + 2 * kernel_half_width + 1] = taps
    return out.astype(np.float32)


def column_ops(column_count, kernel_half_width):
    taps = tap_table(kernel_half_width)
    out = np.zeros((3, 3, column_count, column_count), np.float64)
    for y in range(column_count):
        lo = max(0, y - kernel_half_width)
        hi = min(column_count, y + kernel_half_width + 1)
        for x in range(lo, hi):
            out[:, :, y, x] = taps[:, :, y - x + kernel_half_width]
    return out.astype(np.float32)


def convolve_all(exposures, kernel_coeffs):
    kernel_half_width = KS // 2
    n, height, columns = exposures.shape
    block = 8
    blocks = height // block
    lead = -(-kernel_half_width // block) * block
    reach = -(-(lead + kernel_half_width + block) // block)
    total_rows = (blocks + reach - 1) * block
    padded = jnp.pad(
        exposures, ((0, 0), (lead, total_rows - height - lead), (0, 0))
    ).reshape(n, blocks + reach - 1, block, columns)
    windows = jnp.concatenate([padded[:, j : j + blocks] for j in range(reach)], axis=2)
    rows = jnp.asarray(row_blocks(block, reach * block, kernel_half_width, lead))
    smooth = jnp.einsum("kit,nqtx->nqkix", rows, windows, precision=mxu_value)
    x_np = 2.0 * np.arange(columns, dtype=np.float32) / np.float32(columns - 1) - 1.0
    basis = np.zeros((6, 3, columns), np.float32)
    basis[0, 0] = 1.0
    basis[1, 0] = x_np
    basis[3, 0] = x_np * x_np
    basis[2, 1] = 1.0
    basis[4, 1] = x_np
    basis[5, 2] = 1.0
    fx = jnp.dot(
        kernel_coeffs.reshape(n * 27, 6), jnp.asarray(basis.reshape(6, 3 * columns)),
        precision=largest_value,
    ).reshape(n, 3, 3, 3, 3, columns)
    col_t = jnp.asarray(np.swapaxes(column_ops(columns, kernel_half_width), 2, 3))
    mixed = (
        col_t[None, :, None, 0, None, :, :] * fx[:, :, :, 0, :, :, None]
        + col_t[None, :, None, 1, None, :, :] * fx[:, :, :, 1, :, :, None]
        + col_t[None, :, None, 2, None, :, :] * fx[:, :, :, 2, :, :, None]
    )
    mixed = mixed.reshape(n, 9, 3 * columns, columns)
    fields = jnp.einsum("nqkiy,nkzy->nqiz", smooth, mixed, precision=mxu_value)
    fields = fields.reshape(n, height, 3 * columns)
    y_line = (2.0 * jnp.arange(height).astype(jnp.float32) / (height - 1) - 1.0)[None, :, None]
    return (
        fields[:, :, :columns]
        + y_line * fields[:, :, columns : 2 * columns]
        + (y_line * y_line) * fields[:, :, 2 * columns :]
    )


def place_kernel(index_ref, scale_ref, *refs):
    chunks = refs[:-4]
    coadd_ref, wmap_ref, acc_n, acc_w = refs[-4:]
    senders = len(chunks)
    slots = scale_ref.shape[0]
    capacity = slots // senders
    strip_rows = 8
    lanes = chunks[0].shape[-1]
    lane_blocks = acc_n.shape[0] - 1
    out_rows = coadd_ref.shape[0]
    acc_n[...] = jnp.zeros(acc_n.shape, jnp.float32)
    acc_w[...] = jnp.zeros(acc_w.shape, jnp.float32)
    lane = lax.broadcasted_iota(jnp.int32, (strip_rows, lanes), 1)
    sub = lax.broadcasted_iota(jnp.int32, (strip_rows, lanes), 0)

    for d, chunk in enumerate(chunks):

        def body(j, carry, chunk=chunk, d=d):
            s = d * capacity + j
            q = index_ref[s]
            rem = index_ref[slots + s]
            top = pl.multiple_of(index_ref[2 * slots + s], strip_rows)
            rr = index_ref[3 * slots + s]
            wt = scale_ref[s]
            lane_lo = lane >= rem
            sub_lo = sub >= rr
            nxt = pl.multiple_of(top + strip_rows, strip_rows)
            for part, acc in ((1, acc_n), (0, acc_w)):
                at = pl.multiple_of(j * (2 * strip_rows) + part * strip_rows, strip_rows)
                if len(chunk.shape) == 3:
                    v = chunk[0, pl.ds(at, strip_rows), :] * wt
                else:
                    v = chunk[pl.ds(at, strip_rows), :] * wt
                v = pltpu.roll(v, rem, 1)
                v = pltpu.roll(v, rr, 0)
                zero = jnp.zeros_like(v)
                a = jnp.where(sub_lo, v, zero)
                b = v - a
                acc[q, pl.ds(top, strip_rows), :] += jnp.where(lane_lo, a, zero)
                acc[q + 1, pl.ds(top, strip_rows), :] += jnp.where(lane_lo, zero, a)
                acc[q, pl.ds(nxt, strip_rows), :] += jnp.where(lane_lo, b, zero)
                acc[q + 1, pl.ds(nxt, strip_rows), :] += jnp.where(lane_lo, zero, b)
            return carry

        lax.fori_loop(0, capacity, body, 0, unroll=min(8, capacity))
    for j in range(lane_blocks):
        n = acc_n[j, pl.ds(0, out_rows), :]
        w = acc_w[j, pl.ds(0, out_rows), :]
        wmap_ref[:, pl.ds(j * lanes, lanes)] = w
        coadd_ref[:, pl.ds(j * lanes, lanes)] = n / jnp.maximum(w, 1.0)


def place(chunks, index, scale, patch_rows, patch_cols):
    lanes = chunks[0].shape[-1]
    strip_rows = 8
    lane_blocks = patch_cols // lanes
    smem = pltpu.SMEM
    return pl.pallas_call(
        place_kernel,
        out_shape=(
            jax.ShapeDtypeStruct((patch_rows, patch_cols), jnp.float32),
            jax.ShapeDtypeStruct((patch_rows, patch_cols), jnp.float32),
        ),
        in_specs=[pl.BlockSpec(memory_space=smem)] * 2
        + [pl.BlockSpec(memory_space=pltpu.VMEM)] * len(chunks),
        out_specs=(pl.BlockSpec(memory_space=pltpu.VMEM), pl.BlockSpec(memory_space=pltpu.VMEM)),
        scratch_shapes=[
            pltpu.VMEM((lane_blocks + 1, patch_rows + strip_rows, lanes), jnp.float32),
            pltpu.VMEM((lane_blocks + 1, patch_rows + strip_rows, lanes), jnp.float32),
        ],
    )(index, scale, *chunks)


def shards(
    exposures, variance, mask_bits, kernel_coeffs, ccd_visit, strip_patch, strip_row, strip_col
):
    ccd_count, height, columns = exposures.shape
    strip_total = strip_patch.shape[0]
    per_ccd = strip_total // ccd_count
    strip_rows = height // per_ccd
    devices = lax.axis_size("patch")
    capacity = 2 * strip_total // devices
    usable = (jnp.bitwise_and(mask_bits, 3) != 3).astype(jnp.float32)
    visit_hot = (ccd_visit == jnp.arange(VISITS)[None, :]).astype(jnp.float32)
    local_count = jnp.sum(jnp.sum(usable, axis=(1, 2))[:, None] * visit_hot, axis=0)
    local_load = jnp.sum(jnp.sum(usable * variance, axis=(1, 2))[:, None] * visit_hot, axis=0)

    destination = strip_patch[:, 0]
    strip_ids = jnp.arange(strip_total)
    earlier = strip_ids[None, :] < strip_ids[:, None]
    same_target = destination[None, :] == destination[:, None]
    slot_rank = jnp.sum(jnp.logical_and(earlier, same_target).astype(jnp.int32), axis=1)
    me = lax.axis_index("patch")
    slot_index = ((destination - me) % devices) * capacity + slot_rank
    slot_total = devices * capacity
    chooser = (slot_index[None, :] == jnp.arange(slot_total)[:, None]).astype(jnp.float32)

    strip_visit = jnp.repeat(ccd_visit[:, 0], per_ccd)
    placement = jnp.stack([strip_row, strip_col, strip_visit], axis=1).astype(jnp.float32)
    slot_meta = jnp.dot(chooser, placement, precision=largest_value).reshape(devices, capacity, 3)
    meta = jnp.concatenate(
        [
            jnp.pad(jnp.swapaxes(slot_meta, 1, 2), ((0, 0), (0, 0), (0, columns - capacity))),
            jnp.broadcast_to(
                jnp.pad(
                    jnp.stack([local_count, local_load])[None],
                    ((0, 0), (0, 3), (0, columns - VISITS)),
                ),
                (devices, 5, columns),
            ),
        ],
        axis=1,
    )
    body_rows = capacity * strip_rows
    convolved = convolve_all(exposures, kernel_coeffs)
    tiles = jnp.concatenate(
        [
            usable.reshape(strip_total, strip_rows * columns),
            (usable * convolved).reshape(strip_total, strip_rows * columns),
        ],
        axis=1,
    )
    packed = jnp.dot(chooser, tiles, precision=largest_value).reshape(
        devices, 2 * body_rows, columns
    )
    payload = jnp.concatenate([packed, meta], axis=1)
    received = [payload[0]]
    for shift in range(1, devices):
        pairs = [(i, (i + shift) % devices) for i in range(devices)]
        received.append(lax.ppermute(payload[shift], "patch", pairs))
    got_meta = jnp.stack([chunk[2 * body_rows :, :] for chunk in received], axis=0)
    visit_count = jnp.sum(got_meta[:, 3, :VISITS], axis=0)
    visit_load = jnp.sum(got_meta[:, 4, :VISITS], axis=0)
    visit_weight = (visit_count + 1.0) / (visit_load + 1.0)
    slot_rows = got_meta[:, 0, :capacity].reshape(slot_total).astype(jnp.int32)
    slot_cols = got_meta[:, 1, :capacity].reshape(slot_total).astype(jnp.int32)
    slot_visit = got_meta[:, 2, :capacity].reshape(slot_total).astype(jnp.int32)
    slot_hot = (slot_visit[:, None] == jnp.arange(VISITS)[None, :]).astype(jnp.float32)
    slot_weight = jnp.sum(slot_hot * visit_weight[None, :], axis=1)
    index = jnp.concatenate(
        [
            slot_cols // columns,
            slot_cols % columns,
            (slot_rows // strip_rows) * strip_rows,
            slot_rows % strip_rows,
        ]
    )
    coadd_image, weight_map = place([payload] + received[1:], index, slot_weight, PH, PW)
    return (coadd_image[None], weight_map[None])


def solution(mesh):
    return jax.shard_map(
        shards,
        mesh=mesh,
        in_specs=(
            P(("band", "patch"), None, None),
            P(("band", "patch"), None, None),
            P(("band", "patch"), None, None),
            P(("band", "patch"), None, None),
            P(("band", "patch"), None),
            P(("band", "patch"), None),
            P(("band", "patch")),
            P(("band", "patch")),
        ),
        out_specs=(P(("band", "patch"), None, None), P(("band", "patch"), None, None)),
        check_vma=False,
    )
```

```python
import jax
import numpy as np
import jax.numpy as jnp
from jax import lax
from jax.experimental import pallas as pl
from jax.experimental.pallas import tpu as pltpu
from jax.sharding import PartitionSpec as P


PH = 128
PW = 512
KS = 21
VISITS = 8


gauss_widths = (0.75, 1.5, 3.0)
largest_value = lax.Precision.HIGHEST
mxu_value = lax.Precision.HIGH


def tap_table(kernel_half_width):
    support = np.arange(-kernel_half_width, kernel_half_width + 1).astype(np.float64)
    tables = []
    for spread in gauss_widths:
        s32 = float(np.float32(spread))
        gauss_total = np.sum(np.exp(-support * support / (2.0 * s32 * s32)))
        profile = np.exp(-support * support / (2.0 * s32 * s32)) / gauss_total
        scaled = support / s32
        tables.append(np.stack([profile, profile * scaled, profile * scaled * scaled]))
    return np.stack(tables)


def row_blocks(block_rows, window_rows, kernel_half_width, lead):
    taps = tap_table(kernel_half_width).reshape(9, 2 * kernel_half_width + 1)
    out = np.zeros((9, block_rows, window_rows), np.float64)
    for i in range(block_rows):
        start = lead + i - kernel_half_width
        out[:, i, start : start + 2 * kernel_half_width + 1] = taps
    return out.astype(np.float32)


def column_ops(column_count, kernel_half_width):
    taps = tap_table(kernel_half_width)
    out = np.zeros((3, 3, column_count, column_count), np.float64)
    for y in range(column_count):
        lo = max(0, y - kernel_half_width)
        hi = min(column_count, y + kernel_half_width + 1)
        for x in range(lo, hi):
            out[:, :, y, x] = taps[:, :, y - x + kernel_half_width]
    return out.astype(np.float32)


def convolve_all(exposures, kernel_coeffs):
    kernel_half_width = KS // 2
    n, height, columns = exposures.shape
    block = 8
    blocks = height // block
    lead = -(-kernel_half_width // block) * block
    reach = -(-(lead + kernel_half_width + block) // block)
    total_rows = (blocks + reach - 1) * block
    padded = jnp.pad(
        exposures, ((0, 0), (lead, total_rows - height - lead), (0, 0))
    ).reshape(n, blocks + reach - 1, block, columns)
    windows = jnp.concatenate([padded[:, j : j + blocks] for j in range(reach)], axis=2)
    rows = jnp.asarray(row_blocks(block, reach * block, kernel_half_width, lead))
    smooth = jnp.einsum("kit,nqtx->nqkix", rows, windows, precision=mxu_value)
    x_np = 2.0 * np.arange(columns, dtype=np.float32) / np.float32(columns - 1) - 1.0
    basis = np.zeros((6, 3, columns), np.float32)
    basis[0, 0] = 1.0
    basis[1, 0] = x_np
    basis[3, 0] = x_np * x_np
    basis[2, 1] = 1.0
    basis[4, 1] = x_np
    basis[5, 2] = 1.0
    fx = jnp.dot(
        kernel_coeffs.reshape(n * 27, 6), jnp.asarray(basis.reshape(6, 3 * columns)),
        precision=largest_value,
    ).reshape(n, 3, 3, 3, 3, columns)
    col_t = jnp.asarray(np.swapaxes(column_ops(columns, kernel_half_width), 2, 3))
    mixed = (
        col_t[None, :, None, 0, None, :, :] * fx[:, :, :, 0, :, :, None]
        + col_t[None, :, None, 1, None, :, :] * fx[:, :, :, 1, :, :, None]
        + col_t[None, :, None, 2, None, :, :] * fx[:, :, :, 2, :, :, None]
    )
    mixed = mixed.reshape(n, 9, 3 * columns, columns)
    fields = jnp.einsum("nqkiy,nkzy->nqiz", smooth, mixed, precision=mxu_value)
    fields = fields.reshape(n, height, 3 * columns)
    y_line = (2.0 * jnp.arange(height).astype(jnp.float32) / (height - 1) - 1.0)[None, :, None]
    return (
        fields[:, :, :columns]
        + y_line * fields[:, :, columns : 2 * columns]
        + (y_line * y_line) * fields[:, :, 2 * columns :]
    )


def place_kernel(index_ref, *refs):
    chunks = refs[:-5]
    coadd_ref, wmap_ref, acc_n, acc_w, table = refs[-5:]
    senders = len(chunks)
    slots = index_ref.shape[0] // 5
    capacity = slots // senders
    strip_rows = 8
    lanes = chunks[0].shape[-1]
    sums_at = capacity * 2 * strip_rows
    sums = None
    for chunk in chunks:
        if len(chunk.shape) == 3:
            block = chunk[0, pl.ds(sums_at, strip_rows), :]
        else:
            block = chunk[pl.ds(sums_at, strip_rows), :]
        sums = block if sums is None else sums + block
    visit_weight = (sums[3:4, :] + 1.0) / (sums[4:5, :] + 1.0)
    lane_row = lax.broadcasted_iota(jnp.int32, (1, lanes), 1)
    for visit in range(VISITS):
        picked = jnp.sum(jnp.where(lane_row == visit, visit_weight, 0.0), axis=1, keepdims=True)
        table[visit] = jnp.broadcast_to(picked, (strip_rows, lanes))
    lane_blocks = acc_n.shape[0] - 1
    out_rows = coadd_ref.shape[0]
    acc_n[...] = jnp.zeros(acc_n.shape, jnp.float32)
    acc_w[...] = jnp.zeros(acc_w.shape, jnp.float32)
    lane = lax.broadcasted_iota(jnp.int32, (strip_rows, lanes), 1)
    sub = lax.broadcasted_iota(jnp.int32, (strip_rows, lanes), 0)

    for d, chunk in enumerate(chunks):

        def body(j, carry, chunk=chunk, d=d):
            s = d * capacity + j
            q = index_ref[s]
            rem = index_ref[slots + s]
            top = pl.multiple_of(index_ref[2 * slots + s], strip_rows)
            rr = index_ref[3 * slots + s]
            wt = table[index_ref[4 * slots + s]]
            lane_lo = lane >= rem
            sub_lo = sub >= rr
            nxt = pl.multiple_of(top + strip_rows, strip_rows)
            for part, acc in ((1, acc_n), (0, acc_w)):
                at = pl.multiple_of(j * (2 * strip_rows) + part * strip_rows, strip_rows)
                if len(chunk.shape) == 3:
                    v = chunk[0, pl.ds(at, strip_rows), :] * wt
                else:
                    v = chunk[pl.ds(at, strip_rows), :] * wt
                v = pltpu.roll(v, rem, 1)
                v = pltpu.roll(v, rr, 0)
                zero = jnp.zeros_like(v)
                a = jnp.where(sub_lo, v, zero)
                b = v - a
                acc[q, pl.ds(top, strip_rows), :] += jnp.where(lane_lo, a, zero)
                acc[q + 1, pl.ds(top, strip_rows), :] += jnp.where(lane_lo, zero, a)
                acc[q, pl.ds(nxt, strip_rows), :] += jnp.where(lane_lo, b, zero)
                acc[q + 1, pl.ds(nxt, strip_rows), :] += jnp.where(lane_lo, zero, b)
            return carry

        lax.fori_loop(0, capacity, body, 0, unroll=min(8, capacity))
    for j in range(lane_blocks):
        n = acc_n[j, pl.ds(0, out_rows), :]
        w = acc_w[j, pl.ds(0, out_rows), :]
        wmap_ref[:, pl.ds(j * lanes, lanes)] = w
        coadd_ref[:, pl.ds(j * lanes, lanes)] = n / jnp.maximum(w, 1.0)


def place(chunks, index, patch_rows, patch_cols):
    lanes = chunks[0].shape[-1]
    strip_rows = 8
    lane_blocks = patch_cols // lanes
    smem = pltpu.SMEM
    return pl.pallas_call(
        place_kernel,
        out_shape=(
            jax.ShapeDtypeStruct((patch_rows, patch_cols), jnp.float32),
            jax.ShapeDtypeStruct((patch_rows, patch_cols), jnp.float32),
        ),
        in_specs=[pl.BlockSpec(memory_space=smem)]
        + [pl.BlockSpec(memory_space=pltpu.VMEM)] * len(chunks),
        out_specs=(pl.BlockSpec(memory_space=pltpu.VMEM), pl.BlockSpec(memory_space=pltpu.VMEM)),
        scratch_shapes=[
            pltpu.VMEM((lane_blocks + 1, patch_rows + strip_rows, lanes), jnp.float32),
            pltpu.VMEM((lane_blocks + 1, patch_rows + strip_rows, lanes), jnp.float32),
            pltpu.VMEM((VISITS, strip_rows, lanes), jnp.float32),
        ],
    )(index, *chunks)


def shards(
    exposures, variance, mask_bits, kernel_coeffs, ccd_visit, strip_patch, strip_row, strip_col
):
    ccd_count, height, columns = exposures.shape
    strip_total = strip_patch.shape[0]
    per_ccd = strip_total // ccd_count
    strip_rows = height // per_ccd
    devices = lax.axis_size("patch")
    capacity = 2 * strip_total // devices
    usable = (jnp.bitwise_and(mask_bits, 3) != 3).astype(jnp.float32)
    visit_hot = (ccd_visit == jnp.arange(VISITS)[None, :]).astype(jnp.float32)
    local_count = jnp.sum(jnp.sum(usable, axis=(1, 2))[:, None] * visit_hot, axis=0)
    local_load = jnp.sum(jnp.sum(usable * variance, axis=(1, 2))[:, None] * visit_hot, axis=0)

    destination = strip_patch[:, 0]
    strip_ids = jnp.arange(strip_total)
    earlier = strip_ids[None, :] < strip_ids[:, None]
    same_target = destination[None, :] == destination[:, None]
    slot_rank = jnp.sum(jnp.logical_and(earlier, same_target).astype(jnp.int32), axis=1)
    me = lax.axis_index("patch")
    slot_index = ((destination - me) % devices) * capacity + slot_rank
    slot_total = devices * capacity
    chooser = (slot_index[None, :] == jnp.arange(slot_total)[:, None]).astype(jnp.float32)

    strip_visit = jnp.repeat(ccd_visit[:, 0], per_ccd)
    placement = jnp.stack([strip_row, strip_col, strip_visit], axis=1).astype(jnp.float32)
    slot_meta = jnp.dot(chooser, placement, precision=largest_value).reshape(devices, capacity, 3)
    meta = jnp.concatenate(
        [
            jnp.pad(jnp.swapaxes(slot_meta, 1, 2), ((0, 0), (0, 0), (0, columns - capacity))),
            jnp.broadcast_to(
                jnp.pad(
                    jnp.stack([local_count, local_load])[None],
                    ((0, 0), (0, 3), (0, columns - VISITS)),
                ),
                (devices, 5, columns),
            ),
        ],
        axis=1,
    )
    body_rows = capacity * strip_rows
    convolved = convolve_all(exposures, kernel_coeffs)
    tiles = jnp.concatenate(
        [
            usable.reshape(strip_total, strip_rows * columns),
            (usable * convolved).reshape(strip_total, strip_rows * columns),
        ],
        axis=1,
    )
    packed = jnp.dot(chooser, tiles, precision=largest_value).reshape(
        devices, 2 * body_rows, columns
    )
    payload = jnp.concatenate([packed, meta], axis=1)
    received = [payload[0]]
    for shift in range(1, devices):
        pairs = [(i, (i + shift) % devices) for i in range(devices)]
        received.append(lax.ppermute(payload[shift], "patch", pairs))
    got_meta = jnp.stack([chunk[2 * body_rows :, :] for chunk in received], axis=0)
    slot_rows = got_meta[:, 0, :capacity].reshape(slot_total).astype(jnp.int32)
    slot_cols = got_meta[:, 1, :capacity].reshape(slot_total).astype(jnp.int32)
    slot_visit = got_meta[:, 2, :capacity].reshape(slot_total).astype(jnp.int32)
    index = jnp.concatenate(
        [
            slot_cols // columns,
            slot_cols % columns,
            (slot_rows // strip_rows) * strip_rows,
            slot_rows % strip_rows,
            slot_visit,
        ]
    )
    coadd_image, weight_map = place([payload] + received[1:], index, PH, PW)
    return (coadd_image[None], weight_map[None])


def solution(mesh):
    return jax.shard_map(
        shards,
        mesh=mesh,
        in_specs=(
            P(("band", "patch"), None, None),
            P(("band", "patch"), None, None),
            P(("band", "patch"), None, None),
            P(("band", "patch"), None, None),
            P(("band", "patch"), None),
            P(("band", "patch"), None),
            P(("band", "patch")),
            P(("band", "patch")),
        ),
        out_specs=(P(("band", "patch"), None, None), P(("band", "patch"), None, None)),
        check_vma=False,
    )
```

```python
import jax
import numpy as np
import jax.numpy as jnp
from jax import lax
from jax.experimental import pallas as pl
from jax.experimental.pallas import tpu as pltpu
from jax.sharding import PartitionSpec as P


PH = 128
PW = 512
KS = 21
VISITS = 8


gauss_widths = (0.75, 1.5, 3.0)
largest_value = lax.Precision.HIGHEST
mxu_value = lax.Precision.HIGH


def tap_table(kernel_half_width):
    support = np.arange(-kernel_half_width, kernel_half_width + 1).astype(np.float64)
    tables = []
    for spread in gauss_widths:
        s32 = float(np.float32(spread))
        gauss_total = np.sum(np.exp(-support * support / (2.0 * s32 * s32)))
        profile = np.exp(-support * support / (2.0 * s32 * s32)) / gauss_total
        scaled = support / s32
        tables.append(np.stack([profile, profile * scaled, profile * scaled * scaled]))
    return np.stack(tables)


def row_blocks(block_rows, window_rows, kernel_half_width, lead):
    taps = tap_table(kernel_half_width).reshape(9, 2 * kernel_half_width + 1)
    out = np.zeros((9, block_rows, window_rows), np.float64)
    for i in range(block_rows):
        start = lead + i - kernel_half_width
        out[:, i, start : start + 2 * kernel_half_width + 1] = taps
    return out.astype(np.float32)


def column_ops(column_count, kernel_half_width):
    taps = tap_table(kernel_half_width)
    out = np.zeros((3, 3, column_count, column_count), np.float64)
    for y in range(column_count):
        lo = max(0, y - kernel_half_width)
        hi = min(column_count, y + kernel_half_width + 1)
        for x in range(lo, hi):
            out[:, :, y, x] = taps[:, :, y - x + kernel_half_width]
    return out.astype(np.float32)


def convolve_all(exposures, kernel_coeffs):
    kernel_half_width = KS // 2
    n, height, columns = exposures.shape
    block = 8
    blocks = height // block
    lead = -(-kernel_half_width // block) * block
    reach = -(-(lead + kernel_half_width + block) // block)
    total_rows = (blocks + reach - 1) * block
    padded = jnp.pad(
        exposures, ((0, 0), (lead, total_rows - height - lead), (0, 0))
    ).reshape(n, blocks + reach - 1, block, columns)
    windows = jnp.concatenate([padded[:, j : j + blocks] for j in range(reach)], axis=2)
    rows = jnp.asarray(row_blocks(block, reach * block, kernel_half_width, lead))
    smooth = jnp.einsum("kit,nqtx->nqkix", rows, windows, precision=mxu_value)
    x_np = 2.0 * np.arange(columns, dtype=np.float32) / np.float32(columns - 1) - 1.0
    basis = np.zeros((6, 3, columns), np.float32)
    basis[0, 0] = 1.0
    basis[1, 0] = x_np
    basis[3, 0] = x_np * x_np
    basis[2, 1] = 1.0
    basis[4, 1] = x_np
    basis[5, 2] = 1.0
    fx = jnp.dot(
        kernel_coeffs.reshape(n * 27, 6), jnp.asarray(basis.reshape(6, 3 * columns)),
        precision=largest_value,
    ).reshape(n, 3, 3, 3, 3, columns)
    col_t = jnp.asarray(np.swapaxes(column_ops(columns, kernel_half_width), 2, 3))
    mixed = (
        col_t[None, :, None, 0, None, :, :] * fx[:, :, :, 0, :, :, None]
        + col_t[None, :, None, 1, None, :, :] * fx[:, :, :, 1, :, :, None]
        + col_t[None, :, None, 2, None, :, :] * fx[:, :, :, 2, :, :, None]
    )
    mixed = mixed.reshape(n, 9, 3 * columns, columns)
    fields = jnp.einsum("nqkiy,nkzy->nqiz", smooth, mixed, precision=mxu_value)
    fields = fields.reshape(n, height, 3 * columns)
    y_line = (2.0 * jnp.arange(height).astype(jnp.float32) / (height - 1) - 1.0)[None, :, None]
    return (
        fields[:, :, :columns]
        + y_line * fields[:, :, columns : 2 * columns]
        + (y_line * y_line) * fields[:, :, 2 * columns :]
    )


def place_kernel(index_ref, *refs):
    chunks = refs[:-4]
    coadd_ref, wmap_ref, acc, table = refs[-4:]
    senders = len(chunks)
    slots = index_ref.shape[0] // 5
    capacity = slots // senders
    strip_rows = 8
    lanes = chunks[0].shape[-1]
    sums_at = capacity * 2 * strip_rows
    sums = None
    for chunk in chunks:
        if len(chunk.shape) == 3:
            block = chunk[0, pl.ds(sums_at, strip_rows), :]
        else:
            block = chunk[pl.ds(sums_at, strip_rows), :]
        sums = block if sums is None else sums + block
    visit_weight = (sums[3:4, :] + 1.0) / (sums[4:5, :] + 1.0)
    lane_row = lax.broadcasted_iota(jnp.int32, (1, lanes), 1)
    for visit in range(VISITS):
        picked = jnp.sum(jnp.where(lane_row == visit, visit_weight, 0.0), axis=1, keepdims=True)
        table[visit] = jnp.broadcast_to(picked, (strip_rows, lanes))
    lane_blocks = acc.shape[0] - 1
    out_rows = coadd_ref.shape[0]
    acc[...] = jnp.zeros(acc.shape, jnp.float32)
    lane = lax.broadcasted_iota(jnp.int32, (strip_rows, 2 * lanes), 1) % lanes
    sub = lax.broadcasted_iota(jnp.int32, (strip_rows, 2 * lanes), 0)

    for d, chunk in enumerate(chunks):

        def body(j, carry, chunk=chunk, d=d):
            s = d * capacity + j
            q = index_ref[s]
            rem = index_ref[slots + s]
            top = pl.multiple_of(index_ref[2 * slots + s], strip_rows)
            rr = index_ref[3 * slots + s]
            wt = table[index_ref[4 * slots + s]]
            wt = jnp.concatenate([wt, wt], axis=1)
            lane_lo = lane >= rem
            sub_lo = sub >= rr
            nxt = pl.multiple_of(top + strip_rows, strip_rows)
            halves = []
            for part in (0, 1):
                at = pl.multiple_of(j * (2 * strip_rows) + part * strip_rows, strip_rows)
                if len(chunk.shape) == 3:
                    v = chunk[0, pl.ds(at, strip_rows), :]
                else:
                    v = chunk[pl.ds(at, strip_rows), :]
                halves.append(pltpu.roll(v, rem, 1))
            v = jnp.concatenate(halves, axis=1) * wt
            v = pltpu.roll(v, rr, 0)
            zero = jnp.zeros_like(v)
            a = jnp.where(sub_lo, v, zero)
            b = v - a
            acc[q, pl.ds(top, strip_rows), :] += jnp.where(lane_lo, a, zero)
            acc[q + 1, pl.ds(top, strip_rows), :] += jnp.where(lane_lo, zero, a)
            acc[q, pl.ds(nxt, strip_rows), :] += jnp.where(lane_lo, b, zero)
            acc[q + 1, pl.ds(nxt, strip_rows), :] += jnp.where(lane_lo, zero, b)
            return carry

        lax.fori_loop(0, capacity, body, 0, unroll=min(8, capacity))
    for j in range(lane_blocks):
        w = acc[j, pl.ds(0, out_rows), pl.ds(0, lanes)]
        n = acc[j, pl.ds(0, out_rows), pl.ds(lanes, lanes)]
        wmap_ref[:, pl.ds(j * lanes, lanes)] = w
        coadd_ref[:, pl.ds(j * lanes, lanes)] = n / jnp.maximum(w, 1.0)


def place(chunks, index, patch_rows, patch_cols):
    lanes = chunks[0].shape[-1]
    strip_rows = 8
    lane_blocks = patch_cols // lanes
    smem = pltpu.SMEM
    return pl.pallas_call(
        place_kernel,
        out_shape=(
            jax.ShapeDtypeStruct((patch_rows, patch_cols), jnp.float32),
            jax.ShapeDtypeStruct((patch_rows, patch_cols), jnp.float32),
        ),
        in_specs=[pl.BlockSpec(memory_space=smem)]
        + [pl.BlockSpec(memory_space=pltpu.VMEM)] * len(chunks),
        out_specs=(pl.BlockSpec(memory_space=pltpu.VMEM), pl.BlockSpec(memory_space=pltpu.VMEM)),
        scratch_shapes=[
            pltpu.VMEM((lane_blocks + 1, patch_rows + strip_rows, 2 * lanes), jnp.float32),
            pltpu.VMEM((VISITS, strip_rows, lanes), jnp.float32),
        ],
    )(index, *chunks)


def shards(
    exposures, variance, mask_bits, kernel_coeffs, ccd_visit, strip_patch, strip_row, strip_col
):
    ccd_count, height, columns = exposures.shape
    strip_total = strip_patch.shape[0]
    per_ccd = strip_total // ccd_count
    strip_rows = height // per_ccd
    devices = lax.axis_size("patch")
    capacity = 2 * strip_total // devices
    usable = (jnp.bitwise_and(mask_bits, 3) != 3).astype(jnp.float32)
    visit_hot = (ccd_visit == jnp.arange(VISITS)[None, :]).astype(jnp.float32)
    local_count = jnp.sum(jnp.sum(usable, axis=(1, 2))[:, None] * visit_hot, axis=0)
    local_load = jnp.sum(jnp.sum(usable * variance, axis=(1, 2))[:, None] * visit_hot, axis=0)

    destination = strip_patch[:, 0]
    strip_ids = jnp.arange(strip_total)
    earlier = strip_ids[None, :] < strip_ids[:, None]
    same_target = destination[None, :] == destination[:, None]
    slot_rank = jnp.sum(jnp.logical_and(earlier, same_target).astype(jnp.int32), axis=1)
    me = lax.axis_index("patch")
    slot_index = ((destination - me) % devices) * capacity + slot_rank
    slot_total = devices * capacity
    chooser = (slot_index[None, :] == jnp.arange(slot_total)[:, None]).astype(jnp.float32)

    strip_visit = jnp.repeat(ccd_visit[:, 0], per_ccd)
    placement = jnp.stack([strip_row, strip_col, strip_visit], axis=1).astype(jnp.float32)
    slot_meta = jnp.dot(chooser, placement, precision=largest_value).reshape(devices, capacity, 3)
    meta = jnp.concatenate(
        [
            jnp.pad(jnp.swapaxes(slot_meta, 1, 2), ((0, 0), (0, 0), (0, columns - capacity))),
            jnp.broadcast_to(
                jnp.pad(
                    jnp.stack([local_count, local_load])[None],
                    ((0, 0), (0, 3), (0, columns - VISITS)),
                ),
                (devices, 5, columns),
            ),
        ],
        axis=1,
    )
    body_rows = capacity * strip_rows
    convolved = convolve_all(exposures, kernel_coeffs)
    tiles = jnp.concatenate(
        [
            usable.reshape(strip_total, strip_rows * columns),
            (usable * convolved).reshape(strip_total, strip_rows * columns),
        ],
        axis=1,
    )
    packed = jnp.dot(chooser, tiles, precision=largest_value).reshape(
        devices, 2 * body_rows, columns
    )
    payload = jnp.concatenate([packed, meta], axis=1)
    received = [payload[0]]
    for shift in range(1, devices):
        pairs = [(i, (i + shift) % devices) for i in range(devices)]
        received.append(lax.ppermute(payload[shift], "patch", pairs))
    got_meta = jnp.stack([chunk[2 * body_rows :, :] for chunk in received], axis=0)
    slot_rows = got_meta[:, 0, :capacity].reshape(slot_total).astype(jnp.int32)
    slot_cols = got_meta[:, 1, :capacity].reshape(slot_total).astype(jnp.int32)
    slot_visit = got_meta[:, 2, :capacity].reshape(slot_total).astype(jnp.int32)
    index = jnp.concatenate(
        [
            slot_cols // columns,
            slot_cols % columns,
            (slot_rows // strip_rows) * strip_rows,
            slot_rows % strip_rows,
            slot_visit,
        ]
    )
    coadd_image, weight_map = place([payload] + received[1:], index, PH, PW)
    return (coadd_image[None], weight_map[None])


def solution(mesh):
    return jax.shard_map(
        shards,
        mesh=mesh,
        in_specs=(
            P(("band", "patch"), None, None),
            P(("band", "patch"), None, None),
            P(("band", "patch"), None, None),
            P(("band", "patch"), None, None),
            P(("band", "patch"), None),
            P(("band", "patch"), None),
            P(("band", "patch")),
            P(("band", "patch")),
        ),
        out_specs=(P(("band", "patch"), None, None), P(("band", "patch"), None, None)),
        check_vma=False,
    )
```

```python
import jax
import numpy as np
import jax.numpy as jnp
from jax import lax
from jax.experimental import pallas as pl
from jax.experimental.pallas import tpu as pltpu
from jax.sharding import PartitionSpec as P


PH = 128
PW = 512
KS = 21
VISITS = 8


gauss_widths = (0.75, 1.5, 3.0)
largest_value = lax.Precision.HIGHEST
mxu_value = lax.Precision.HIGH


def tap_table(kernel_half_width):
    support = np.arange(-kernel_half_width, kernel_half_width + 1).astype(np.float64)
    tables = []
    for spread in gauss_widths:
        s32 = float(np.float32(spread))
        gauss_total = np.sum(np.exp(-support * support / (2.0 * s32 * s32)))
        profile = np.exp(-support * support / (2.0 * s32 * s32)) / gauss_total
        scaled = support / s32
        tables.append(np.stack([profile, profile * scaled, profile * scaled * scaled]))
    return np.stack(tables)


def row_blocks(block_rows, window_rows, kernel_half_width, lead):
    taps = tap_table(kernel_half_width).reshape(9, 2 * kernel_half_width + 1)
    out = np.zeros((9, block_rows, window_rows), np.float64)
    for i in range(block_rows):
        start = lead + i - kernel_half_width
        out[:, i, start : start + 2 * kernel_half_width + 1] = taps
    return out.astype(np.float32)


def column_ops(column_count, kernel_half_width):
    taps = tap_table(kernel_half_width)
    out = np.zeros((3, 3, column_count, column_count), np.float64)
    for y in range(column_count):
        lo = max(0, y - kernel_half_width)
        hi = min(column_count, y + kernel_half_width + 1)
        for x in range(lo, hi):
            out[:, :, y, x] = taps[:, :, y - x + kernel_half_width]
    return out.astype(np.float32)


def convolve_all(exposures, kernel_coeffs):
    kernel_half_width = KS // 2
    n, height, columns = exposures.shape
    block = 8
    blocks = height // block
    lead = -(-kernel_half_width // block) * block
    reach = -(-(lead + kernel_half_width + block) // block)
    total_rows = (blocks + reach - 1) * block
    padded = jnp.pad(
        exposures, ((0, 0), (lead, total_rows - height - lead), (0, 0))
    ).reshape(n, blocks + reach - 1, block, columns)
    windows = jnp.concatenate([padded[:, j : j + blocks] for j in range(reach)], axis=2)
    rows = jnp.asarray(row_blocks(block, reach * block, kernel_half_width, lead))
    smooth = jnp.einsum("kit,nqtx->nqkix", rows, windows, precision=mxu_value)
    x_np = 2.0 * np.arange(columns, dtype=np.float32) / np.float32(columns - 1) - 1.0
    basis = np.zeros((6, 3, columns), np.float32)
    basis[0, 0] = 1.0
    basis[1, 0] = x_np
    basis[3, 0] = x_np * x_np
    basis[2, 1] = 1.0
    basis[4, 1] = x_np
    basis[5, 2] = 1.0
    fx = jnp.dot(
        kernel_coeffs.reshape(n * 27, 6), jnp.asarray(basis.reshape(6, 3 * columns)),
        precision=largest_value,
    ).reshape(n, 3, 3, 3, 3, columns)
    col_t = jnp.asarray(np.swapaxes(column_ops(columns, kernel_half_width), 2, 3))
    mixed = (
        col_t[None, :, None, 0, None, :, :] * fx[:, :, :, 0, :, :, None]
        + col_t[None, :, None, 1, None, :, :] * fx[:, :, :, 1, :, :, None]
        + col_t[None, :, None, 2, None, :, :] * fx[:, :, :, 2, :, :, None]
    )
    mixed = mixed.reshape(n, 9, 3 * columns, columns)
    fields = jnp.einsum("nqkiy,nkzy->nqiz", smooth, mixed, precision=mxu_value)
    fields = fields.reshape(n, height, 3 * columns)
    y_line = (2.0 * jnp.arange(height).astype(jnp.float32) / (height - 1) - 1.0)[None, :, None]
    return (
        fields[:, :, :columns]
        + y_line * fields[:, :, columns : 2 * columns]
        + (y_line * y_line) * fields[:, :, 2 * columns :]
    )


def place_kernel(index_ref, *refs):
    chunks = refs[:-5]
    coadd_ref, wmap_ref, acc_n, acc_w, table = refs[-5:]
    senders = len(chunks)
    slots = index_ref.shape[0] // 5
    capacity = slots // senders
    strip_rows = 8
    lanes = chunks[0].shape[-1]
    sums_at = capacity * 2 * strip_rows
    sums = None
    for chunk in chunks:
        if len(chunk.shape) == 3:
            block = chunk[0, pl.ds(sums_at, strip_rows), :]
        else:
            block = chunk[pl.ds(sums_at, strip_rows), :]
        sums = block if sums is None else sums + block
    visit_weight = (sums[3:4, :] + 1.0) / (sums[4:5, :] + 1.0)
    lane_row = lax.broadcasted_iota(jnp.int32, (1, lanes), 1)
    for visit in range(VISITS):
        picked = jnp.sum(jnp.where(lane_row == visit, visit_weight, 0.0), axis=1, keepdims=True)
        table[visit] = jnp.broadcast_to(picked, (strip_rows, lanes))
    lane_blocks = acc_n.shape[0] - 1
    out_rows = coadd_ref.shape[0]
    acc_n[...] = jnp.zeros(acc_n.shape, jnp.float32)
    acc_w[...] = jnp.zeros(acc_w.shape, jnp.float32)
    lane = lax.broadcasted_iota(jnp.int32, (strip_rows, lanes), 1)
    sub = lax.broadcasted_iota(jnp.int32, (strip_rows, lanes), 0)

    for d, chunk in enumerate(chunks):

        def body(j, carry, chunk=chunk, d=d):
            s = d * capacity + j
            q = index_ref[s]
            rem = index_ref[slots + s]
            top = pl.multiple_of(index_ref[2 * slots + s], strip_rows)
            rr = index_ref[3 * slots + s]
            wt = table[index_ref[4 * slots + s]]
            lane_lo = lane >= rem
            sub_lo = sub >= rr
            nxt = pl.multiple_of(top + strip_rows, strip_rows)
            for part, acc in ((1, acc_n), (0, acc_w)):
                at = pl.multiple_of(j * (2 * strip_rows) + part * strip_rows, strip_rows)
                if len(chunk.shape) == 3:
                    v = chunk[0, pl.ds(at, strip_rows), :] * wt
                else:
                    v = chunk[pl.ds(at, strip_rows), :] * wt
                v = pltpu.roll(v, rem, 1)
                v = pltpu.roll(v, rr, 0)
                zero = jnp.zeros_like(v)
                a = jnp.where(sub_lo, v, zero)
                b = v - a
                acc[q, pl.ds(top, strip_rows), :] += jnp.where(lane_lo, a, zero)
                acc[q + 1, pl.ds(top, strip_rows), :] += jnp.where(lane_lo, zero, a)
                acc[q, pl.ds(nxt, strip_rows), :] += jnp.where(lane_lo, b, zero)
                acc[q + 1, pl.ds(nxt, strip_rows), :] += jnp.where(lane_lo, zero, b)
            return carry

        lax.fori_loop(0, capacity, body, 0, unroll=min(16, capacity))
    for j in range(lane_blocks):
        n = acc_n[j, pl.ds(0, out_rows), :]
        w = acc_w[j, pl.ds(0, out_rows), :]
        wmap_ref[:, pl.ds(j * lanes, lanes)] = w
        coadd_ref[:, pl.ds(j * lanes, lanes)] = n / jnp.maximum(w, 1.0)


def place(chunks, index, patch_rows, patch_cols):
    lanes = chunks[0].shape[-1]
    strip_rows = 8
    lane_blocks = patch_cols // lanes
    smem = pltpu.SMEM
    return pl.pallas_call(
        place_kernel,
        out_shape=(
            jax.ShapeDtypeStruct((patch_rows, patch_cols), jnp.float32),
            jax.ShapeDtypeStruct((patch_rows, patch_cols), jnp.float32),
        ),
        in_specs=[pl.BlockSpec(memory_space=smem)]
        + [pl.BlockSpec(memory_space=pltpu.VMEM)] * len(chunks),
        out_specs=(pl.BlockSpec(memory_space=pltpu.VMEM), pl.BlockSpec(memory_space=pltpu.VMEM)),
        scratch_shapes=[
            pltpu.VMEM((lane_blocks + 1, patch_rows + strip_rows, lanes), jnp.float32),
            pltpu.VMEM((lane_blocks + 1, patch_rows + strip_rows, lanes), jnp.float32),
            pltpu.VMEM((VISITS, strip_rows, lanes), jnp.float32),
        ],
    )(index, *chunks)


def shards(
    exposures, variance, mask_bits, kernel_coeffs, ccd_visit, strip_patch, strip_row, strip_col
):
    ccd_count, height, columns = exposures.shape
    strip_total = strip_patch.shape[0]
    per_ccd = strip_total // ccd_count
    strip_rows = height // per_ccd
    devices = lax.axis_size("patch")
    capacity = 2 * strip_total // devices
    usable = (jnp.bitwise_and(mask_bits, 3) != 3).astype(jnp.float32)
    visit_hot = (ccd_visit == jnp.arange(VISITS)[None, :]).astype(jnp.float32)
    local_count = jnp.sum(jnp.sum(usable, axis=(1, 2))[:, None] * visit_hot, axis=0)
    local_load = jnp.sum(jnp.sum(usable * variance, axis=(1, 2))[:, None] * visit_hot, axis=0)

    destination = strip_patch[:, 0]
    strip_ids = jnp.arange(strip_total)
    earlier = strip_ids[None, :] < strip_ids[:, None]
    same_target = destination[None, :] == destination[:, None]
    slot_rank = jnp.sum(jnp.logical_and(earlier, same_target).astype(jnp.int32), axis=1)
    me = lax.axis_index("patch")
    slot_index = ((destination - me) % devices) * capacity + slot_rank
    slot_total = devices * capacity
    chooser = (slot_index[None, :] == jnp.arange(slot_total)[:, None]).astype(jnp.float32)

    strip_visit = jnp.repeat(ccd_visit[:, 0], per_ccd)
    placement = jnp.stack([strip_row, strip_col, strip_visit], axis=1).astype(jnp.float32)
    slot_meta = jnp.dot(chooser, placement, precision=largest_value).reshape(devices, capacity, 3)
    meta = jnp.concatenate(
        [
            jnp.pad(jnp.swapaxes(slot_meta, 1, 2), ((0, 0), (0, 0), (0, columns - capacity))),
            jnp.broadcast_to(
                jnp.pad(
                    jnp.stack([local_count, local_load])[None],
                    ((0, 0), (0, 3), (0, columns - VISITS)),
                ),
                (devices, 5, columns),
            ),
        ],
        axis=1,
    )
    body_rows = capacity * strip_rows
    convolved = convolve_all(exposures, kernel_coeffs)
    tiles = jnp.concatenate(
        [
            usable.reshape(strip_total, strip_rows * columns),
            (usable * convolved).reshape(strip_total, strip_rows * columns),
        ],
        axis=1,
    )
    packed = jnp.dot(chooser, tiles, precision=largest_value).reshape(
        devices, 2 * body_rows, columns
    )
    payload = jnp.concatenate([packed, meta], axis=1)
    received = [payload[0]]
    for shift in range(1, devices):
        pairs = [(i, (i + shift) % devices) for i in range(devices)]
        received.append(lax.ppermute(payload[shift], "patch", pairs))
    got_meta = jnp.stack([chunk[2 * body_rows :, :] for chunk in received], axis=0)
    slot_rows = got_meta[:, 0, :capacity].reshape(slot_total).astype(jnp.int32)
    slot_cols = got_meta[:, 1, :capacity].reshape(slot_total).astype(jnp.int32)
    slot_visit = got_meta[:, 2, :capacity].reshape(slot_total).astype(jnp.int32)
    index = jnp.concatenate(
        [
            slot_cols // columns,
            slot_cols % columns,
            (slot_rows // strip_rows) * strip_rows,
            slot_rows % strip_rows,
            slot_visit,
        ]
    )
    coadd_image, weight_map = place([payload] + received[1:], index, PH, PW)
    return (coadd_image[None], weight_map[None])


def solution(mesh):
    return jax.shard_map(
        shards,
        mesh=mesh,
        in_specs=(
            P(("band", "patch"), None, None),
            P(("band", "patch"), None, None),
            P(("band", "patch"), None, None),
            P(("band", "patch"), None, None),
            P(("band", "patch"), None),
            P(("band", "patch"), None),
            P(("band", "patch")),
            P(("band", "patch")),
        ),
        out_specs=(P(("band", "patch"), None, None), P(("band", "patch"), None, None)),
        check_vma=False,
    )
```

```python
import jax
import numpy as np
import jax.numpy as jnp
from jax import lax
from jax.experimental import pallas as pl
from jax.experimental.pallas import tpu as pltpu
from jax.sharding import PartitionSpec as P


PH = 128
PW = 512
KS = 21
VISITS = 8
ACC_SETS = 2


gauss_widths = (0.75, 1.5, 3.0)
largest_value = lax.Precision.HIGHEST
mxu_value = lax.Precision.HIGH


def tap_table(kernel_half_width):
    support = np.arange(-kernel_half_width, kernel_half_width + 1).astype(np.float64)
    tables = []
    for spread in gauss_widths:
        s32 = float(np.float32(spread))
        gauss_total = np.sum(np.exp(-support * support / (2.0 * s32 * s32)))
        profile = np.exp(-support * support / (2.0 * s32 * s32)) / gauss_total
        scaled = support / s32
        tables.append(np.stack([profile, profile * scaled, profile * scaled * scaled]))
    return np.stack(tables)


def row_blocks(block_rows, window_rows, kernel_half_width, lead):
    taps = tap_table(kernel_half_width).reshape(9, 2 * kernel_half_width + 1)
    out = np.zeros((9, block_rows, window_rows), np.float64)
    for i in range(block_rows):
        start = lead + i - kernel_half_width
        out[:, i, start : start + 2 * kernel_half_width + 1] = taps
    return out.astype(np.float32)


def column_ops(column_count, kernel_half_width):
    taps = tap_table(kernel_half_width)
    out = np.zeros((3, 3, column_count, column_count), np.float64)
    for y in range(column_count):
        lo = max(0, y - kernel_half_width)
        hi = min(column_count, y + kernel_half_width + 1)
        for x in range(lo, hi):
            out[:, :, y, x] = taps[:, :, y - x + kernel_half_width]
    return out.astype(np.float32)


def convolve_all(exposures, kernel_coeffs):
    kernel_half_width = KS // 2
    n, height, columns = exposures.shape
    block = 8
    blocks = height // block
    lead = -(-kernel_half_width // block) * block
    reach = -(-(lead + kernel_half_width + block) // block)
    total_rows = (blocks + reach - 1) * block
    padded = jnp.pad(
        exposures, ((0, 0), (lead, total_rows - height - lead), (0, 0))
    ).reshape(n, blocks + reach - 1, block, columns)
    windows = jnp.concatenate([padded[:, j : j + blocks] for j in range(reach)], axis=2)
    rows = jnp.asarray(row_blocks(block, reach * block, kernel_half_width, lead))
    smooth = jnp.einsum("kit,nqtx->nqkix", rows, windows, precision=mxu_value)
    x_np = 2.0 * np.arange(columns, dtype=np.float32) / np.float32(columns - 1) - 1.0
    basis = np.zeros((6, 3, columns), np.float32)
    basis[0, 0] = 1.0
    basis[1, 0] = x_np
    basis[3, 0] = x_np * x_np
    basis[2, 1] = 1.0
    basis[4, 1] = x_np
    basis[5, 2] = 1.0
    fx = jnp.dot(
        kernel_coeffs.reshape(n * 27, 6), jnp.asarray(basis.reshape(6, 3 * columns)),
        precision=largest_value,
    ).reshape(n, 3, 3, 3, 3, columns)
    col_t = jnp.asarray(np.swapaxes(column_ops(columns, kernel_half_width), 2, 3))
    mixed = (
        col_t[None, :, None, 0, None, :, :] * fx[:, :, :, 0, :, :, None]
        + col_t[None, :, None, 1, None, :, :] * fx[:, :, :, 1, :, :, None]
        + col_t[None, :, None, 2, None, :, :] * fx[:, :, :, 2, :, :, None]
    )
    mixed = mixed.reshape(n, 9, 3 * columns, columns)
    fields = jnp.einsum("nqkiy,nkzy->nqiz", smooth, mixed, precision=mxu_value)
    fields = fields.reshape(n, height, 3 * columns)
    y_line = (2.0 * jnp.arange(height).astype(jnp.float32) / (height - 1) - 1.0)[None, :, None]
    return (
        fields[:, :, :columns]
        + y_line * fields[:, :, columns : 2 * columns]
        + (y_line * y_line) * fields[:, :, 2 * columns :]
    )


def place_kernel(index_ref, *refs):
    chunks = refs[: -3 - 2 * ACC_SETS]
    coadd_ref, wmap_ref = refs[-3 - 2 * ACC_SETS : -1 - 2 * ACC_SETS]
    accs_n = refs[-1 - 2 * ACC_SETS : -1 - ACC_SETS]
    accs_w = refs[-1 - ACC_SETS : -1]
    table = refs[-1]
    senders = len(chunks)
    slots = index_ref.shape[0] // 5
    capacity = slots // senders
    strip_rows = 8
    lanes = chunks[0].shape[-1]
    sums_at = capacity * 2 * strip_rows
    sums = None
    for chunk in chunks:
        if len(chunk.shape) == 3:
            block = chunk[0, pl.ds(sums_at, strip_rows), :]
        else:
            block = chunk[pl.ds(sums_at, strip_rows), :]
        sums = block if sums is None else sums + block
    visit_weight = (sums[3:4, :] + 1.0) / (sums[4:5, :] + 1.0)
    lane_row = lax.broadcasted_iota(jnp.int32, (1, lanes), 1)
    for visit in range(VISITS):
        picked = jnp.sum(jnp.where(lane_row == visit, visit_weight, 0.0), axis=1, keepdims=True)
        table[visit] = jnp.broadcast_to(picked, (strip_rows, lanes))
    lane_blocks = accs_n[0].shape[0] - 1
    ways = min(ACC_SETS, capacity)
    out_rows = coadd_ref.shape[0]
    for acc in accs_n + accs_w:
        acc[...] = jnp.zeros(acc.shape, jnp.float32)
    lane = lax.broadcasted_iota(jnp.int32, (strip_rows, lanes), 1)
    sub = lax.broadcasted_iota(jnp.int32, (strip_rows, lanes), 0)

    for d, chunk in enumerate(chunks):

        def body(jj, carry, chunk=chunk, d=d):
          for t in range(ways):
            j = jj * ways + t
            acc_n = accs_n[t]
            acc_w = accs_w[t]
            s = d * capacity + j
            q = index_ref[s]
            rem = index_ref[slots + s]
            top = pl.multiple_of(index_ref[2 * slots + s], strip_rows)
            rr = index_ref[3 * slots + s]
            wt = table[index_ref[4 * slots + s]]
            lane_lo = lane >= rem
            sub_lo = sub >= rr
            nxt = pl.multiple_of(top + strip_rows, strip_rows)
            for part, acc in ((1, acc_n), (0, acc_w)):
                at = pl.multiple_of(j * (2 * strip_rows) + part * strip_rows, strip_rows)
                if len(chunk.shape) == 3:
                    v = chunk[0, pl.ds(at, strip_rows), :] * wt
                else:
                    v = chunk[pl.ds(at, strip_rows), :] * wt
                v = pltpu.roll(v, rem, 1)
                v = pltpu.roll(v, rr, 0)
                zero = jnp.zeros_like(v)
                a = jnp.where(sub_lo, v, zero)
                b = v - a
                acc[q, pl.ds(top, strip_rows), :] += jnp.where(lane_lo, a, zero)
                acc[q + 1, pl.ds(top, strip_rows), :] += jnp.where(lane_lo, zero, a)
                acc[q, pl.ds(nxt, strip_rows), :] += jnp.where(lane_lo, b, zero)
                acc[q + 1, pl.ds(nxt, strip_rows), :] += jnp.where(lane_lo, zero, b)
          return carry

        lax.fori_loop(0, capacity // ways, body, 0, unroll=capacity // ways)
    for j in range(lane_blocks):
        n = accs_n[0][j, pl.ds(0, out_rows), :]
        w = accs_w[0][j, pl.ds(0, out_rows), :]
        for t in range(1, ways):
            n = n + accs_n[t][j, pl.ds(0, out_rows), :]
            w = w + accs_w[t][j, pl.ds(0, out_rows), :]
        wmap_ref[:, pl.ds(j * lanes, lanes)] = w
        coadd_ref[:, pl.ds(j * lanes, lanes)] = n / jnp.maximum(w, 1.0)


def place(chunks, index, patch_rows, patch_cols):
    lanes = chunks[0].shape[-1]
    strip_rows = 8
    lane_blocks = patch_cols // lanes
    smem = pltpu.SMEM
    return pl.pallas_call(
        place_kernel,
        out_shape=(
            jax.ShapeDtypeStruct((patch_rows, patch_cols), jnp.float32),
            jax.ShapeDtypeStruct((patch_rows, patch_cols), jnp.float32),
        ),
        in_specs=[pl.BlockSpec(memory_space=smem)]
        + [pl.BlockSpec(memory_space=pltpu.VMEM)] * len(chunks),
        out_specs=(pl.BlockSpec(memory_space=pltpu.VMEM), pl.BlockSpec(memory_space=pltpu.VMEM)),
        scratch_shapes=[
            *[pltpu.VMEM((lane_blocks + 1, patch_rows + strip_rows, lanes), jnp.float32)]
            * (2 * ACC_SETS),
            pltpu.VMEM((VISITS, strip_rows, lanes), jnp.float32),
        ],
    )(index, *chunks)


def shards(
    exposures, variance, mask_bits, kernel_coeffs, ccd_visit, strip_patch, strip_row, strip_col
):
    ccd_count, height, columns = exposures.shape
    strip_total = strip_patch.shape[0]
    per_ccd = strip_total // ccd_count
    strip_rows = height // per_ccd
    devices = lax.axis_size("patch")
    capacity = 2 * strip_total // devices
    usable = (jnp.bitwise_and(mask_bits, 3) != 3).astype(jnp.float32)
    visit_hot = (ccd_visit == jnp.arange(VISITS)[None, :]).astype(jnp.float32)
    local_count = jnp.sum(jnp.sum(usable, axis=(1, 2))[:, None] * visit_hot, axis=0)
    local_load = jnp.sum(jnp.sum(usable * variance, axis=(1, 2))[:, None] * visit_hot, axis=0)

    destination = strip_patch[:, 0]
    strip_ids = jnp.arange(strip_total)
    earlier = strip_ids[None, :] < strip_ids[:, None]
    same_target = destination[None, :] == destination[:, None]
    slot_rank = jnp.sum(jnp.logical_and(earlier, same_target).astype(jnp.int32), axis=1)
    me = lax.axis_index("patch")
    slot_index = ((destination - me) % devices) * capacity + slot_rank
    slot_total = devices * capacity
    chooser = (slot_index[None, :] == jnp.arange(slot_total)[:, None]).astype(jnp.float32)

    strip_visit = jnp.repeat(ccd_visit[:, 0], per_ccd)
    placement = jnp.stack([strip_row, strip_col, strip_visit], axis=1).astype(jnp.float32)
    slot_meta = jnp.dot(chooser, placement, precision=largest_value).reshape(devices, capacity, 3)
    meta = jnp.concatenate(
        [
            jnp.pad(jnp.swapaxes(slot_meta, 1, 2), ((0, 0), (0, 0), (0, columns - capacity))),
            jnp.broadcast_to(
                jnp.pad(
                    jnp.stack([local_count, local_load])[None],
                    ((0, 0), (0, 3), (0, columns - VISITS)),
                ),
                (devices, 5, columns),
            ),
        ],
        axis=1,
    )
    body_rows = capacity * strip_rows
    convolved = convolve_all(exposures, kernel_coeffs)
    tiles = jnp.concatenate(
        [
            usable.reshape(strip_total, strip_rows * columns),
            (usable * convolved).reshape(strip_total, strip_rows * columns),
        ],
        axis=1,
    )
    packed = jnp.dot(chooser, tiles, precision=largest_value).reshape(
        devices, 2 * body_rows, columns
    )
    payload = jnp.concatenate([packed, meta], axis=1)
    received = [payload[0]]
    for shift in range(1, devices):
        pairs = [(i, (i + shift) % devices) for i in range(devices)]
        received.append(lax.ppermute(payload[shift], "patch", pairs))
    got_meta = jnp.stack([chunk[2 * body_rows :, :] for chunk in received], axis=0)
    slot_rows = got_meta[:, 0, :capacity].reshape(slot_total).astype(jnp.int32)
    slot_cols = got_meta[:, 1, :capacity].reshape(slot_total).astype(jnp.int32)
    slot_visit = got_meta[:, 2, :capacity].reshape(slot_total).astype(jnp.int32)
    index = jnp.concatenate(
        [
            slot_cols // columns,
            slot_cols % columns,
            (slot_rows // strip_rows) * strip_rows,
            slot_rows % strip_rows,
            slot_visit,
        ]
    )
    coadd_image, weight_map = place([payload] + received[1:], index, PH, PW)
    return (coadd_image[None], weight_map[None])


def solution(mesh):
    return jax.shard_map(
        shards,
        mesh=mesh,
        in_specs=(
            P(("band", "patch"), None, None),
            P(("band", "patch"), None, None),
            P(("band", "patch"), None, None),
            P(("band", "patch"), None, None),
            P(("band", "patch"), None),
            P(("band", "patch"), None),
            P(("band", "patch")),
            P(("band", "patch")),
        ),
        out_specs=(P(("band", "patch"), None, None), P(("band", "patch"), None, None)),
        check_vma=False,
    )
```

```python
import jax
import numpy as np
import jax.numpy as jnp
from jax import lax
from jax.experimental import pallas as pl
from jax.experimental.pallas import tpu as pltpu
from jax.sharding import PartitionSpec as P


PH = 128
PW = 512
KS = 21
VISITS = 8


gauss_widths = (0.75, 1.5, 3.0)
largest_value = lax.Precision.HIGHEST
mxu_value = lax.Precision.HIGH


def tap_table(kernel_half_width):
    support = np.arange(-kernel_half_width, kernel_half_width + 1).astype(np.float64)
    tables = []
    for spread in gauss_widths:
        s32 = float(np.float32(spread))
        gauss_total = np.sum(np.exp(-support * support / (2.0 * s32 * s32)))
        profile = np.exp(-support * support / (2.0 * s32 * s32)) / gauss_total
        scaled = support / s32
        tables.append(np.stack([profile, profile * scaled, profile * scaled * scaled]))
    return np.stack(tables)


def row_blocks(block_rows, window_rows, kernel_half_width, lead):
    taps = tap_table(kernel_half_width).reshape(9, 2 * kernel_half_width + 1)
    out = np.zeros((9, block_rows, window_rows), np.float64)
    for i in range(block_rows):
        start = lead + i - kernel_half_width
        out[:, i, start : start + 2 * kernel_half_width + 1] = taps
    return out.astype(np.float32)


def column_ops(column_count, kernel_half_width):
    taps = tap_table(kernel_half_width)
    out = np.zeros((3, 3, column_count, column_count), np.float64)
    for y in range(column_count):
        lo = max(0, y - kernel_half_width)
        hi = min(column_count, y + kernel_half_width + 1)
        for x in range(lo, hi):
            out[:, :, y, x] = taps[:, :, y - x + kernel_half_width]
    return out.astype(np.float32)


def convolve_all(exposures, kernel_coeffs):
    kernel_half_width = KS // 2
    n, height, columns = exposures.shape
    block = 8
    blocks = height // block
    lead = -(-kernel_half_width // block) * block
    reach = -(-(lead + kernel_half_width + block) // block)
    total_rows = (blocks + reach - 1) * block
    padded = jnp.pad(
        exposures, ((0, 0), (lead, total_rows - height - lead), (0, 0))
    ).reshape(n, blocks + reach - 1, block, columns)
    windows = jnp.concatenate([padded[:, j : j + blocks] for j in range(reach)], axis=2)
    rows = jnp.asarray(row_blocks(block, reach * block, kernel_half_width, lead))
    smooth = jnp.einsum("kit,nqtx->nqkix", rows, windows, precision=mxu_value)
    x_np = 2.0 * np.arange(columns, dtype=np.float32) / np.float32(columns - 1) - 1.0
    basis = np.zeros((6, 3, columns), np.float32)
    basis[0, 0] = 1.0
    basis[1, 0] = x_np
    basis[3, 0] = x_np * x_np
    basis[2, 1] = 1.0
    basis[4, 1] = x_np
    basis[5, 2] = 1.0
    fx = jnp.dot(
        kernel_coeffs.reshape(n * 27, 6), jnp.asarray(basis.reshape(6, 3 * columns)),
        precision=largest_value,
    ).reshape(n, 3, 3, 3, 3, columns)
    col_t = jnp.asarray(np.swapaxes(column_ops(columns, kernel_half_width), 2, 3))
    mixed = (
        col_t[None, :, None, 0, None, :, :] * fx[:, :, :, 0, :, :, None]
        + col_t[None, :, None, 1, None, :, :] * fx[:, :, :, 1, :, :, None]
        + col_t[None, :, None, 2, None, :, :] * fx[:, :, :, 2, :, :, None]
    )
    mixed = mixed.reshape(n, 9, 3 * columns, columns)
    fields = jnp.einsum("nqkiy,nkzy->nqiz", smooth, mixed, precision=mxu_value)
    fields = fields.reshape(n, height, 3 * columns)
    y_line = (2.0 * jnp.arange(height).astype(jnp.float32) / (height - 1) - 1.0)[None, :, None]
    return (
        fields[:, :, :columns]
        + y_line * fields[:, :, columns : 2 * columns]
        + (y_line * y_line) * fields[:, :, 2 * columns :]
    )


def place_kernel(index_ref, *refs):
    chunks = refs[:-5]
    coadd_ref, wmap_ref, acc_n, acc_w, table = refs[-5:]
    senders = len(chunks)
    slots = index_ref.shape[0] // 5
    capacity = slots // senders
    strip_rows = 8
    lanes = chunks[0].shape[-1]
    sums_at = capacity * 2 * strip_rows
    sums = None
    for chunk in chunks:
        if len(chunk.shape) == 3:
            block = chunk[0, pl.ds(sums_at, strip_rows), :]
        else:
            block = chunk[pl.ds(sums_at, strip_rows), :]
        sums = block if sums is None else sums + block
    visit_weight = (sums[3:4, :] + 1.0) / (sums[4:5, :] + 1.0)
    lane_row = lax.broadcasted_iota(jnp.int32, (1, lanes), 1)
    for visit in range(VISITS):
        picked = jnp.sum(jnp.where(lane_row == visit, visit_weight, 0.0), axis=1, keepdims=True)
        table[visit] = jnp.broadcast_to(picked, (strip_rows, lanes))
    lane_blocks = acc_n.shape[0]
    out_rows = coadd_ref.shape[0]
    acc_n[...] = jnp.zeros(acc_n.shape, jnp.float32)
    acc_w[...] = jnp.zeros(acc_w.shape, jnp.float32)
    lane = lax.broadcasted_iota(jnp.int32, (strip_rows, lanes), 1)
    sub = lax.broadcasted_iota(jnp.int32, (strip_rows, lanes), 0)

    for d, chunk in enumerate(chunks):

        def body(j, carry, chunk=chunk, d=d):
            s = d * capacity + j
            q = index_ref[s]
            rem = index_ref[slots + s]
            top = pl.multiple_of(index_ref[2 * slots + s], strip_rows)
            rr = index_ref[3 * slots + s]
            wt = table[index_ref[4 * slots + s]]
            lane_lo = lane >= rem
            sub_lo = sub >= rr
            nxt = pl.multiple_of(jnp.minimum(top + strip_rows, out_rows - strip_rows), strip_rows)
            q1 = jnp.minimum(q + 1, lane_blocks - 1)
            for part, acc in ((1, acc_n), (0, acc_w)):
                at = pl.multiple_of(j * (2 * strip_rows) + part * strip_rows, strip_rows)
                if len(chunk.shape) == 3:
                    v = chunk[0, pl.ds(at, strip_rows), :] * wt
                else:
                    v = chunk[pl.ds(at, strip_rows), :] * wt
                v = pltpu.roll(v, rem, 1)
                v = pltpu.roll(v, rr, 0)
                zero = jnp.zeros_like(v)
                a = jnp.where(sub_lo, v, zero)
                b = v - a
                acc[q, pl.ds(top, strip_rows), :] += jnp.where(lane_lo, a, zero)
                acc[q1, pl.ds(top, strip_rows), :] += jnp.where(lane_lo, zero, a)
                acc[q, pl.ds(nxt, strip_rows), :] += jnp.where(lane_lo, b, zero)
                acc[q1, pl.ds(nxt, strip_rows), :] += jnp.where(lane_lo, zero, b)
            return carry

        lax.fori_loop(0, capacity, body, 0, unroll=min(16, capacity))
    for j in range(lane_blocks):
        n = acc_n[j, pl.ds(0, out_rows), :]
        w = acc_w[j, pl.ds(0, out_rows), :]
        wmap_ref[:, pl.ds(j * lanes, lanes)] = w
        coadd_ref[:, pl.ds(j * lanes, lanes)] = n / jnp.maximum(w, 1.0)


def place(chunks, index, patch_rows, patch_cols):
    lanes = chunks[0].shape[-1]
    strip_rows = 8
    lane_blocks = patch_cols // lanes
    smem = pltpu.SMEM
    return pl.pallas_call(
        place_kernel,
        out_shape=(
            jax.ShapeDtypeStruct((patch_rows, patch_cols), jnp.float32),
            jax.ShapeDtypeStruct((patch_rows, patch_cols), jnp.float32),
        ),
        in_specs=[pl.BlockSpec(memory_space=smem)]
        + [pl.BlockSpec(memory_space=pltpu.VMEM)] * len(chunks),
        out_specs=(pl.BlockSpec(memory_space=pltpu.VMEM), pl.BlockSpec(memory_space=pltpu.VMEM)),
        scratch_shapes=[
            pltpu.VMEM((lane_blocks, patch_rows, lanes), jnp.float32),
            pltpu.VMEM((lane_blocks, patch_rows, lanes), jnp.float32),
            pltpu.VMEM((VISITS, strip_rows, lanes), jnp.float32),
        ],
    )(index, *chunks)


def shards(
    exposures, variance, mask_bits, kernel_coeffs, ccd_visit, strip_patch, strip_row, strip_col
):
    ccd_count, height, columns = exposures.shape
    strip_total = strip_patch.shape[0]
    per_ccd = strip_total // ccd_count
    strip_rows = height // per_ccd
    devices = lax.axis_size("patch")
    capacity = 2 * strip_total // devices
    usable = (jnp.bitwise_and(mask_bits, 3) != 3).astype(jnp.float32)
    visit_hot = (ccd_visit == jnp.arange(VISITS)[None, :]).astype(jnp.float32)
    local_count = jnp.sum(jnp.sum(usable, axis=(1, 2))[:, None] * visit_hot, axis=0)
    local_load = jnp.sum(jnp.sum(usable * variance, axis=(1, 2))[:, None] * visit_hot, axis=0)

    destination = strip_patch[:, 0]
    strip_ids = jnp.arange(strip_total)
    earlier = strip_ids[None, :] < strip_ids[:, None]
    same_target = destination[None, :] == destination[:, None]
    slot_rank = jnp.sum(jnp.logical_and(earlier, same_target).astype(jnp.int32), axis=1)
    me = lax.axis_index("patch")
    slot_index = ((destination - me) % devices) * capacity + slot_rank
    slot_total = devices * capacity
    chooser = (slot_index[None, :] == jnp.arange(slot_total)[:, None]).astype(jnp.float32)

    strip_visit = jnp.repeat(ccd_visit[:, 0], per_ccd)
    placement = jnp.stack([strip_row, strip_col, strip_visit], axis=1).astype(jnp.float32)
    slot_meta = jnp.dot(chooser, placement, precision=largest_value).reshape(devices, capacity, 3)
    meta = jnp.concatenate(
        [
            jnp.pad(jnp.swapaxes(slot_meta, 1, 2), ((0, 0), (0, 0), (0, columns - capacity))),
            jnp.broadcast_to(
                jnp.pad(
                    jnp.stack([local_count, local_load])[None],
                    ((0, 0), (0, 3), (0, columns - VISITS)),
                ),
                (devices, 5, columns),
            ),
        ],
        axis=1,
    )
    body_rows = capacity * strip_rows
    convolved = convolve_all(exposures, kernel_coeffs)
    tiles = jnp.concatenate(
        [
            usable.reshape(strip_total, strip_rows * columns),
            (usable * convolved).reshape(strip_total, strip_rows * columns),
        ],
        axis=1,
    )
    packed = jnp.dot(chooser, tiles, precision=largest_value).reshape(
        devices, 2 * body_rows, columns
    )
    payload = jnp.concatenate([packed, meta], axis=1)
    received = [payload[0]]
    for shift in range(1, devices):
        pairs = [(i, (i + shift) % devices) for i in range(devices)]
        received.append(lax.ppermute(payload[shift], "patch", pairs))
    got_meta = jnp.stack([chunk[2 * body_rows :, :] for chunk in received], axis=0)
    slot_rows = got_meta[:, 0, :capacity].reshape(slot_total).astype(jnp.int32)
    slot_cols = got_meta[:, 1, :capacity].reshape(slot_total).astype(jnp.int32)
    slot_visit = got_meta[:, 2, :capacity].reshape(slot_total).astype(jnp.int32)
    index = jnp.concatenate(
        [
            slot_cols // columns,
            slot_cols % columns,
            (slot_rows // strip_rows) * strip_rows,
            slot_rows % strip_rows,
            slot_visit,
        ]
    )
    coadd_image, weight_map = place([payload] + received[1:], index, PH, PW)
    return (coadd_image[None], weight_map[None])


def solution(mesh):
    return jax.shard_map(
        shards,
        mesh=mesh,
        in_specs=(
            P(("band", "patch"), None, None),
            P(("band", "patch"), None, None),
            P(("band", "patch"), None, None),
            P(("band", "patch"), None, None),
            P(("band", "patch"), None),
            P(("band", "patch"), None),
            P(("band", "patch")),
            P(("band", "patch")),
        ),
        out_specs=(P(("band", "patch"), None, None), P(("band", "patch"), None, None)),
        check_vma=False,
    )
```

```python
import jax
import numpy as np
import jax.numpy as jnp
from jax import lax
from jax.experimental import pallas as pl
from jax.experimental.pallas import tpu as pltpu
from jax.sharding import PartitionSpec as P


PH = 128
PW = 512
KS = 21
VISITS = 8


gauss_widths = (0.75, 1.5, 3.0)
largest_value = lax.Precision.HIGHEST
mxu_value = lax.Precision.HIGH


def tap_table(kernel_half_width):
    support = np.arange(-kernel_half_width, kernel_half_width + 1).astype(np.float64)
    tables = []
    for spread in gauss_widths:
        s32 = float(np.float32(spread))
        gauss_total = np.sum(np.exp(-support * support / (2.0 * s32 * s32)))
        profile = np.exp(-support * support / (2.0 * s32 * s32)) / gauss_total
        scaled = support / s32
        tables.append(np.stack([profile, profile * scaled, profile * scaled * scaled]))
    return np.stack(tables)


def row_blocks(block_rows, window_rows, kernel_half_width, lead):
    taps = tap_table(kernel_half_width).reshape(9, 2 * kernel_half_width + 1)
    out = np.zeros((9, block_rows, window_rows), np.float64)
    for i in range(block_rows):
        start = lead + i - kernel_half_width
        out[:, i, start : start + 2 * kernel_half_width + 1] = taps
    return out.astype(np.float32)


def column_ops(column_count, kernel_half_width):
    taps = tap_table(kernel_half_width)
    out = np.zeros((3, 3, column_count, column_count), np.float64)
    for y in range(column_count):
        lo = max(0, y - kernel_half_width)
        hi = min(column_count, y + kernel_half_width + 1)
        for x in range(lo, hi):
            out[:, :, y, x] = taps[:, :, y - x + kernel_half_width]
    return out.astype(np.float32)


def convolve_all(exposures, kernel_coeffs):
    kernel_half_width = KS // 2
    n, height, columns = exposures.shape
    block = 8
    blocks = height // block
    lead = -(-kernel_half_width // block) * block
    reach = -(-(lead + kernel_half_width + block) // block)
    total_rows = (blocks + reach - 1) * block
    padded = jnp.pad(
        exposures, ((0, 0), (lead, total_rows - height - lead), (0, 0))
    ).reshape(n, blocks + reach - 1, block, columns)
    windows = jnp.concatenate([padded[:, j : j + blocks] for j in range(reach)], axis=2)
    rows = jnp.asarray(row_blocks(block, reach * block, kernel_half_width, lead))
    smooth = jnp.einsum("kit,nqtx->nqkix", rows, windows, precision=mxu_value)
    x_np = 2.0 * np.arange(columns, dtype=np.float32) / np.float32(columns - 1) - 1.0
    basis = np.zeros((6, 3, columns), np.float32)
    basis[0, 0] = 1.0
    basis[1, 0] = x_np
    basis[3, 0] = x_np * x_np
    basis[2, 1] = 1.0
    basis[4, 1] = x_np
    basis[5, 2] = 1.0
    fx = jnp.dot(
        kernel_coeffs.reshape(n * 27, 6), jnp.asarray(basis.reshape(6, 3 * columns)),
        precision=largest_value,
    ).reshape(n, 3, 3, 3, 3, columns)
    col_t = jnp.asarray(np.swapaxes(column_ops(columns, kernel_half_width), 2, 3))
    mixed = (
        col_t[None, :, None, 0, None, :, :] * fx[:, :, :, 0, :, :, None]
        + col_t[None, :, None, 1, None, :, :] * fx[:, :, :, 1, :, :, None]
        + col_t[None, :, None, 2, None, :, :] * fx[:, :, :, 2, :, :, None]
    )
    mixed = mixed.reshape(n, 9, 3 * columns, columns)
    fields = jnp.einsum("nqkiy,nkzy->nqiz", smooth, mixed, precision=mxu_value)
    fields = fields.reshape(n, height, 3 * columns)
    y_line = (2.0 * jnp.arange(height).astype(jnp.float32) / (height - 1) - 1.0)[None, :, None]
    return (
        fields[:, :, :columns]
        + y_line * fields[:, :, columns : 2 * columns]
        + (y_line * y_line) * fields[:, :, 2 * columns :]
    )


def place_kernel(index_ref, *refs):
    chunks = refs[:-5]
    coadd_ref, wmap_ref, acc_n, acc_w, table = refs[-5:]
    senders = len(chunks)
    slots = index_ref.shape[0] // 5
    capacity = slots // senders
    strip_rows = 8
    lanes = chunks[0].shape[-1]
    sums_at = capacity * 2 * strip_rows
    sums = None
    for chunk in chunks:
        if len(chunk.shape) == 3:
            block = chunk[0, pl.ds(sums_at, strip_rows), :]
        else:
            block = chunk[pl.ds(sums_at, strip_rows), :]
        sums = block if sums is None else sums + block
    visit_weight = (sums[3:4, :] + 1.0) / (sums[4:5, :] + 1.0)
    lane_row = lax.broadcasted_iota(jnp.int32, (1, lanes), 1)
    for visit in range(VISITS):
        picked = jnp.sum(jnp.where(lane_row == visit, visit_weight, 0.0), axis=1, keepdims=True)
        table[visit] = jnp.broadcast_to(picked, (strip_rows, lanes))
    lane_blocks = acc_n.shape[0] - 1
    out_rows = coadd_ref.shape[0]
    acc_n[...] = jnp.zeros(acc_n.shape, jnp.float32)
    acc_w[...] = jnp.zeros(acc_w.shape, jnp.float32)
    lane = lax.broadcasted_iota(jnp.int32, (strip_rows, lanes), 1)
    sub = lax.broadcasted_iota(jnp.int32, (strip_rows, lanes), 0)

    for d, chunk in enumerate(chunks):

        def body(j, carry, chunk=chunk, d=d):
            s = d * capacity + j
            q = index_ref[s]
            rem = index_ref[slots + s]
            top = pl.multiple_of(index_ref[2 * slots + s], strip_rows)
            rr = index_ref[3 * slots + s]
            wt = table[index_ref[4 * slots + s]]
            lane_lo = lane >= rem
            sub_lo = sub >= rr
            nxt = pl.multiple_of(top + strip_rows, strip_rows)
            for part, acc in ((1, acc_n), (0, acc_w)):
                at = pl.multiple_of(j * (2 * strip_rows) + part * strip_rows, strip_rows)
                if len(chunk.shape) == 3:
                    v = chunk[0, pl.ds(at, strip_rows), :] * wt
                else:
                    v = chunk[pl.ds(at, strip_rows), :] * wt
                v = pltpu.roll(v, rem, 1)
                v = pltpu.roll(v, rr, 0)
                zero = jnp.zeros_like(v)
                a = jnp.where(sub_lo, v, zero)
                b = v - a
                acc[q, pl.ds(top, strip_rows), :] += jnp.where(lane_lo, a, zero)
                acc[q + 1, pl.ds(top, strip_rows), :] += jnp.where(lane_lo, zero, a)
                acc[q, pl.ds(nxt, strip_rows), :] += jnp.where(lane_lo, b, zero)
                acc[q + 1, pl.ds(nxt, strip_rows), :] += jnp.where(lane_lo, zero, b)
            return carry

        lax.fori_loop(0, capacity, body, 0, unroll=min(16, capacity))
    for j in range(lane_blocks):
        n = acc_n[j, pl.ds(0, out_rows), :]
        w = acc_w[j, pl.ds(0, out_rows), :]
        wmap_ref[:, pl.ds(j * lanes, lanes)] = w
        coadd_ref[:, pl.ds(j * lanes, lanes)] = n / jnp.maximum(w, 1.0)


def place(chunks, index, patch_rows, patch_cols):
    lanes = chunks[0].shape[-1]
    strip_rows = 8
    lane_blocks = patch_cols // lanes
    smem = pltpu.SMEM
    return pl.pallas_call(
        place_kernel,
        out_shape=(
            jax.ShapeDtypeStruct((patch_rows, patch_cols), jnp.float32),
            jax.ShapeDtypeStruct((patch_rows, patch_cols), jnp.float32),
        ),
        in_specs=[pl.BlockSpec(memory_space=smem)]
        + [pl.BlockSpec(memory_space=pltpu.VMEM)] * len(chunks),
        out_specs=(pl.BlockSpec(memory_space=pltpu.VMEM), pl.BlockSpec(memory_space=pltpu.VMEM)),
        scratch_shapes=[
            pltpu.VMEM((lane_blocks + 1, patch_rows + strip_rows, lanes), jnp.float32),
            pltpu.VMEM((lane_blocks + 1, patch_rows + strip_rows, lanes), jnp.float32),
            pltpu.VMEM((VISITS, strip_rows, lanes), jnp.float32),
        ],
    )(index, *chunks)


def shards(
    exposures, variance, mask_bits, kernel_coeffs, ccd_visit, strip_patch, strip_row, strip_col
):
    ccd_count, height, columns = exposures.shape
    strip_total = strip_patch.shape[0]
    per_ccd = strip_total // ccd_count
    strip_rows = height // per_ccd
    devices = lax.axis_size("patch")
    capacity = 2 * strip_total // devices
    usable = (jnp.bitwise_and(mask_bits, 3) != 3).astype(jnp.float32)
    visit_hot = (ccd_visit == jnp.arange(VISITS)[None, :]).astype(jnp.float32)
    local_count = jnp.sum(jnp.sum(usable, axis=(1, 2))[:, None] * visit_hot, axis=0)
    local_load = jnp.sum(jnp.sum(usable * variance, axis=(1, 2))[:, None] * visit_hot, axis=0)

    destination = strip_patch[:, 0]
    strip_ids = jnp.arange(strip_total)
    earlier = strip_ids[None, :] < strip_ids[:, None]
    same_target = destination[None, :] == destination[:, None]
    slot_rank = jnp.sum(jnp.logical_and(earlier, same_target).astype(jnp.int32), axis=1)
    me = lax.axis_index("patch")
    slot_index = ((destination - me) % devices) * capacity + slot_rank
    slot_total = devices * capacity
    chooser = (slot_index[None, :] == jnp.arange(slot_total)[:, None]).astype(jnp.float32)

    strip_visit = jnp.repeat(ccd_visit[:, 0], per_ccd)
    placement = jnp.stack([strip_row, strip_col, strip_visit], axis=1).astype(jnp.float32)
    slot_meta = jnp.dot(chooser, placement, precision=largest_value).reshape(devices, capacity, 3)
    meta = jnp.concatenate(
        [
            jnp.pad(jnp.swapaxes(slot_meta, 1, 2), ((0, 0), (0, 0), (0, columns - capacity))),
            jnp.broadcast_to(
                jnp.pad(
                    jnp.stack([local_count, local_load])[None],
                    ((0, 0), (0, 3), (0, columns - VISITS)),
                ),
                (devices, 5, columns),
            ),
        ],
        axis=1,
    )
    body_rows = capacity * strip_rows
    convolved = convolve_all(exposures, kernel_coeffs)
    tiles = jnp.concatenate(
        [
            usable.reshape(strip_total, strip_rows * columns),
            (usable * convolved).reshape(strip_total, strip_rows * columns),
        ],
        axis=1,
    )
    packed = jnp.dot(chooser, tiles, precision=mxu_value).reshape(
        devices, 2 * body_rows, columns
    )
    payload = jnp.concatenate([packed, meta], axis=1)
    received = [payload[0]]
    for shift in range(1, devices):
        pairs = [(i, (i + shift) % devices) for i in range(devices)]
        received.append(lax.ppermute(payload[shift], "patch", pairs))
    got_meta = jnp.stack([chunk[2 * body_rows :, :] for chunk in received], axis=0)
    slot_rows = got_meta[:, 0, :capacity].reshape(slot_total).astype(jnp.int32)
    slot_cols = got_meta[:, 1, :capacity].reshape(slot_total).astype(jnp.int32)
    slot_visit = got_meta[:, 2, :capacity].reshape(slot_total).astype(jnp.int32)
    index = jnp.concatenate(
        [
            slot_cols // columns,
            slot_cols % columns,
            (slot_rows // strip_rows) * strip_rows,
            slot_rows % strip_rows,
            slot_visit,
        ]
    )
    coadd_image, weight_map = place([payload] + received[1:], index, PH, PW)
    return (coadd_image[None], weight_map[None])


def solution(mesh):
    return jax.shard_map(
        shards,
        mesh=mesh,
        in_specs=(
            P(("band", "patch"), None, None),
            P(("band", "patch"), None, None),
            P(("band", "patch"), None, None),
            P(("band", "patch"), None, None),
            P(("band", "patch"), None),
            P(("band", "patch"), None),
            P(("band", "patch")),
            P(("band", "patch")),
        ),
        out_specs=(P(("band", "patch"), None, None), P(("band", "patch"), None, None)),
        check_vma=False,
    )
```
